256 devices in a mesh: seq: 64 (over z, x, core), head: 4 (over y).
Axes of the slice: x: 4, y: 4, z: 8, core: 2. Of those that a mesh axis runs over, the one named last changes fastest.
Arguments:
- features: bfloat16 [8192, 4096], P('seq', 'head'), may hold values from -6 to 6
- proj_weight: bfloat16 [4096, 4096], P(None, 'head'), may hold values from -0.09375 to 0.09375
- query_vectors: bfloat16 [8192, 4096], P('seq', 'head'), may hold values from -6 to 6
- key_vectors: bfloat16 [8192, 4096], P('seq', 'head'), may hold values from -6 to 6
Outputs:
- rotated_queries: bfloat16 [8192, 4096], P('seq', 'head')
- rotated_keys: bfloat16 [8192, 4096], P('seq', 'head')
The draws below stay inside these ranges and needn't reach their ends.
All inputs are finite; a program needn't handle non-finite values.
Results may differ from the reference program's by a relative error of at most 0.0024.
Values may be sent and summed in bfloat16 or wider, within the bound.
No kernel may reach another device: no remote copies, remote signals or barrier semaphores. Data moves between devices by JAX's collectives and lax.ppermute only.
A program may use at most 128 MiB of HBM per device.

```python
import jax
import jax.numpy as jnp
from jax import lax

D = 4096
HEADS = 32
HEAD_DIM = 128
TOKENS = 8192


def levels(rng, dims, shards, smallest, high):
    def one(position, parts):
        heights = jax.random.uniform(jax.random.fold_in(jax.random.fold_in(rng, 6), position), (parts,), jnp.float32, smallest / len(shards), high / len(shards))
        return jnp.repeat(jnp.exp(heights), dims[position] // parts).reshape((-1,) + (1,) * (len(dims) - position - 1))

    loudness = one(*shards[0])
    for cut in shards[1:]:
        loudness = loudness * one(*cut)
    return loudness


def centred(stream_key, extent, scale, most, cuts=(), kind=jnp.bfloat16):
    values = scale * jax.random.normal(stream_key, extent, jnp.float32)
    if cuts:
        values = values * levels(stream_key, extent, cuts, -0.22, 0.18)
    return jnp.clip(values, -most, most).astype(kind)


def setup_inputs(seed: int = 0) -> dict:
    keys = jax.random.split(jax.random.key(seed), 5)
    return {
        "features": centred(keys[0], (TOKENS, D), 1.0, 6.0, ((0, 64), (1, 4))),
        "proj_weight": centred(keys[1], (D, HEADS * HEAD_DIM), D ** -0.5, 0.09375, ((1, 4),)),
        "query_vectors": centred(keys[2], (TOKENS, HEADS * HEAD_DIM), 1.0, 6.0, ((0, 64), (1, 4))),
        "key_vectors": centred(keys[3], (TOKENS, HEADS * HEAD_DIM), 1.0, 6.0, ((0, 64), (1, 4))),
    }


def reference(features, proj_weight, query_vectors, key_vectors):
    highest = lax.Precision.HIGHEST
    raw_proj = jnp.dot(features, proj_weight, preferred_element_type=jnp.float32)
    raw_proj = raw_proj.reshape(TOKENS, HEADS, HEAD_DIM)
    directions = raw_proj * lax.rsqrt(lax.optimization_barrier(jnp.sum(raw_proj * raw_proj, axis=-1, keepdims=True)) + 1e-06)
    queries = query_vectors.astype(jnp.float32).reshape(TOKENS, HEADS, HEAD_DIM)
    keys_all = key_vectors.astype(jnp.float32).reshape(TOKENS, HEADS, HEAD_DIM)

    def advance(product, item):
        vector, query_row, key_row = item
        along = jnp.einsum('hde,he->hd', product, vector, precision=highest)
        product = product - 2.0 * along[:, :, None] * vector[:, None, :]
        out_query = jnp.einsum('hde,he->hd', product, query_row, precision=highest)
        out_key = jnp.einsum('hde,he->hd', product, key_row, precision=highest)
        return (product, (out_query, out_key))
    start = jnp.broadcast_to(jnp.eye(HEAD_DIM, dtype=jnp.float32), (HEADS, HEAD_DIM, HEAD_DIM))
    final, outputs = lax.scan(advance, start, (directions, queries, keys_all))
    rotated_queries = outputs[0].reshape(TOKENS, HEADS * HEAD_DIM).astype(jnp.bfloat16)
    rotated_keys = outputs[1].reshape(TOKENS, HEADS * HEAD_DIM).astype(jnp.bfloat16)
    return (rotated_queries, rotated_keys)
```

```python
import functools

import jax
import jax.numpy as jnp
from jax import lax
from jax.sharding import PartitionSpec as P

HEAD_DIM = 128


def entering(array, axis, count, combine, identity):
    place = lax.axis_index(axis)
    start = jnp.broadcast_to(jnp.asarray(identity, array.dtype), array.shape)
    span = array
    before = None
    shift = 1
    while shift < count:
        pairs = [(k, k + shift) for k in range(count - shift)]
        arrived = lax.ppermute(span, axis, pairs)
        reached = place >= shift
        last = shift * 2 >= count
        if before is None:
            before = jnp.where(reached, arrived, start)
            if not last:
                span = jnp.where(reached, combine(arrived, span), span)
        elif last:
            before = jnp.where(reached, combine(arrived, before), before)
        else:
            width = array.shape[-1]
            both = combine(arrived, jnp.concatenate([span, before], axis=-1))
            span = jnp.where(reached, both[..., :width], span)
            before = jnp.where(reached, both[..., width:], before)
        shift = shift * 2
    return before if before is not None else start


def small_inverse(matrix):
    highest = lax.Precision.HIGHEST
    size = matrix.shape[-1]
    position = jnp.arange(size)
    strict = (position[:, None] < position[None, :]).astype(jnp.float32)
    eye_block = jnp.eye(size, dtype=jnp.float32)
    power = -2.0 * matrix * strict[None]
    result = eye_block[None] + power
    reach = 2
    while reach < size:
        power = jnp.einsum("hij,hjk->hik", power, power, precision=highest)
        result = result + jnp.einsum("hij,hjk->hik", result, power, precision=highest)
        reach = reach * 2
    return 2.0 * result


def triangle_inverse(matrix):
    highest = lax.Precision.HIGHEST
    size = matrix.shape[-1]
    if size <= 16:
        return small_inverse(matrix)
    half = size // 2
    first = triangle_inverse(matrix[:, :half, :half])
    second = triangle_inverse(matrix[:, half:, half:])
    coupling = matrix[:, :half, half:]
    middle = jnp.einsum("hij,hjk->hik", first, coupling, precision=highest)
    corner = -jnp.einsum("hij,hjk->hik", middle, second, precision=highest)
    lower_left = jnp.zeros((matrix.shape[0], size - half, half), jnp.float32)
    top = jnp.concatenate([first, corner], axis=2)
    bottom = jnp.concatenate([lower_left, second], axis=2)
    return jnp.concatenate([top, bottom], axis=1)


def upper_solve(matrix, right_side):
    highest = lax.Precision.HIGHEST
    rows = matrix.shape[1]
    size = min(128, rows)
    count = rows // size
    solved_blocks = []
    for i in reversed(range(count)):
        inverse_block = triangle_inverse(matrix)
        solved_blocks.append(
            jnp.einsum("hij,hjk->hik", inverse_block, right_side, precision=highest)
        )
    return jnp.concatenate(solved_blocks[::-1], axis=1)


def body(seq_count, features, proj_weight, query_vectors, key_vectors):
    highest = lax.Precision.HIGHEST
    tok_rows = query_vectors.shape[0]
    width = proj_weight.shape[1]
    local_heads = width // HEAD_DIM
    raw_proj = jnp.dot(
        lax.all_gather(features, "head", axis=1, tiled=True),
        proj_weight,
        preferred_element_type=jnp.float32,
    )
    raw_proj = raw_proj.reshape(tok_rows, local_heads, HEAD_DIM)
    directions = raw_proj * lax.rsqrt(jnp.sum(raw_proj * raw_proj, axis=-1, keepdims=True) + 1e-06)
    reflectors = jnp.transpose(directions, (1, 0, 2))
    targets = jnp.concatenate(
        [
            query_vectors.reshape(tok_rows, local_heads, HEAD_DIM),
            key_vectors.reshape(tok_rows, local_heads, HEAD_DIM),
        ],
        axis=0,
    )
    targets = jnp.transpose(targets.astype(jnp.float32), (1, 0, 2))
    gram = jnp.einsum("hid,hjd->hij", reflectors, reflectors, precision=highest)
    position = jnp.arange(tok_rows)
    upper = (position[:, None] < position[None, :]).astype(jnp.float32)
    identity_tok = jnp.eye(tok_rows, dtype=jnp.float32)
    inverse_t = gram * upper[None] + 0.5 * identity_tok[None]
    projected = jnp.einsum("hid,htd->hit", reflectors, targets, precision=highest)
    target_pos = jnp.concatenate([position, position])
    keep = (position[:, None] <= target_pos[None, :]).astype(jnp.float32)
    masked = projected * keep[None]
    right_side = jnp.concatenate([masked, reflectors], axis=2)
    solved = upper_solve(inverse_t, right_side)
    weights_tok = solved[:, :, : 2 * tok_rows]
    factor = solved[:, :, 2 * tok_rows :]
    local_part = targets - jnp.einsum("hit,hid->htd", weights_tok, reflectors, precision=highest)
    identity = jnp.broadcast_to(
        jnp.eye(HEAD_DIM, dtype=jnp.float32), (local_heads, HEAD_DIM, HEAD_DIM)
    )
    block_product = identity - jnp.einsum("hid,hie->hde", reflectors, factor, precision=highest)

    def combine(earlier, later):
        return jnp.einsum("hde,hef->hdf", earlier, later, precision=highest)

    carried = entering(block_product, "seq", seq_count, combine, identity)
    rotated = jnp.einsum("hde,hte->htd", carried, local_part, precision=highest)
    rotated = jnp.transpose(rotated, (1, 0, 2))
    rotated_queries = rotated[:tok_rows].reshape(tok_rows, width).astype(jnp.bfloat16)
    rotated_keys = rotated[tok_rows:].reshape(tok_rows, width).astype(jnp.bfloat16)
    return (rotated_queries, rotated_keys)


def solution(mesh):
    in_specs = (P("seq", "head"), P(None, "head"), P("seq", "head"), P("seq", "head"))
    out_specs = (P("seq", "head"), P("seq", "head"))
    return jax.shard_map(functools.partial(body, mesh.shape["seq"]), mesh=mesh, in_specs=in_specs, out_specs=out_specs, check_vma=False)
```

```python
import functools

import jax
import jax.numpy as jnp
from jax import lax
from jax.sharding import PartitionSpec as P

HEAD_DIM = 128


def entering(array, axis, count, combine, identity):
    place = lax.axis_index(axis)
    start = jnp.broadcast_to(jnp.asarray(identity, array.dtype), array.shape)
    span = array
    before = None
    shift = 1
    while shift < count:
        pairs = [(k, k + shift) for k in range(count - shift)]
        arrived = lax.ppermute(span, axis, pairs)
        reached = place >= shift
        last = shift * 2 >= count
        if before is None:
            before = jnp.where(reached, arrived, start)
            if not last:
                span = jnp.where(reached, combine(arrived, span), span)
        elif last:
            before = jnp.where(reached, combine(arrived, before), before)
        else:
            width = array.shape[-1]
            both = combine(arrived, jnp.concatenate([span, before], axis=-1))
            span = jnp.where(reached, both[..., :width], span)
            before = jnp.where(reached, both[..., width:], before)
        shift = shift * 2
    return before if before is not None else start


def paired_entering(array, axis, count, combine, identity):
    place = lax.axis_index(axis)
    core = place % 2
    first = core == 0
    half = array.shape[0] // 2
    swap = [(k, k ^ 1) for k in range(count)]
    mate = lax.ppermute(array, axis, swap)
    chip = combine(jnp.where(first, array, mate), jnp.where(first, mate, array))
    inner = jnp.where(first, jnp.broadcast_to(identity, array.shape), mate)
    mine = lax.dynamic_slice_in_dim(chip, core * half, half, 0)
    start = jnp.broadcast_to(identity, mine.shape)
    span = mine
    before = start
    shift = 2
    while shift < count:
        pairs = [(k, k + shift) for k in range(count - shift)]
        arrived = lax.ppermute(span, axis, pairs)
        reached = place >= shift
        last = shift * 2 >= count
        if shift == 2:
            before = jnp.where(reached, arrived, start)
            if not last:
                span = jnp.where(reached, combine(arrived, span), span)
        elif last:
            before = jnp.where(reached, combine(arrived, before), before)
        else:
            width = array.shape[-1]
            both = combine(arrived, jnp.concatenate([span, before], axis=-1))
            span = jnp.where(reached, both[..., :width], span)
            before = jnp.where(reached, both[..., width:], before)
        shift = shift * 2
    other = lax.ppermute(before, axis, swap)
    full = jnp.where(
        first,
        jnp.concatenate([before, other], axis=0),
        jnp.concatenate([other, before], axis=0),
    )
    return combine(full, inner)


def gathered_projection(features, proj_weight, axis, count):
    place = lax.axis_index(axis)
    width = features.shape[1]
    rows = lambda owner: lax.dynamic_slice_in_dim(proj_weight, owner * width, width, 0)
    total = jnp.dot(features, rows(place), preferred_element_type=jnp.float32)
    for step in range(1, count):
        pairs = [(k, (k + step) % count) for k in range(count)]
        part = lax.ppermute(features, axis, pairs)
        owner = (place + count - step) % count
        total = total + jnp.dot(part, rows(owner), preferred_element_type=jnp.float32)
    return total


def small_inverse(matrix):
    highest = lax.Precision.HIGHEST
    size = matrix.shape[-1]
    position = jnp.arange(size)
    strict = (position[:, None] < position[None, :]).astype(jnp.float32)
    eye_block = jnp.eye(size, dtype=jnp.float32)
    power = -2.0 * matrix * strict[None]
    result = eye_block[None] + power
    reach = 2
    while reach < size:
        power = jnp.einsum("hij,hjk->hik", power, power, precision=highest)
        result = result + jnp.einsum("hij,hjk->hik", result, power, precision=highest)
        reach = reach * 2
    return 2.0 * result


def triangle_inverse(matrix):
    highest = lax.Precision.HIGHEST
    size = matrix.shape[-1]
    if size <= 16:
        return small_inverse(matrix)
    half = size // 2
    first = triangle_inverse(matrix[:, :half, :half])
    second = triangle_inverse(matrix[:, half:, half:])
    coupling = matrix[:, :half, half:]
    middle = jnp.einsum("hij,hjk->hik", first, coupling, precision=highest)
    corner = -jnp.einsum("hij,hjk->hik", middle, second, precision=highest)
    lower_left = jnp.zeros((matrix.shape[0], size - half, half), jnp.float32)
    top = jnp.concatenate([first, corner], axis=2)
    bottom = jnp.concatenate([lower_left, second], axis=2)
    return jnp.concatenate([top, bottom], axis=1)


def upper_solve(matrix, right_side):
    highest = lax.Precision.HIGHEST
    rows = matrix.shape[1]
    size = min(128, rows)
    count = rows // size
    solved_blocks = []
    for i in reversed(range(count)):
        inverse_block = triangle_inverse(matrix)
        solved_blocks.append(
            jnp.einsum("hij,hjk->hik", inverse_block, right_side, precision=highest)
        )
    return jnp.concatenate(solved_blocks[::-1], axis=1)


def body(seq_count, head_count, features, proj_weight, query_vectors, key_vectors):
    highest = lax.Precision.HIGHEST
    tok_rows = query_vectors.shape[0]
    width = proj_weight.shape[1]
    local_heads = width // HEAD_DIM
    raw_proj = gathered_projection(features, proj_weight, "head", head_count)
    raw_proj = raw_proj.reshape(tok_rows, local_heads, HEAD_DIM)
    directions = raw_proj * lax.rsqrt(jnp.sum(raw_proj * raw_proj, axis=-1, keepdims=True) + 1e-06)
    reflectors = jnp.transpose(directions, (1, 0, 2))
    targets = jnp.concatenate(
        [
            query_vectors.reshape(tok_rows, local_heads, HEAD_DIM),
            key_vectors.reshape(tok_rows, local_heads, HEAD_DIM),
        ],
        axis=0,
    )
    targets = jnp.transpose(targets.astype(jnp.float32), (1, 0, 2))
    gram = jnp.einsum("hid,hjd->hij", reflectors, reflectors, precision=highest)
    position = jnp.arange(tok_rows)
    upper = (position[:, None] < position[None, :]).astype(jnp.float32)
    identity_tok = jnp.eye(tok_rows, dtype=jnp.float32)
    inverse_t = gram * upper[None] + 0.5 * identity_tok[None]
    projected = jnp.einsum("hid,htd->hit", reflectors, targets, precision=highest)
    target_pos = jnp.concatenate([position, position])
    keep = (position[:, None] <= target_pos[None, :]).astype(jnp.float32)
    masked = projected * keep[None]
    right_side = jnp.concatenate([masked, reflectors], axis=2)
    solved = upper_solve(inverse_t, right_side)
    weights_tok = solved[:, :, : 2 * tok_rows]
    factor = solved[:, :, 2 * tok_rows :]
    local_part = targets - jnp.einsum("hit,hid->htd", weights_tok, reflectors, precision=highest)
    identity = jnp.broadcast_to(
        jnp.eye(HEAD_DIM, dtype=jnp.float32), (local_heads, HEAD_DIM, HEAD_DIM)
    )
    block_product = identity - jnp.einsum("hid,hie->hde", reflectors, factor, precision=highest)

    def combine(earlier, later):
        return jnp.einsum("hde,hef->hdf", earlier, later, precision=highest)

    if seq_count % 2 == 0 and local_heads % 2 == 0:
        carried = paired_entering(block_product, "seq", seq_count, combine, identity[0])
    else:
        carried = entering(block_product, "seq", seq_count, combine, identity)
    rotated = jnp.einsum("hde,hte->htd", carried, local_part, precision=highest)
    rotated = jnp.transpose(rotated, (1, 0, 2))
    rotated_queries = rotated[:tok_rows].reshape(tok_rows, width).astype(jnp.bfloat16)
    rotated_keys = rotated[tok_rows:].reshape(tok_rows, width).astype(jnp.bfloat16)
    return (rotated_queries, rotated_keys)


def solution(mesh):
    in_specs = (P("seq", "head"), P(None, "head"), P("seq", "head"), P("seq", "head"))
    out_specs = (P("seq", "head"), P("seq", "head"))
    return jax.shard_map(functools.partial(body, mesh.shape["seq"], mesh.shape["head"]), mesh=mesh, in_specs=in_specs, out_specs=out_specs, check_vma=False)
```

```python
import functools

import jax
import jax.numpy as jnp
from jax import lax
from jax.sharding import PartitionSpec as P

HEAD_DIM = 128


def entering(array, axis, count, combine, identity):
    place = lax.axis_index(axis)
    start = jnp.broadcast_to(jnp.asarray(identity, array.dtype), array.shape)
    span = array
    before = None
    shift = 1
    while shift < count:
        pairs = [(k, k + shift) for k in range(count - shift)]
        arrived = lax.ppermute(span, axis, pairs)
        reached = place >= shift
        last = shift * 2 >= count
        if before is None:
            before = jnp.where(reached, arrived, start)
            if not last:
                span = jnp.where(reached, combine(arrived, span), span)
        elif last:
            before = jnp.where(reached, combine(arrived, before), before)
        else:
            width = array.shape[-1]
            both = combine(arrived, jnp.concatenate([span, before], axis=-1))
            span = jnp.where(reached, both[..., :width], span)
            before = jnp.where(reached, both[..., width:], before)
        shift = shift * 2
    return before if before is not None else start


def paired_entering(array, axis, count, combine, identity):
    place = lax.axis_index(axis)
    core = place % 2
    first = core == 0
    half = array.shape[0] // 2
    swap = [(k, k ^ 1) for k in range(count)]
    mate = lax.ppermute(array, axis, swap)
    chip = combine(jnp.where(first, array, mate), jnp.where(first, mate, array))
    inner = jnp.where(first, jnp.broadcast_to(identity, array.shape), mate)
    mine = lax.dynamic_slice_in_dim(chip, core * half, half, 0)
    start = jnp.broadcast_to(identity, mine.shape)
    span = mine
    before = start
    shift = 2
    while shift < count:
        pairs = [(k, k + shift) for k in range(count - shift)]
        arrived = lax.ppermute(span, axis, pairs)
        reached = place >= shift
        last = shift * 2 >= count
        if shift == 2:
            before = jnp.where(reached, arrived, start)
            if not last:
                span = jnp.where(reached, combine(arrived, span), span)
        elif last:
            before = jnp.where(reached, combine(arrived, before), before)
        else:
            width = array.shape[-1]
            both = combine(arrived, jnp.concatenate([span, before], axis=-1))
            span = jnp.where(reached, both[..., :width], span)
            before = jnp.where(reached, both[..., width:], before)
        shift = shift * 2
    other = lax.ppermute(before, axis, swap)
    full = jnp.where(
        first,
        jnp.concatenate([before, other], axis=0),
        jnp.concatenate([other, before], axis=0),
    )
    return combine(full, inner)


def strided_scan(array, axis, count, stride, combine, start):
    place = lax.axis_index(axis)
    span = array
    before = start
    shift = stride
    while shift < count:
        pairs = [(k, k + shift) for k in range(count - shift)]
        arrived = lax.ppermute(span, axis, pairs)
        reached = place >= shift
        last = shift * 2 >= count
        if shift == stride:
            before = jnp.where(reached, arrived, start)
            if not last:
                span = jnp.where(reached, combine(arrived, span), span)
        elif last:
            before = jnp.where(reached, combine(arrived, before), before)
        else:
            width = array.shape[-1]
            both = combine(arrived, jnp.concatenate([span, before], axis=-1))
            span = jnp.where(reached, both[..., :width], span)
            before = jnp.where(reached, both[..., width:], before)
        shift = shift * 2
    return before


def row_exchange(pieces, axis, count, row):
    place = lax.axis_index(axis)
    pos = place % row
    got = [pieces(pos)]
    for step in range(1, row):
        pairs = [(k, (k // row) * row + (k % row + step) % row) for k in range(count)]
        got.append(lax.ppermute(pieces((pos + step) % row), axis, pairs))
    order = (pos + row - jnp.arange(row)) % row
    return jnp.take(jnp.stack(got), order, axis=0)


def row_entering(array, axis, count, row, combine, identity):
    place = lax.axis_index(axis)
    heads, size = array.shape[0], array.shape[-1]
    share = heads // row
    eye = jnp.broadcast_to(identity, (share, size, size))
    blocks = row_exchange(
        lambda g: lax.dynamic_slice_in_dim(array, g * share, share, 0), axis, count, row
    )
    prefix = [eye]
    for q in range(1, row):
        prefix.append(combine(prefix[-1], blocks[q - 1]))
    whole = combine(prefix[-1], blocks[row - 1])
    outer = strided_scan(whole, axis, count, row, combine, eye)
    spread = jnp.broadcast_to(outer[None], (row, share, size, size)).reshape(row * share, size, size)
    carried = combine(spread, jnp.stack(prefix).reshape(row * share, size, size))
    carried = carried.reshape(row, share, size, size)
    full = row_exchange(
        lambda q: lax.dynamic_index_in_dim(carried, q, 0, keepdims=False), axis, count, row
    )
    return full.reshape(heads, size, size)


def gathered_projection(features, proj_weight, axis, count):
    place = lax.axis_index(axis)
    width = features.shape[1]
    rows = lambda owner: lax.dynamic_slice_in_dim(proj_weight, owner * width, width, 0)
    total = jnp.dot(features, rows(place), preferred_element_type=jnp.float32)
    for step in range(1, count):
        pairs = [(k, (k + step) % count) for k in range(count)]
        part = lax.ppermute(features, axis, pairs)
        owner = (place + count - step) % count
        total = total + jnp.dot(part, rows(owner), preferred_element_type=jnp.float32)
    return total


def small_inverse(matrix):
    highest = lax.Precision.HIGHEST
    size = matrix.shape[-1]
    position = jnp.arange(size)
    strict = (position[:, None] < position[None, :]).astype(jnp.float32)
    eye_block = jnp.eye(size, dtype=jnp.float32)
    power = -2.0 * matrix * strict[None]
    result = eye_block[None] + power
    reach = 2
    while reach < size:
        power = jnp.einsum("hij,hjk->hik", power, power, precision=highest)
        result = result + jnp.einsum("hij,hjk->hik", result, power, precision=highest)
        reach = reach * 2
    return 2.0 * result


def triangle_inverse(matrix):
    highest = lax.Precision.HIGHEST
    size = matrix.shape[-1]
    if size <= 16:
        return small_inverse(matrix)
    half = size // 2
    first = triangle_inverse(matrix[:, :half, :half])
    second = triangle_inverse(matrix[:, half:, half:])
    coupling = matrix[:, :half, half:]
    middle = jnp.einsum("hij,hjk->hik", first, coupling, precision=highest)
    corner = -jnp.einsum("hij,hjk->hik", middle, second, precision=highest)
    lower_left = jnp.zeros((matrix.shape[0], size - half, half), jnp.float32)
    top = jnp.concatenate([first, corner], axis=2)
    bottom = jnp.concatenate([lower_left, second], axis=2)
    return jnp.concatenate([top, bottom], axis=1)


def upper_solve(matrix, right_side):
    highest = lax.Precision.HIGHEST
    rows = matrix.shape[1]
    size = min(128, rows)
    count = rows // size
    solved_blocks = []
    for i in reversed(range(count)):
        inverse_block = triangle_inverse(matrix)
        solved_blocks.append(
            jnp.einsum("hij,hjk->hik", inverse_block, right_side, precision=highest)
        )
    return jnp.concatenate(solved_blocks[::-1], axis=1)


def body(seq_count, head_count, features, proj_weight, query_vectors, key_vectors):
    highest = lax.Precision.HIGHEST
    tok_rows = query_vectors.shape[0]
    width = proj_weight.shape[1]
    local_heads = width // HEAD_DIM
    raw_proj = gathered_projection(features, proj_weight, "head", head_count)
    raw_proj = raw_proj.reshape(tok_rows, local_heads, HEAD_DIM)
    directions = raw_proj * lax.rsqrt(jnp.sum(raw_proj * raw_proj, axis=-1, keepdims=True) + 1e-06)
    reflectors = jnp.transpose(directions, (1, 0, 2))
    targets = jnp.concatenate(
        [
            query_vectors.reshape(tok_rows, local_heads, HEAD_DIM),
            key_vectors.reshape(tok_rows, local_heads, HEAD_DIM),
        ],
        axis=0,
    )
    targets = jnp.transpose(targets.astype(jnp.float32), (1, 0, 2))
    gram = jnp.einsum("hid,hjd->hij", reflectors, reflectors, precision=highest)
    position = jnp.arange(tok_rows)
    upper = (position[:, None] < position[None, :]).astype(jnp.float32)
    identity_tok = jnp.eye(tok_rows, dtype=jnp.float32)
    inverse_t = gram * upper[None] + 0.5 * identity_tok[None]
    projected = jnp.einsum("hid,htd->hit", reflectors, targets, precision=highest)
    target_pos = jnp.concatenate([position, position])
    keep = (position[:, None] <= target_pos[None, :]).astype(jnp.float32)
    masked = projected * keep[None]
    right_side = jnp.concatenate([masked, reflectors], axis=2)
    solved = upper_solve(inverse_t, right_side)
    weights_tok = solved[:, :, : 2 * tok_rows]
    factor = solved[:, :, 2 * tok_rows :]
    local_part = targets - jnp.einsum("hit,hid->htd", weights_tok, reflectors, precision=highest)
    identity = jnp.broadcast_to(
        jnp.eye(HEAD_DIM, dtype=jnp.float32), (local_heads, HEAD_DIM, HEAD_DIM)
    )
    block_product = identity - jnp.einsum("hid,hie->hde", reflectors, factor, precision=highest)

    def combine(earlier, later):
        return jnp.einsum("hde,hef->hdf", earlier, later, precision=highest)

    row = 8
    if seq_count % row == 0 and seq_count > row and local_heads % row == 0:
        carried = row_entering(block_product, "seq", seq_count, row, combine, identity[0])
    elif seq_count % 2 == 0 and local_heads % 2 == 0:
        carried = paired_entering(block_product, "seq", seq_count, combine, identity[0])
    else:
        carried = entering(block_product, "seq", seq_count, combine, identity)
    rotated = jnp.einsum("hde,hte->htd", carried, local_part, precision=highest)
    rotated = jnp.transpose(rotated, (1, 0, 2))
    rotated_queries = rotated[:tok_rows].reshape(tok_rows, width).astype(jnp.bfloat16)
    rotated_keys = rotated[tok_rows:].reshape(tok_rows, width).astype(jnp.bfloat16)
    return (rotated_queries, rotated_keys)


def solution(mesh):
    in_specs = (P("seq", "head"), P(None, "head"), P("seq", "head"), P("seq", "head"))
    out_specs = (P("seq", "head"), P("seq", "head"))
    return jax.shard_map(functools.partial(body, mesh.shape["seq"], mesh.shape["head"]), mesh=mesh, in_specs=in_specs, out_specs=out_specs, check_vma=False)
```

```python
import functools

import jax
import jax.numpy as jnp
from jax import lax
from jax.sharding import PartitionSpec as P

HEAD_DIM = 128


def entering(array, axis, count, combine, identity):
    place = lax.axis_index(axis)
    start = jnp.broadcast_to(jnp.asarray(identity, array.dtype), array.shape)
    span = array
    before = None
    shift = 1
    while shift < count:
        pairs = [(k, k + shift) for k in range(count - shift)]
        arrived = lax.ppermute(span, axis, pairs)
        reached = place >= shift
        last = shift * 2 >= count
        if before is None:
            before = jnp.where(reached, arrived, start)
            if not last:
                span = jnp.where(reached, combine(arrived, span), span)
        elif last:
            before = jnp.where(reached, combine(arrived, before), before)
        else:
            width = array.shape[-1]
            both = combine(arrived, jnp.concatenate([span, before], axis=-1))
            span = jnp.where(reached, both[..., :width], span)
            before = jnp.where(reached, both[..., width:], before)
        shift = shift * 2
    return before if before is not None else start


def paired_entering(array, axis, count, combine, identity):
    place = lax.axis_index(axis)
    core = place % 2
    first = core == 0
    half = array.shape[0] // 2
    swap = [(k, k ^ 1) for k in range(count)]
    mate = lax.ppermute(array, axis, swap)
    chip = combine(jnp.where(first, array, mate), jnp.where(first, mate, array))
    inner = jnp.where(first, jnp.broadcast_to(identity, array.shape), mate)
    mine = lax.dynamic_slice_in_dim(chip, core * half, half, 0)
    start = jnp.broadcast_to(identity, mine.shape)
    span = mine
    before = start
    shift = 2
    while shift < count:
        pairs = [(k, k + shift) for k in range(count - shift)]
        arrived = lax.ppermute(span, axis, pairs)
        reached = place >= shift
        last = shift * 2 >= count
        if shift == 2:
            before = jnp.where(reached, arrived, start)
            if not last:
                span = jnp.where(reached, combine(arrived, span), span)
        elif last:
            before = jnp.where(reached, combine(arrived, before), before)
        else:
            width = array.shape[-1]
            both = combine(arrived, jnp.concatenate([span, before], axis=-1))
            span = jnp.where(reached, both[..., :width], span)
            before = jnp.where(reached, both[..., width:], before)
        shift = shift * 2
    other = lax.ppermute(before, axis, swap)
    full = jnp.where(
        first,
        jnp.concatenate([before, other], axis=0),
        jnp.concatenate([other, before], axis=0),
    )
    return combine(full, inner)


def strided_scan(array, axis, count, stride, combine, start):
    place = lax.axis_index(axis)
    span = array
    before = start
    shift = stride
    while shift < count:
        pairs = [(k, k + shift) for k in range(count - shift)]
        arrived = lax.ppermute(span, axis, pairs)
        reached = place >= shift
        last = shift * 2 >= count
        if shift == stride:
            before = jnp.where(reached, arrived, start)
            if not last:
                span = jnp.where(reached, combine(arrived, span), span)
        elif last:
            before = jnp.where(reached, combine(arrived, before), before)
        else:
            width = array.shape[-1]
            both = combine(arrived, jnp.concatenate([span, before], axis=-1))
            span = jnp.where(reached, both[..., :width], span)
            before = jnp.where(reached, both[..., width:], before)
        shift = shift * 2
    return before


def row_exchange(pieces, axis, count, row):
    place = lax.axis_index(axis)
    pos = place % row
    got = [pieces(pos)]
    for step in range(1, row):
        pairs = [(k, (k // row) * row + (k % row + step) % row) for k in range(count)]
        got.append(lax.ppermute(pieces((pos + step) % row), axis, pairs))
    order = (pos + row - jnp.arange(row)) % row
    return jnp.take(jnp.stack(got), order, axis=0)


def row_entering(array, axis, count, row, combine, identity):
    place = lax.axis_index(axis)
    heads, size = array.shape[0], array.shape[-1]
    share = heads // row
    eye = jnp.broadcast_to(identity, (share, size, size))
    blocks = row_exchange(
        lambda g: lax.dynamic_slice_in_dim(array, g * share, share, 0), axis, count, row
    )
    prefix = [eye]
    for q in range(1, row):
        prefix.append(combine(prefix[-1], blocks[q - 1]))
    whole = combine(prefix[-1], blocks[row - 1])
    outer = strided_scan(whole, axis, count, row, combine, eye)
    spread = jnp.broadcast_to(outer[None], (row, share, size, size)).reshape(row * share, size, size)
    carried = combine(spread, jnp.stack(prefix).reshape(row * share, size, size))
    carried = carried.reshape(row, share, size, size)
    full = row_exchange(
        lambda q: lax.dynamic_index_in_dim(carried, q, 0, keepdims=False), axis, count, row
    )
    return full.reshape(heads, size, size)


def gathered_projection(features, proj_weight, axis, count):
    place = lax.axis_index(axis)
    got = [features]
    for step in range(1, count):
        pairs = [(k, (k + step) % count) for k in range(count)]
        got.append(lax.ppermute(features, axis, pairs))
    order = (place + count - jnp.arange(count)) % count
    ordered = jnp.take(jnp.stack(got), order, axis=0)
    rows, width = features.shape
    whole = jnp.transpose(ordered, (1, 0, 2)).reshape(rows, count * width)
    return jnp.dot(whole, proj_weight, preferred_element_type=jnp.float32)


def small_inverse(matrix):
    highest = lax.Precision.HIGHEST
    size = matrix.shape[-1]
    position = jnp.arange(size)
    strict = (position[:, None] < position[None, :]).astype(jnp.float32)
    eye_block = jnp.eye(size, dtype=jnp.float32)
    power = -2.0 * matrix * strict[None]
    result = eye_block[None] + power
    reach = 2
    while reach < size:
        power = jnp.einsum("hij,hjk->hik", power, power, precision=highest)
        result = result + jnp.einsum("hij,hjk->hik", result, power, precision=highest)
        reach = reach * 2
    return 2.0 * result


def triangle_inverse(matrix):
    highest = lax.Precision.HIGHEST
    size = matrix.shape[-1]
    if size <= 16:
        return small_inverse(matrix)
    half = size // 2
    first = triangle_inverse(matrix[:, :half, :half])
    second = triangle_inverse(matrix[:, half:, half:])
    coupling = matrix[:, :half, half:]
    middle = jnp.einsum("hij,hjk->hik", first, coupling, precision=highest)
    corner = -jnp.einsum("hij,hjk->hik", middle, second, precision=highest)
    lower_left = jnp.zeros((matrix.shape[0], size - half, half), jnp.float32)
    top = jnp.concatenate([first, corner], axis=2)
    bottom = jnp.concatenate([lower_left, second], axis=2)
    return jnp.concatenate([top, bottom], axis=1)


def batched_triangle_inverse(matrix):
    highest = lax.Precision.HIGHEST
    heads, size = matrix.shape[0], matrix.shape[-1]
    leaf = min(16, size)
    count = size // leaf
    diagonal = jnp.stack(
        [matrix[:, i * leaf : (i + 1) * leaf, i * leaf : (i + 1) * leaf] for i in range(count)],
        axis=1,
    )
    inverse = small_inverse(diagonal.reshape(heads * count, leaf, leaf))
    inverse = inverse.reshape(heads, count, leaf, leaf)
    width = leaf
    while width < size:
        pairs = size // (2 * width)
        first = inverse[:, 0::2]
        second = inverse[:, 1::2]
        coupling = jnp.stack(
            [
                matrix[:, 2 * j * width : (2 * j + 1) * width, (2 * j + 1) * width : (2 * j + 2) * width]
                for j in range(pairs)
            ],
            axis=1,
        )
        middle = jnp.einsum("hbij,hbjk->hbik", first, coupling, precision=highest)
        corner = -jnp.einsum("hbij,hbjk->hbik", middle, second, precision=highest)
        lower_left = jnp.zeros_like(corner)
        top = jnp.concatenate([first, corner], axis=3)
        bottom = jnp.concatenate([lower_left, second], axis=3)
        inverse = jnp.concatenate([top, bottom], axis=2)
        width = width * 2
    return inverse[:, 0]


def upper_solve(matrix, right_side):
    highest = lax.Precision.HIGHEST
    rows = matrix.shape[1]
    size = min(128, rows)
    count = rows // size
    solved_blocks = []
    for i in reversed(range(count)):
        inverse_block = batched_triangle_inverse(matrix)
        solved_blocks.append(
            jnp.einsum("hij,hjk->hik", inverse_block, right_side, precision=highest)
        )
    return jnp.concatenate(solved_blocks[::-1], axis=1)


def body(seq_count, head_count, features, proj_weight, query_vectors, key_vectors):
    highest = lax.Precision.HIGHEST
    tok_rows = query_vectors.shape[0]
    width = proj_weight.shape[1]
    local_heads = width // HEAD_DIM
    raw_proj = gathered_projection(features, proj_weight, "head", head_count)
    raw_proj = raw_proj.reshape(tok_rows, local_heads, HEAD_DIM)
    directions = raw_proj * lax.rsqrt(jnp.sum(raw_proj * raw_proj, axis=-1, keepdims=True) + 1e-06)
    reflectors = jnp.transpose(directions, (1, 0, 2))
    targets = jnp.concatenate(
        [
            query_vectors.reshape(tok_rows, local_heads, HEAD_DIM),
            key_vectors.reshape(tok_rows, local_heads, HEAD_DIM),
        ],
        axis=0,
    )
    targets = jnp.transpose(targets.astype(jnp.float32), (1, 0, 2))
    gram = jnp.einsum("hid,hjd->hij", reflectors, reflectors, precision=highest)
    position = jnp.arange(tok_rows)
    upper = (position[:, None] < position[None, :]).astype(jnp.float32)
    identity_tok = jnp.eye(tok_rows, dtype=jnp.float32)
    inverse_t = gram * upper[None] + 0.5 * identity_tok[None]
    projected = jnp.einsum("hid,htd->hit", reflectors, targets, precision=highest)
    target_pos = jnp.concatenate([position, position])
    keep = (position[:, None] <= target_pos[None, :]).astype(jnp.float32)
    masked = projected * keep[None]
    right_side = jnp.concatenate([masked, reflectors], axis=2)
    solved = upper_solve(inverse_t, right_side)
    weights_tok = solved[:, :, : 2 * tok_rows]
    factor = solved[:, :, 2 * tok_rows :]
    local_part = targets - jnp.einsum("hit,hid->htd", weights_tok, reflectors, precision=highest)
    identity = jnp.broadcast_to(
        jnp.eye(HEAD_DIM, dtype=jnp.float32), (local_heads, HEAD_DIM, HEAD_DIM)
    )
    block_product = identity - jnp.einsum("hid,hie->hde", reflectors, factor, precision=highest)

    def combine(earlier, later):
        return jnp.einsum("hde,hef->hdf", earlier, later, precision=highest)

    row = 8
    if seq_count % row == 0 and seq_count > row and local_heads % row == 0:
        carried = row_entering(block_product, "seq", seq_count, row, combine, identity[0])
    elif seq_count % 2 == 0 and local_heads % 2 == 0:
        carried = paired_entering(block_product, "seq", seq_count, combine, identity[0])
    else:
        carried = entering(block_product, "seq", seq_count, combine, identity)
    rotated = jnp.einsum("hde,hte->htd", carried, local_part, precision=highest)
    rotated = jnp.transpose(rotated, (1, 0, 2))
    rotated_queries = rotated[:tok_rows].reshape(tok_rows, width).astype(jnp.bfloat16)
    rotated_keys = rotated[tok_rows:].reshape(tok_rows, width).astype(jnp.bfloat16)
    return (rotated_queries, rotated_keys)


def solution(mesh):
    in_specs = (P("seq", "head"), P(None, "head"), P("seq", "head"), P("seq", "head"))
    out_specs = (P("seq", "head"), P("seq", "head"))
    return jax.shard_map(functools.partial(body, mesh.shape["seq"], mesh.shape["head"]), mesh=mesh, in_specs=in_specs, out_specs=out_specs, check_vma=False)
```

```python
import functools

import jax
import jax.numpy as jnp
from jax import lax
from jax.sharding import PartitionSpec as P

HEAD_DIM = 128


def entering(array, axis, count, combine, identity):
    place = lax.axis_index(axis)
    start = jnp.broadcast_to(jnp.asarray(identity, array.dtype), array.shape)
    span = array
    before = None
    shift = 1
    while shift < count:
        pairs = [(k, k + shift) for k in range(count - shift)]
        arrived = lax.ppermute(span, axis, pairs)
        reached = place >= shift
        last = shift * 2 >= count
        if before is None:
            before = jnp.where(reached, arrived, start)
            if not last:
                span = jnp.where(reached, combine(arrived, span), span)
        elif last:
            before = jnp.where(reached, combine(arrived, before), before)
        else:
            width = array.shape[-1]
            both = combine(arrived, jnp.concatenate([span, before], axis=-1))
            span = jnp.where(reached, both[..., :width], span)
            before = jnp.where(reached, both[..., width:], before)
        shift = shift * 2
    return before if before is not None else start


def paired_entering(array, axis, count, combine, identity):
    place = lax.axis_index(axis)
    core = place % 2
    first = core == 0
    half = array.shape[0] // 2
    swap = [(k, k ^ 1) for k in range(count)]
    mate = lax.ppermute(array, axis, swap)
    chip = combine(jnp.where(first, array, mate), jnp.where(first, mate, array))
    inner = jnp.where(first, jnp.broadcast_to(identity, array.shape), mate)
    mine = lax.dynamic_slice_in_dim(chip, core * half, half, 0)
    start = jnp.broadcast_to(identity, mine.shape)
    span = mine
    before = start
    shift = 2
    while shift < count:
        pairs = [(k, k + shift) for k in range(count - shift)]
        arrived = lax.ppermute(span, axis, pairs)
        reached = place >= shift
        last = shift * 2 >= count
        if shift == 2:
            before = jnp.where(reached, arrived, start)
            if not last:
                span = jnp.where(reached, combine(arrived, span), span)
        elif last:
            before = jnp.where(reached, combine(arrived, before), before)
        else:
            width = array.shape[-1]
            both = combine(arrived, jnp.concatenate([span, before], axis=-1))
            span = jnp.where(reached, both[..., :width], span)
            before = jnp.where(reached, both[..., width:], before)
        shift = shift * 2
    other = lax.ppermute(before, axis, swap)
    full = jnp.where(
        first,
        jnp.concatenate([before, other], axis=0),
        jnp.concatenate([other, before], axis=0),
    )
    return combine(full, inner)


def strided_scan(array, axis, count, stride, combine, start):
    place = lax.axis_index(axis)
    span = array
    before = start
    shift = stride
    while shift < count:
        pairs = [(k, k + shift) for k in range(count - shift)]
        arrived = lax.ppermute(span, axis, pairs)
        reached = place >= shift
        last = shift * 2 >= count
        if shift == stride:
            before = jnp.where(reached, arrived, start)
            if not last:
                span = jnp.where(reached, combine(arrived, span), span)
        elif last:
            before = jnp.where(reached, combine(arrived, before), before)
        else:
            width = array.shape[-1]
            both = combine(arrived, jnp.concatenate([span, before], axis=-1))
            span = jnp.where(reached, both[..., :width], span)
            before = jnp.where(reached, both[..., width:], before)
        shift = shift * 2
    return before


def row_exchange(pieces, axis, count, row):
    place = lax.axis_index(axis)
    pos = place % row
    got = [pieces(pos)]
    for step in range(1, row):
        pairs = [(k, (k // row) * row + (k % row + step) % row) for k in range(count)]
        got.append(lax.ppermute(pieces((pos + step) % row), axis, pairs))
    order = (pos + row - jnp.arange(row)) % row
    return jnp.take(jnp.stack(got), order, axis=0)


def ring_prefix(array, axis, count, stride, combine, start):
    place = lax.axis_index(axis)
    size = count // stride
    me = place // stride
    got = [array]
    for step in range(1, size):
        pairs = [(k, ((k // stride + step) % size) * stride + k % stride) for k in range(count)]
        got.append(lax.ppermute(array, axis, pairs))
    order = (me + size - jnp.arange(size)) % size
    ordered = jnp.take(jnp.stack(got), order, axis=0)
    prefix = [start]
    for j in range(size - 1):
        prefix.append(combine(prefix[-1], ordered[j]))
    return jnp.take(jnp.stack(prefix), me, axis=0)


def row_entering(array, axis, count, row, combine, identity):
    place = lax.axis_index(axis)
    heads, size = array.shape[0], array.shape[-1]
    share = heads // row
    eye = jnp.broadcast_to(identity, (share, size, size))
    blocks = row_exchange(
        lambda g: lax.dynamic_slice_in_dim(array, g * share, share, 0), axis, count, row
    )
    prefix = [eye]
    for q in range(1, row):
        prefix.append(combine(prefix[-1], blocks[q - 1]))
    whole = combine(prefix[-1], blocks[row - 1])
    outer = ring_prefix(whole, axis, count, row, combine, eye)
    spread = jnp.broadcast_to(outer[None], (row, share, size, size)).reshape(row * share, size, size)
    carried = combine(spread, jnp.stack(prefix).reshape(row * share, size, size))
    carried = carried.reshape(row, share, size, size)
    full = row_exchange(
        lambda q: lax.dynamic_index_in_dim(carried, q, 0, keepdims=False), axis, count, row
    )
    return full.reshape(heads, size, size)


def gathered_projection(features, proj_weight, axis, count):
    place = lax.axis_index(axis)
    got = [features]
    for step in range(1, count):
        pairs = [(k, (k + step) % count) for k in range(count)]
        got.append(lax.ppermute(features, axis, pairs))
    order = (place + count - jnp.arange(count)) % count
    ordered = jnp.take(jnp.stack(got), order, axis=0)
    whole = jnp.concatenate([ordered[j] for j in range(count)], axis=1)
    return jnp.dot(whole, proj_weight, preferred_element_type=jnp.float32)


def small_inverse(matrix):
    highest = lax.Precision.HIGHEST
    size = matrix.shape[-1]
    position = jnp.arange(size)
    strict = (position[:, None] < position[None, :]).astype(jnp.float32)
    eye_block = jnp.eye(size, dtype=jnp.float32)
    power = -2.0 * matrix * strict[None]
    result = eye_block[None] + power
    reach = 2
    while reach < size:
        power = jnp.einsum("hij,hjk->hik", power, power, precision=highest)
        result = result + jnp.einsum("hij,hjk->hik", result, power, precision=highest)
        reach = reach * 2
    return 2.0 * result


def triangle_inverse(matrix):
    highest = lax.Precision.HIGHEST
    size = matrix.shape[-1]
    if size <= 16:
        return small_inverse(matrix)
    half = size // 2
    first = triangle_inverse(matrix[:, :half, :half])
    second = triangle_inverse(matrix[:, half:, half:])
    coupling = matrix[:, :half, half:]
    middle = jnp.einsum("hij,hjk->hik", first, coupling, precision=highest)
    corner = -jnp.einsum("hij,hjk->hik", middle, second, precision=highest)
    lower_left = jnp.zeros((matrix.shape[0], size - half, half), jnp.float32)
    top = jnp.concatenate([first, corner], axis=2)
    bottom = jnp.concatenate([lower_left, second], axis=2)
    return jnp.concatenate([top, bottom], axis=1)


def batched_triangle_inverse(matrix):
    highest = lax.Precision.HIGHEST
    heads, size = matrix.shape[0], matrix.shape[-1]
    leaf = min(16, size)
    count = size // leaf
    diagonal = jnp.stack(
        [matrix[:, i * leaf : (i + 1) * leaf, i * leaf : (i + 1) * leaf] for i in range(count)],
        axis=1,
    )
    inverse = small_inverse(diagonal.reshape(heads * count, leaf, leaf))
    inverse = inverse.reshape(heads, count, leaf, leaf)
    width = leaf
    while width < size:
        pairs = size // (2 * width)
        first = inverse[:, 0::2]
        second = inverse[:, 1::2]
        coupling = jnp.stack(
            [
                matrix[:, 2 * j * width : (2 * j + 1) * width, (2 * j + 1) * width : (2 * j + 2) * width]
                for j in range(pairs)
            ],
            axis=1,
        )
        middle = jnp.einsum("hbij,hbjk->hbik", first, coupling, precision=highest)
        corner = -jnp.einsum("hbij,hbjk->hbik", middle, second, precision=highest)
        lower_left = jnp.zeros_like(corner)
        top = jnp.concatenate([first, corner], axis=3)
        bottom = jnp.concatenate([lower_left, second], axis=3)
        inverse = jnp.concatenate([top, bottom], axis=2)
        width = width * 2
    return inverse[:, 0]


def upper_solve(matrix, right_side):
    highest = lax.Precision.HIGHEST
    rows = matrix.shape[1]
    size = min(128, rows)
    count = rows // size
    solved_blocks = []
    for i in reversed(range(count)):
        inverse_block = batched_triangle_inverse(matrix)
        solved_blocks.append(
            jnp.einsum("hij,hjk->hik", inverse_block, right_side, precision=highest)
        )
    return jnp.concatenate(solved_blocks[::-1], axis=1)


def body(seq_count, head_count, features, proj_weight, query_vectors, key_vectors):
    highest = lax.Precision.HIGHEST
    tok_rows = query_vectors.shape[0]
    width = proj_weight.shape[1]
    local_heads = width // HEAD_DIM
    raw_proj = gathered_projection(features, proj_weight, "head", head_count)
    raw_proj = raw_proj.reshape(tok_rows, local_heads, HEAD_DIM)
    directions = raw_proj * lax.rsqrt(jnp.sum(raw_proj * raw_proj, axis=-1, keepdims=True) + 1e-06)
    reflectors = jnp.transpose(directions, (1, 0, 2))
    targets = jnp.concatenate(
        [
            query_vectors.reshape(tok_rows, local_heads, HEAD_DIM),
            key_vectors.reshape(tok_rows, local_heads, HEAD_DIM),
        ],
        axis=0,
    )
    targets = jnp.transpose(targets.astype(jnp.float32), (1, 0, 2))
    gram = jnp.einsum("hid,hjd->hij", reflectors, reflectors, precision=highest)
    position = jnp.arange(tok_rows)
    upper = (position[:, None] < position[None, :]).astype(jnp.float32)
    identity_tok = jnp.eye(tok_rows, dtype=jnp.float32)
    inverse_t = gram * upper[None] + 0.5 * identity_tok[None]
    projected = jnp.einsum("hid,htd->hit", reflectors, targets, precision=highest)
    target_pos = jnp.concatenate([position, position])
    keep = (position[:, None] <= target_pos[None, :]).astype(jnp.float32)
    masked = projected * keep[None]
    right_side = jnp.concatenate([masked, reflectors], axis=2)
    solved = upper_solve(inverse_t, right_side)
    weights_tok = solved[:, :, : 2 * tok_rows]
    factor = solved[:, :, 2 * tok_rows :]
    local_part = targets - jnp.einsum("hit,hid->htd", weights_tok, reflectors, precision=highest)
    identity = jnp.broadcast_to(
        jnp.eye(HEAD_DIM, dtype=jnp.float32), (local_heads, HEAD_DIM, HEAD_DIM)
    )
    block_product = identity - jnp.einsum("hid,hie->hde", reflectors, factor, precision=highest)

    def combine(earlier, later):
        return jnp.einsum("hde,hef->hdf", earlier, later, precision=highest)

    row = 8
    if seq_count % row == 0 and seq_count > row and local_heads % row == 0:
        carried = row_entering(block_product, "seq", seq_count, row, combine, identity[0])
    elif seq_count % 2 == 0 and local_heads % 2 == 0:
        carried = paired_entering(block_product, "seq", seq_count, combine, identity[0])
    else:
        carried = entering(block_product, "seq", seq_count, combine, identity)
    rotated = jnp.einsum("hde,hte->htd", carried, local_part, precision=highest)
    rotated = jnp.transpose(rotated, (1, 0, 2))
    rotated_queries = rotated[:tok_rows].reshape(tok_rows, width).astype(jnp.bfloat16)
    rotated_keys = rotated[tok_rows:].reshape(tok_rows, width).astype(jnp.bfloat16)
    return (rotated_queries, rotated_keys)


def solution(mesh):
    in_specs = (P("seq", "head"), P(None, "head"), P("seq", "head"), P("seq", "head"))
    out_specs = (P("seq", "head"), P("seq", "head"))
    return jax.shard_map(functools.partial(body, mesh.shape["seq"], mesh.shape["head"]), mesh=mesh, in_specs=in_specs, out_specs=out_specs, check_vma=False)
```

```python
import functools

import jax
import jax.numpy as jnp
from jax import lax
from jax.sharding import PartitionSpec as P

HEAD_DIM = 128


def entering(array, axis, count, combine, identity):
    place = lax.axis_index(axis)
    start = jnp.broadcast_to(jnp.asarray(identity, array.dtype), array.shape)
    span = array
    before = None
    shift = 1
    while shift < count:
        pairs = [(k, k + shift) for k in range(count - shift)]
        arrived = lax.ppermute(span, axis, pairs)
        reached = place >= shift
        last = shift * 2 >= count
        if before is None:
            before = jnp.where(reached, arrived, start)
            if not last:
                span = jnp.where(reached, combine(arrived, span), span)
        elif last:
            before = jnp.where(reached, combine(arrived, before), before)
        else:
            width = array.shape[-1]
            both = combine(arrived, jnp.concatenate([span, before], axis=-1))
            span = jnp.where(reached, both[..., :width], span)
            before = jnp.where(reached, both[..., width:], before)
        shift = shift * 2
    return before if before is not None else start


def paired_entering(array, axis, count, combine, identity):
    place = lax.axis_index(axis)
    core = place % 2
    first = core == 0
    half = array.shape[0] // 2
    swap = [(k, k ^ 1) for k in range(count)]
    mate = lax.ppermute(array, axis, swap)
    chip = combine(jnp.where(first, array, mate), jnp.where(first, mate, array))
    inner = jnp.where(first, jnp.broadcast_to(identity, array.shape), mate)
    mine = lax.dynamic_slice_in_dim(chip, core * half, half, 0)
    start = jnp.broadcast_to(identity, mine.shape)
    span = mine
    before = start
    shift = 2
    while shift < count:
        pairs = [(k, k + shift) for k in range(count - shift)]
        arrived = lax.ppermute(span, axis, pairs)
        reached = place >= shift
        last = shift * 2 >= count
        if shift == 2:
            before = jnp.where(reached, arrived, start)
            if not last:
                span = jnp.where(reached, combine(arrived, span), span)
        elif last:
            before = jnp.where(reached, combine(arrived, before), before)
        else:
            width = array.shape[-1]
            both = combine(arrived, jnp.concatenate([span, before], axis=-1))
            span = jnp.where(reached, both[..., :width], span)
            before = jnp.where(reached, both[..., width:], before)
        shift = shift * 2
    other = lax.ppermute(before, axis, swap)
    full = jnp.where(
        first,
        jnp.concatenate([before, other], axis=0),
        jnp.concatenate([other, before], axis=0),
    )
    return combine(full, inner)


def strided_scan(array, axis, count, stride, combine, start):
    place = lax.axis_index(axis)
    span = array
    before = start
    shift = stride
    while shift < count:
        pairs = [(k, k + shift) for k in range(count - shift)]
        arrived = lax.ppermute(span, axis, pairs)
        reached = place >= shift
        last = shift * 2 >= count
        if shift == stride:
            before = jnp.where(reached, arrived, start)
            if not last:
                span = jnp.where(reached, combine(arrived, span), span)
        elif last:
            before = jnp.where(reached, combine(arrived, before), before)
        else:
            width = array.shape[-1]
            both = combine(arrived, jnp.concatenate([span, before], axis=-1))
            span = jnp.where(reached, both[..., :width], span)
            before = jnp.where(reached, both[..., width:], before)
        shift = shift * 2
    return before


def row_exchange(pieces, axis, count, row):
    place = lax.axis_index(axis)
    pos = place % row
    got = [pieces(pos)]
    for step in range(1, row):
        pairs = [(k, (k // row) * row + (k % row + step) % row) for k in range(count)]
        got.append(lax.ppermute(pieces((pos + step) % row), axis, pairs))
    order = (pos + row - jnp.arange(row)) % row
    return jnp.take(jnp.stack(got), order, axis=0)


def ring_prefix(array, axis, count, stride, combine, start):
    place = lax.axis_index(axis)
    size = count // stride
    me = place // stride
    got = [array]
    for step in range(1, size):
        pairs = [(k, ((k // stride + step) % size) * stride + k % stride) for k in range(count)]
        got.append(lax.ppermute(array, axis, pairs))
    order = (me + size - jnp.arange(size)) % size
    ordered = jnp.take(jnp.stack(got), order, axis=0)
    prefix = [start]
    for j in range(size - 1):
        prefix.append(combine(prefix[-1], ordered[j]))
    return jnp.take(jnp.stack(prefix), me, axis=0)


def row_entering(array, axis, count, row, combine, identity):
    place = lax.axis_index(axis)
    heads, size = array.shape[0], array.shape[-1]
    share = heads // row
    eye = jnp.broadcast_to(identity, (share, size, size))
    blocks = row_exchange(
        lambda g: lax.dynamic_slice_in_dim(array, g * share, share, 0), axis, count, row
    )
    prefix = [eye]
    for q in range(1, row):
        prefix.append(combine(prefix[-1], blocks[q - 1]))
    whole = combine(prefix[-1], blocks[row - 1])
    outer = strided_scan(whole, axis, count, row, combine, eye)
    spread = jnp.broadcast_to(outer[None], (row, share, size, size)).reshape(row * share, size, size)
    carried = combine(spread, jnp.stack(prefix).reshape(row * share, size, size))
    carried = carried.reshape(row, share, size, size)
    full = row_exchange(
        lambda q: lax.dynamic_index_in_dim(carried, q, 0, keepdims=False), axis, count, row
    )
    return full.reshape(heads, size, size)


def gathered_projection(features, proj_weight, axis, count):
    place = lax.axis_index(axis)
    got = [features]
    for step in range(1, count):
        pairs = [(k, (k + step) % count) for k in range(count)]
        got.append(lax.ppermute(features, axis, pairs))
    order = (place + count - jnp.arange(count)) % count
    ordered = jnp.take(jnp.stack(got), order, axis=0)
    whole = jnp.concatenate([ordered[j] for j in range(count)], axis=1)
    return jnp.dot(whole, proj_weight, preferred_element_type=jnp.float32)


def small_inverse(matrix):
    highest = lax.Precision.HIGHEST
    size = matrix.shape[-1]
    position = jnp.arange(size)
    strict = (position[:, None] < position[None, :]).astype(jnp.float32)
    eye_block = jnp.eye(size, dtype=jnp.float32)
    power = -2.0 * matrix * strict[None]
    result = eye_block[None] + power
    reach = 2
    while reach < size:
        power = jnp.einsum("hij,hjk->hik", power, power, precision=highest)
        result = result + jnp.einsum("hij,hjk->hik", result, power, precision=highest)
        reach = reach * 2
    return 2.0 * result


def triangle_inverse(matrix):
    highest = lax.Precision.HIGHEST
    size = matrix.shape[-1]
    if size <= 16:
        return small_inverse(matrix)
    half = size // 2
    first = triangle_inverse(matrix[:, :half, :half])
    second = triangle_inverse(matrix[:, half:, half:])
    coupling = matrix[:, :half, half:]
    middle = jnp.einsum("hij,hjk->hik", first, coupling, precision=highest)
    corner = -jnp.einsum("hij,hjk->hik", middle, second, precision=highest)
    lower_left = jnp.zeros((matrix.shape[0], size - half, half), jnp.float32)
    top = jnp.concatenate([first, corner], axis=2)
    bottom = jnp.concatenate([lower_left, second], axis=2)
    return jnp.concatenate([top, bottom], axis=1)


def batched_triangle_inverse(matrix):
    highest = lax.Precision.HIGHEST
    heads, size = matrix.shape[0], matrix.shape[-1]
    leaf = min(16, size)
    count = size // leaf
    diagonal = jnp.stack(
        [matrix[:, i * leaf : (i + 1) * leaf, i * leaf : (i + 1) * leaf] for i in range(count)],
        axis=1,
    )
    inverse = small_inverse(diagonal.reshape(heads * count, leaf, leaf))
    inverse = inverse.reshape(heads, count, leaf, leaf)
    width = leaf
    while width < size:
        pairs = size // (2 * width)
        first = inverse[:, 0::2]
        second = inverse[:, 1::2]
        coupling = jnp.stack(
            [
                matrix[:, 2 * j * width : (2 * j + 1) * width, (2 * j + 1) * width : (2 * j + 2) * width]
                for j in range(pairs)
            ],
            axis=1,
        )
        middle = jnp.einsum("hbij,hbjk->hbik", first, coupling, precision=highest)
        corner = -jnp.einsum("hbij,hbjk->hbik", middle, second, precision=highest)
        lower_left = jnp.zeros_like(corner)
        top = jnp.concatenate([first, corner], axis=3)
        bottom = jnp.concatenate([lower_left, second], axis=3)
        inverse = jnp.concatenate([top, bottom], axis=2)
        width = width * 2
    return inverse[:, 0]


def upper_solve(matrix, right_side):
    highest = lax.Precision.HIGHEST
    rows = matrix.shape[1]
    size = min(128, rows)
    count = rows // size
    solved_blocks = []
    for i in reversed(range(count)):
        inverse_block = batched_triangle_inverse(matrix)
        solved_blocks.append(
            jnp.einsum("hij,hjk->hik", inverse_block, right_side, precision=highest)
        )
    return jnp.concatenate(solved_blocks[::-1], axis=1)


def body(seq_count, head_count, features, proj_weight, query_vectors, key_vectors):
    highest = lax.Precision.HIGHEST
    tok_rows = query_vectors.shape[0]
    width = proj_weight.shape[1]
    local_heads = width // HEAD_DIM
    raw_proj = gathered_projection(features, proj_weight, "head", head_count)
    raw_proj = raw_proj.reshape(tok_rows, local_heads, HEAD_DIM)
    directions = raw_proj * lax.rsqrt(jnp.sum(raw_proj * raw_proj, axis=-1, keepdims=True) + 1e-06)
    reflectors = jnp.transpose(directions, (1, 0, 2))
    targets = jnp.concatenate(
        [
            query_vectors.reshape(tok_rows, local_heads, HEAD_DIM),
            key_vectors.reshape(tok_rows, local_heads, HEAD_DIM),
        ],
        axis=0,
    )
    targets = jnp.transpose(targets.astype(jnp.float32), (1, 0, 2))
    gram = jnp.einsum("hid,hjd->hij", reflectors, reflectors, precision=highest)
    position = jnp.arange(tok_rows)
    upper = (position[:, None] < position[None, :]).astype(jnp.float32)
    identity_tok = jnp.eye(tok_rows, dtype=jnp.float32)
    inverse_t = gram * upper[None] + 0.5 * identity_tok[None]
    inverse = batched_triangle_inverse(inverse_t)
    factor = jnp.einsum("hij,hjk->hik", inverse, reflectors, precision=highest)
    identity = jnp.broadcast_to(
        jnp.eye(HEAD_DIM, dtype=jnp.float32), (local_heads, HEAD_DIM, HEAD_DIM)
    )
    block_product = identity - jnp.einsum("hid,hie->hde", reflectors, factor, precision=highest)
    projected = jnp.einsum("hid,htd->hit", reflectors, targets, precision=highest)
    target_pos = jnp.concatenate([position, position])
    keep = (position[:, None] <= target_pos[None, :]).astype(jnp.float32)
    masked = projected * keep[None]
    weights_tok = jnp.einsum("hij,hjk->hik", inverse, masked, precision=highest)
    local_part = targets - jnp.einsum("hit,hid->htd", weights_tok, reflectors, precision=highest)

    def combine(earlier, later):
        return jnp.einsum("hde,hef->hdf", earlier, later, precision=highest)

    row = 8
    if seq_count % row == 0 and seq_count > row and local_heads % row == 0:
        carried = row_entering(block_product, "seq", seq_count, row, combine, identity[0])
    elif seq_count % 2 == 0 and local_heads % 2 == 0:
        carried = paired_entering(block_product, "seq", seq_count, combine, identity[0])
    else:
        carried = entering(block_product, "seq", seq_count, combine, identity)
    rotated = jnp.einsum("hde,hte->htd", carried, local_part, precision=highest)
    rotated = jnp.transpose(rotated, (1, 0, 2))
    rotated_queries = rotated[:tok_rows].reshape(tok_rows, width).astype(jnp.bfloat16)
    rotated_keys = rotated[tok_rows:].reshape(tok_rows, width).astype(jnp.bfloat16)
    return (rotated_queries, rotated_keys)


def solution(mesh):
    in_specs = (P("seq", "head"), P(None, "head"), P("seq", "head"), P("seq", "head"))
    out_specs = (P("seq", "head"), P("seq", "head"))
    return jax.shard_map(functools.partial(body, mesh.shape["seq"], mesh.shape["head"]), mesh=mesh, in_specs=in_specs, out_specs=out_specs, check_vma=False)
```

```python
import functools

import jax
import jax.numpy as jnp
from jax import lax
from jax.sharding import PartitionSpec as P

HEAD_DIM = 128


def entering(array, axis, count, combine, identity):
    place = lax.axis_index(axis)
    start = jnp.broadcast_to(jnp.asarray(identity, array.dtype), array.shape)
    span = array
    before = None
    shift = 1
    while shift < count:
        pairs = [(k, k + shift) for k in range(count - shift)]
        arrived = lax.ppermute(span, axis, pairs)
        reached = place >= shift
        last = shift * 2 >= count
        if before is None:
            before = jnp.where(reached, arrived, start)
            if not last:
                span = jnp.where(reached, combine(arrived, span), span)
        elif last:
            before = jnp.where(reached, combine(arrived, before), before)
        else:
            width = array.shape[-1]
            both = combine(arrived, jnp.concatenate([span, before], axis=-1))
            span = jnp.where(reached, both[..., :width], span)
            before = jnp.where(reached, both[..., width:], before)
        shift = shift * 2
    return before if before is not None else start


def paired_entering(array, axis, count, combine, identity):
    place = lax.axis_index(axis)
    core = place % 2
    first = core == 0
    half = array.shape[0] // 2
    swap = [(k, k ^ 1) for k in range(count)]
    mate = lax.ppermute(array, axis, swap)
    chip = combine(jnp.where(first, array, mate), jnp.where(first, mate, array))
    inner = jnp.where(first, jnp.broadcast_to(identity, array.shape), mate)
    mine = lax.dynamic_slice_in_dim(chip, core * half, half, 0)
    start = jnp.broadcast_to(identity, mine.shape)
    span = mine
    before = start
    shift = 2
    while shift < count:
        pairs = [(k, k + shift) for k in range(count - shift)]
        arrived = lax.ppermute(span, axis, pairs)
        reached = place >= shift
        last = shift * 2 >= count
        if shift == 2:
            before = jnp.where(reached, arrived, start)
            if not last:
                span = jnp.where(reached, combine(arrived, span), span)
        elif last:
            before = jnp.where(reached, combine(arrived, before), before)
        else:
            width = array.shape[-1]
            both = combine(arrived, jnp.concatenate([span, before], axis=-1))
            span = jnp.where(reached, both[..., :width], span)
            before = jnp.where(reached, both[..., width:], before)
        shift = shift * 2
    other = lax.ppermute(before, axis, swap)
    full = jnp.where(
        first,
        jnp.concatenate([before, other], axis=0),
        jnp.concatenate([other, before], axis=0),
    )
    return combine(full, inner)


def strided_scan(array, axis, count, stride, combine, start):
    place = lax.axis_index(axis)
    span = array
    before = start
    shift = stride
    while shift < count:
        pairs = [(k, k + shift) for k in range(count - shift)]
        arrived = lax.ppermute(span, axis, pairs)
        reached = place >= shift
        last = shift * 2 >= count
        if shift == stride:
            before = jnp.where(reached, arrived, start)
            if not last:
                span = jnp.where(reached, combine(arrived, span), span)
        elif last:
            before = jnp.where(reached, combine(arrived, before), before)
        else:
            width = array.shape[-1]
            both = combine(arrived, jnp.concatenate([span, before], axis=-1))
            span = jnp.where(reached, both[..., :width], span)
            before = jnp.where(reached, both[..., width:], before)
        shift = shift * 2
    return before


def row_exchange(pieces, axis, count, row):
    place = lax.axis_index(axis)
    pos = place % row
    got = [pieces(pos)]
    for step in range(1, row):
        pairs = [(k, (k // row) * row + (k % row + step) % row) for k in range(count)]
        got.append(lax.ppermute(pieces((pos + step) % row), axis, pairs))
    order = (pos + row - jnp.arange(row)) % row
    return jnp.take(jnp.stack(got), order, axis=0)


def ring_prefix(array, axis, count, stride, combine, start):
    place = lax.axis_index(axis)
    size = count // stride
    me = place // stride
    got = [array]
    for step in range(1, size):
        pairs = [(k, ((k // stride + step) % size) * stride + k % stride) for k in range(count)]
        got.append(lax.ppermute(array, axis, pairs))
    order = (me + size - jnp.arange(size)) % size
    ordered = jnp.take(jnp.stack(got), order, axis=0)
    prefix = [start]
    for j in range(size - 1):
        prefix.append(combine(prefix[-1], ordered[j]))
    return jnp.take(jnp.stack(prefix), me, axis=0)


def flat_combine(combine, earlier, later):
    shape = later.shape
    size = shape[-1]
    merged = combine(earlier.reshape(-1, size, size), later.reshape(-1, size, size))
    return merged.reshape(shape)


def near_far_prefix(array, axis, count, stride, combine, start):
    place = lax.axis_index(axis)
    size = count // stride
    me = place // stride

    def shifted(value, step):
        pairs = [(k, ((k // stride + step) % size) * stride + k % stride) for k in range(count)]
        return lax.ppermute(value, axis, pairs)

    trio = jnp.stack([shifted(array, 1), array, shifted(array, size - 1)])
    far_left = shifted(trio, 3)
    far_right = shifted(trio, size - 3)
    by_offset = jnp.stack(
        [trio[1], trio[2], far_right[0], far_right[1], far_right[2], far_left[1], far_left[2], trio[0]]
    )
    rows = jnp.arange(size)
    ordered = jnp.take(by_offset, (rows + size - me) % size, axis=0)
    keep = (rows < me).reshape((size,) + (1,) * array.ndim)
    terms = jnp.where(keep, ordered, jnp.broadcast_to(start, ordered.shape))
    while terms.shape[0] > 1:
        terms = flat_combine(combine, terms[0::2], terms[1::2])
    return terms[0]


def row_entering(array, axis, count, row, combine, identity):
    place = lax.axis_index(axis)
    heads, size = array.shape[0], array.shape[-1]
    share = heads // row
    eye = jnp.broadcast_to(identity, (share, size, size))
    blocks = row_exchange(
        lambda g: lax.dynamic_slice_in_dim(array, g * share, share, 0), axis, count, row
    )
    spans = blocks
    step = 1
    while step < row:
        moved = flat_combine(combine, spans[:-step], spans[step:])
        spans = jnp.concatenate([spans[:step], moved], axis=0)
        step = step * 2
    prefix = jnp.concatenate([eye[None], spans[:-1]], axis=0)
    whole = spans[-1]
    if count // row == 8:
        outer = near_far_prefix(whole, axis, count, row, combine, eye)
    else:
        outer = strided_scan(whole, axis, count, row, combine, eye)
    spread = jnp.broadcast_to(outer[None], (row, share, size, size)).reshape(row * share, size, size)
    carried = combine(spread, prefix.reshape(row * share, size, size))
    carried = carried.reshape(row, share, size, size)
    full = row_exchange(
        lambda q: lax.dynamic_index_in_dim(carried, q, 0, keepdims=False), axis, count, row
    )
    return full.reshape(heads, size, size)


def gathered_projection(features, proj_weight, axis, count):
    place = lax.axis_index(axis)
    got = [features]
    for step in range(1, count):
        pairs = [(k, (k + step) % count) for k in range(count)]
        got.append(lax.ppermute(features, axis, pairs))
    order = (place + count - jnp.arange(count)) % count
    ordered = jnp.take(jnp.stack(got), order, axis=0)
    whole = jnp.concatenate([ordered[j] for j in range(count)], axis=1)
    return jnp.dot(whole, proj_weight, preferred_element_type=jnp.float32)


def small_inverse(matrix):
    highest = lax.Precision.HIGHEST
    size = matrix.shape[-1]
    position = jnp.arange(size)
    strict = (position[:, None] < position[None, :]).astype(jnp.float32)
    eye_block = jnp.eye(size, dtype=jnp.float32)
    power = -2.0 * matrix * strict[None]
    result = eye_block[None] + power
    reach = 2
    while reach < size:
        power = jnp.einsum("hij,hjk->hik", power, power, precision=highest)
        result = result + jnp.einsum("hij,hjk->hik", result, power, precision=highest)
        reach = reach * 2
    return 2.0 * result


def triangle_inverse(matrix):
    highest = lax.Precision.HIGHEST
    size = matrix.shape[-1]
    if size <= 16:
        return small_inverse(matrix)
    half = size // 2
    first = triangle_inverse(matrix[:, :half, :half])
    second = triangle_inverse(matrix[:, half:, half:])
    coupling = matrix[:, :half, half:]
    middle = jnp.einsum("hij,hjk->hik", first, coupling, precision=highest)
    corner = -jnp.einsum("hij,hjk->hik", middle, second, precision=highest)
    lower_left = jnp.zeros((matrix.shape[0], size - half, half), jnp.float32)
    top = jnp.concatenate([first, corner], axis=2)
    bottom = jnp.concatenate([lower_left, second], axis=2)
    return jnp.concatenate([top, bottom], axis=1)


def batched_triangle_inverse(matrix):
    highest = lax.Precision.HIGHEST
    heads, size = matrix.shape[0], matrix.shape[-1]
    leaf = min(16, size)
    count = size // leaf
    diagonal = jnp.stack(
        [matrix[:, i * leaf : (i + 1) * leaf, i * leaf : (i + 1) * leaf] for i in range(count)],
        axis=1,
    )
    inverse = small_inverse(diagonal.reshape(heads * count, leaf, leaf))
    inverse = inverse.reshape(heads, count, leaf, leaf)
    width = leaf
    while width < size:
        pairs = size // (2 * width)
        first = inverse[:, 0::2]
        second = inverse[:, 1::2]
        coupling = jnp.stack(
            [
                matrix[:, 2 * j * width : (2 * j + 1) * width, (2 * j + 1) * width : (2 * j + 2) * width]
                for j in range(pairs)
            ],
            axis=1,
        )
        middle = jnp.einsum("hbij,hbjk->hbik", first, coupling, precision=highest)
        corner = -jnp.einsum("hbij,hbjk->hbik", middle, second, precision=highest)
        lower_left = jnp.zeros_like(corner)
        top = jnp.concatenate([first, corner], axis=3)
        bottom = jnp.concatenate([lower_left, second], axis=3)
        inverse = jnp.concatenate([top, bottom], axis=2)
        width = width * 2
    return inverse[:, 0]


def upper_solve(matrix, right_side):
    highest = lax.Precision.HIGHEST
    rows = matrix.shape[1]
    size = min(128, rows)
    count = rows // size
    solved_blocks = []
    for i in reversed(range(count)):
        inverse_block = batched_triangle_inverse(matrix)
        solved_blocks.append(
            jnp.einsum("hij,hjk->hik", inverse_block, right_side, precision=highest)
        )
    return jnp.concatenate(solved_blocks[::-1], axis=1)


def body(seq_count, head_count, features, proj_weight, query_vectors, key_vectors):
    highest = lax.Precision.HIGHEST
    tok_rows = query_vectors.shape[0]
    width = proj_weight.shape[1]
    local_heads = width // HEAD_DIM
    raw_proj = gathered_projection(features, proj_weight, "head", head_count)
    raw_proj = raw_proj.reshape(tok_rows, local_heads, HEAD_DIM)
    directions = raw_proj * lax.rsqrt(jnp.sum(raw_proj * raw_proj, axis=-1, keepdims=True) + 1e-06)
    reflectors = jnp.transpose(directions, (1, 0, 2))
    targets = jnp.concatenate(
        [
            query_vectors.reshape(tok_rows, local_heads, HEAD_DIM),
            key_vectors.reshape(tok_rows, local_heads, HEAD_DIM),
        ],
        axis=0,
    )
    targets = jnp.transpose(targets.astype(jnp.float32), (1, 0, 2))
    gram = jnp.einsum("hid,hjd->hij", reflectors, reflectors, precision=highest)
    position = jnp.arange(tok_rows)
    upper = (position[:, None] < position[None, :]).astype(jnp.float32)
    identity_tok = jnp.eye(tok_rows, dtype=jnp.float32)
    inverse_t = gram * upper[None] + 0.5 * identity_tok[None]
    inverse = batched_triangle_inverse(inverse_t)
    factor = jnp.einsum("hij,hjk->hik", inverse, reflectors, precision=highest)
    identity = jnp.broadcast_to(
        jnp.eye(HEAD_DIM, dtype=jnp.float32), (local_heads, HEAD_DIM, HEAD_DIM)
    )
    block_product = identity - jnp.einsum("hid,hie->hde", reflectors, factor, precision=highest)
    projected = jnp.einsum("hid,htd->hit", reflectors, targets, precision=highest)
    target_pos = jnp.concatenate([position, position])
    keep = (position[:, None] <= target_pos[None, :]).astype(jnp.float32)
    masked = projected * keep[None]
    weights_tok = jnp.einsum("hij,hjk->hik", inverse, masked, precision=highest)
    local_part = targets - jnp.einsum("hit,hid->htd", weights_tok, reflectors, precision=highest)

    def combine(earlier, later):
        return jnp.einsum("hde,hef->hdf", earlier, later, precision=highest)

    row = 8
    if seq_count % row == 0 and seq_count > row and local_heads % row == 0:
        carried = row_entering(block_product, "seq", seq_count, row, combine, identity[0])
    elif seq_count % 2 == 0 and local_heads % 2 == 0:
        carried = paired_entering(block_product, "seq", seq_count, combine, identity[0])
    else:
        carried = entering(block_product, "seq", seq_count, combine, identity)
    rotated = jnp.einsum("hde,hte->htd", carried, local_part, precision=highest)
    rotated = jnp.transpose(rotated, (1, 0, 2))
    rotated_queries = rotated[:tok_rows].reshape(tok_rows, width).astype(jnp.bfloat16)
    rotated_keys = rotated[tok_rows:].reshape(tok_rows, width).astype(jnp.bfloat16)
    return (rotated_queries, rotated_keys)


def solution(mesh):
    in_specs = (P("seq", "head"), P(None, "head"), P("seq", "head"), P("seq", "head"))
    out_specs = (P("seq", "head"), P("seq", "head"))
    return jax.shard_map(functools.partial(body, mesh.shape["seq"], mesh.shape["head"]), mesh=mesh, in_specs=in_specs, out_specs=out_specs, check_vma=False)
```

```python
import functools

import jax
import jax.numpy as jnp
from jax import lax
from jax.sharding import PartitionSpec as P

HEAD_DIM = 128


def entering(array, axis, count, combine, identity):
    place = lax.axis_index(axis)
    start = jnp.broadcast_to(jnp.asarray(identity, array.dtype), array.shape)
    span = array
    before = None
    shift = 1
    while shift < count:
        pairs = [(k, k + shift) for k in range(count - shift)]
        arrived = lax.ppermute(span, axis, pairs)
        reached = place >= shift
        last = shift * 2 >= count
        if before is None:
            before = jnp.where(reached, arrived, start)
            if not last:
                span = jnp.where(reached, combine(arrived, span), span)
        elif last:
            before = jnp.where(reached, combine(arrived, before), before)
        else:
            width = array.shape[-1]
            both = combine(arrived, jnp.concatenate([span, before], axis=-1))
            span = jnp.where(reached, both[..., :width], span)
            before = jnp.where(reached, both[..., width:], before)
        shift = shift * 2
    return before if before is not None else start


def paired_entering(array, axis, count, combine, identity):
    place = lax.axis_index(axis)
    core = place % 2
    first = core == 0
    half = array.shape[0] // 2
    swap = [(k, k ^ 1) for k in range(count)]
    mate = lax.ppermute(array, axis, swap)
    chip = combine(jnp.where(first, array, mate), jnp.where(first, mate, array))
    inner = jnp.where(first, jnp.broadcast_to(identity, array.shape), mate)
    mine = lax.dynamic_slice_in_dim(chip, core * half, half, 0)
    start = jnp.broadcast_to(identity, mine.shape)
    span = mine
    before = start
    shift = 2
    while shift < count:
        pairs = [(k, k + shift) for k in range(count - shift)]
        arrived = lax.ppermute(span, axis, pairs)
        reached = place >= shift
        last = shift * 2 >= count
        if shift == 2:
            before = jnp.where(reached, arrived, start)
            if not last:
                span = jnp.where(reached, combine(arrived, span), span)
        elif last:
            before = jnp.where(reached, combine(arrived, before), before)
        else:
            width = array.shape[-1]
            both = combine(arrived, jnp.concatenate([span, before], axis=-1))
            span = jnp.where(reached, both[..., :width], span)
            before = jnp.where(reached, both[..., width:], before)
        shift = shift * 2
    other = lax.ppermute(before, axis, swap)
    full = jnp.where(
        first,
        jnp.concatenate([before, other], axis=0),
        jnp.concatenate([other, before], axis=0),
    )
    return combine(full, inner)


def strided_scan(array, axis, count, stride, combine, start):
    place = lax.axis_index(axis)
    span = array
    before = start
    shift = stride
    while shift < count:
        pairs = [(k, k + shift) for k in range(count - shift)]
        arrived = lax.ppermute(span, axis, pairs)
        reached = place >= shift
        last = shift * 2 >= count
        if shift == stride:
            before = jnp.where(reached, arrived, start)
            if not last:
                span = jnp.where(reached, combine(arrived, span), span)
        elif last:
            before = jnp.where(reached, combine(arrived, before), before)
        else:
            width = array.shape[-1]
            both = combine(arrived, jnp.concatenate([span, before], axis=-1))
            span = jnp.where(reached, both[..., :width], span)
            before = jnp.where(reached, both[..., width:], before)
        shift = shift * 2
    return before


def row_exchange(pieces, axis, count, row):
    place = lax.axis_index(axis)
    pos = place % row
    got = [pieces(pos)]
    for step in range(1, row):
        pairs = [(k, (k // row) * row + (k % row + step) % row) for k in range(count)]
        got.append(lax.ppermute(pieces((pos + step) % row), axis, pairs))
    order = (pos + row - jnp.arange(row)) % row
    return jnp.take(jnp.stack(got), order, axis=0)


def ring_prefix(array, axis, count, stride, combine, start):
    place = lax.axis_index(axis)
    size = count // stride
    me = place // stride
    got = [array]
    for step in range(1, size):
        pairs = [(k, ((k // stride + step) % size) * stride + k % stride) for k in range(count)]
        got.append(lax.ppermute(array, axis, pairs))
    order = (me + size - jnp.arange(size)) % size
    ordered = jnp.take(jnp.stack(got), order, axis=0)
    prefix = [start]
    for j in range(size - 1):
        prefix.append(combine(prefix[-1], ordered[j]))
    return jnp.take(jnp.stack(prefix), me, axis=0)


def flat_combine(combine, earlier, later):
    shape = later.shape
    size = shape[-1]
    merged = combine(earlier.reshape(-1, size, size), later.reshape(-1, size, size))
    return merged.reshape(shape)


def row_entering(array, axis, count, row, combine, identity):
    place = lax.axis_index(axis)
    heads, size = array.shape[0], array.shape[-1]
    share = heads // row
    eye = jnp.broadcast_to(identity, (share, size, size))
    blocks = row_exchange(
        lambda g: lax.dynamic_slice_in_dim(array, g * share, share, 0), axis, count, row
    )
    spans = blocks
    step = 1
    while step < row:
        moved = flat_combine(combine, spans[:-step], spans[step:])
        spans = jnp.concatenate([spans[:step], moved], axis=0)
        step = step * 2
    prefix = jnp.concatenate([eye[None], spans[:-1]], axis=0)
    whole = spans[-1]
    outer = strided_scan(whole, axis, count, row, combine, eye)
    spread = jnp.broadcast_to(outer[None], (row, share, size, size)).reshape(row * share, size, size)
    carried = combine(spread, prefix.reshape(row * share, size, size))
    carried = carried.reshape(row, share, size, size)
    full = row_exchange(
        lambda q: lax.dynamic_index_in_dim(carried, q, 0, keepdims=False), axis, count, row
    )
    return full.reshape(heads, size, size)


def gathered_projection(features, proj_weight, axis, count):
    place = lax.axis_index(axis)
    got = [features]
    for step in range(1, count):
        pairs = [(k, (k + step) % count) for k in range(count)]
        got.append(lax.ppermute(features, axis, pairs))
    order = (place + count - jnp.arange(count)) % count
    ordered = jnp.take(jnp.stack(got), order, axis=0)
    whole = jnp.concatenate([ordered[j] for j in range(count)], axis=1)
    return jnp.dot(whole, proj_weight, preferred_element_type=jnp.float32)


def small_inverse(matrix):
    highest = lax.Precision.HIGHEST
    size = matrix.shape[-1]
    position = jnp.arange(size)
    strict = (position[:, None] < position[None, :]).astype(jnp.float32)
    eye_block = jnp.eye(size, dtype=jnp.float32)
    power = -2.0 * matrix * strict[None]
    result = eye_block[None] + power
    reach = 2
    while reach < size:
        power = jnp.einsum("hij,hjk->hik", power, power, precision=highest)
        result = result + jnp.einsum("hij,hjk->hik", result, power, precision=highest)
        reach = reach * 2
    return 2.0 * result


def triangle_inverse(matrix):
    highest = lax.Precision.HIGHEST
    size = matrix.shape[-1]
    if size <= 16:
        return small_inverse(matrix)
    half = size // 2
    first = triangle_inverse(matrix[:, :half, :half])
    second = triangle_inverse(matrix[:, half:, half:])
    coupling = matrix[:, :half, half:]
    middle = jnp.einsum("hij,hjk->hik", first, coupling, precision=highest)
    corner = -jnp.einsum("hij,hjk->hik", middle, second, precision=highest)
    lower_left = jnp.zeros((matrix.shape[0], size - half, half), jnp.float32)
    top = jnp.concatenate([first, corner], axis=2)
    bottom = jnp.concatenate([lower_left, second], axis=2)
    return jnp.concatenate([top, bottom], axis=1)


def batched_triangle_inverse(matrix):
    highest = lax.Precision.HIGHEST
    heads, size = matrix.shape[0], matrix.shape[-1]
    leaf = min(16, size)
    count = size // leaf
    diagonal = jnp.stack(
        [matrix[:, i * leaf : (i + 1) * leaf, i * leaf : (i + 1) * leaf] for i in range(count)],
        axis=1,
    )
    inverse = small_inverse(diagonal.reshape(heads * count, leaf, leaf))
    inverse = inverse.reshape(heads, count, leaf, leaf)
    width = leaf
    while width < size:
        pairs = size // (2 * width)
        first = inverse[:, 0::2]
        second = inverse[:, 1::2]
        coupling = jnp.stack(
            [
                matrix[:, 2 * j * width : (2 * j + 1) * width, (2 * j + 1) * width : (2 * j + 2) * width]
                for j in range(pairs)
            ],
            axis=1,
        )
        middle = jnp.einsum("hbij,hbjk->hbik", first, coupling, precision=highest)
        corner = -jnp.einsum("hbij,hbjk->hbik", middle, second, precision=highest)
        lower_left = jnp.zeros_like(corner)
        top = jnp.concatenate([first, corner], axis=3)
        bottom = jnp.concatenate([lower_left, second], axis=3)
        inverse = jnp.concatenate([top, bottom], axis=2)
        width = width * 2
    return inverse[:, 0]


def upper_solve(matrix, right_side):
    highest = lax.Precision.HIGHEST
    rows = matrix.shape[1]
    size = min(128, rows)
    count = rows // size
    solved_blocks = []
    for i in reversed(range(count)):
        inverse_block = batched_triangle_inverse(matrix)
        solved_blocks.append(
            jnp.einsum("hij,hjk->hik", inverse_block, right_side, precision=highest)
        )
    return jnp.concatenate(solved_blocks[::-1], axis=1)


def body(seq_count, head_count, features, proj_weight, query_vectors, key_vectors):
    highest = lax.Precision.HIGHEST
    tok_rows = query_vectors.shape[0]
    width = proj_weight.shape[1]
    local_heads = width // HEAD_DIM
    raw_proj = gathered_projection(features, proj_weight, "head", head_count)
    raw_proj = raw_proj.reshape(tok_rows, local_heads, HEAD_DIM)
    directions = raw_proj * lax.rsqrt(jnp.sum(raw_proj * raw_proj, axis=-1, keepdims=True) + 1e-06)
    reflectors = jnp.transpose(directions, (1, 0, 2))
    targets = jnp.concatenate(
        [
            query_vectors.reshape(tok_rows, local_heads, HEAD_DIM),
            key_vectors.reshape(tok_rows, local_heads, HEAD_DIM),
        ],
        axis=0,
    )
    targets = jnp.transpose(targets.astype(jnp.float32), (1, 0, 2))
    gram = jnp.einsum("hid,hjd->hij", reflectors, reflectors, precision=highest)
    position = jnp.arange(tok_rows)
    upper = (position[:, None] < position[None, :]).astype(jnp.float32)
    identity_tok = jnp.eye(tok_rows, dtype=jnp.float32)
    inverse_t = gram * upper[None] + 0.5 * identity_tok[None]
    inverse = batched_triangle_inverse(inverse_t)
    factor = jnp.einsum("hij,hjk->hik", inverse, reflectors, precision=highest)
    identity = jnp.broadcast_to(
        jnp.eye(HEAD_DIM, dtype=jnp.float32), (local_heads, HEAD_DIM, HEAD_DIM)
    )
    block_product = identity - jnp.einsum("hid,hie->hde", reflectors, factor, precision=highest)
    projected = jnp.einsum("hid,htd->hit", reflectors, targets, precision=highest)
    target_pos = jnp.concatenate([position, position])
    keep = (position[:, None] <= target_pos[None, :]).astype(jnp.float32)
    masked = projected * keep[None]
    weights_tok = jnp.einsum("hij,hjk->hik", inverse, masked, precision=highest)
    local_part = targets - jnp.einsum("hit,hid->htd", weights_tok, reflectors, precision=highest)

    def combine(earlier, later):
        return jnp.einsum("hde,hef->hdf", earlier, later, precision=highest)

    row = 8
    if seq_count % row == 0 and seq_count > row and local_heads % row == 0:
        carried = row_entering(block_product, "seq", seq_count, row, combine, identity[0])
    elif seq_count % 2 == 0 and local_heads % 2 == 0:
        carried = paired_entering(block_product, "seq", seq_count, combine, identity[0])
    else:
        carried = entering(block_product, "seq", seq_count, combine, identity)
    rotated = jnp.einsum("hde,hte->htd", carried, local_part, precision=highest)
    rotated = jnp.transpose(rotated, (1, 0, 2))
    rotated_queries = rotated[:tok_rows].reshape(tok_rows, width).astype(jnp.bfloat16)
    rotated_keys = rotated[tok_rows:].reshape(tok_rows, width).astype(jnp.bfloat16)
    return (rotated_queries, rotated_keys)


def solution(mesh):
    in_specs = (P("seq", "head"), P(None, "head"), P("seq", "head"), P("seq", "head"))
    out_specs = (P("seq", "head"), P("seq", "head"))
    return jax.shard_map(functools.partial(body, mesh.shape["seq"], mesh.shape["head"]), mesh=mesh, in_specs=in_specs, out_specs=out_specs, check_vma=False)
```

```python
import functools

import jax
import jax.numpy as jnp
from jax import lax
from jax.sharding import PartitionSpec as P

HEAD_DIM = 128


def entering(array, axis, count, combine, identity):
    place = lax.axis_index(axis)
    start = jnp.broadcast_to(jnp.asarray(identity, array.dtype), array.shape)
    span = array
    before = None
    shift = 1
    while shift < count:
        pairs = [(k, k + shift) for k in range(count - shift)]
        arrived = lax.ppermute(span, axis, pairs)
        reached = place >= shift
        last = shift * 2 >= count
        if before is None:
            before = jnp.where(reached, arrived, start)
            if not last:
                span = jnp.where(reached, combine(arrived, span), span)
        elif last:
            before = jnp.where(reached, combine(arrived, before), before)
        else:
            width = array.shape[-1]
            both = combine(arrived, jnp.concatenate([span, before], axis=-1))
            span = jnp.where(reached, both[..., :width], span)
            before = jnp.where(reached, both[..., width:], before)
        shift = shift * 2
    return before if before is not None else start


def paired_entering(array, axis, count, combine, identity):
    place = lax.axis_index(axis)
    core = place % 2
    first = core == 0
    half = array.shape[0] // 2
    swap = [(k, k ^ 1) for k in range(count)]
    mate = lax.ppermute(array, axis, swap)
    chip = combine(jnp.where(first, array, mate), jnp.where(first, mate, array))
    inner = jnp.where(first, jnp.broadcast_to(identity, array.shape), mate)
    mine = lax.dynamic_slice_in_dim(chip, core * half, half, 0)
    start = jnp.broadcast_to(identity, mine.shape)
    span = mine
    before = start
    shift = 2
    while shift < count:
        pairs = [(k, k + shift) for k in range(count - shift)]
        arrived = lax.ppermute(span, axis, pairs)
        reached = place >= shift
        last = shift * 2 >= count
        if shift == 2:
            before = jnp.where(reached, arrived, start)
            if not last:
                span = jnp.where(reached, combine(arrived, span), span)
        elif last:
            before = jnp.where(reached, combine(arrived, before), before)
        else:
            width = array.shape[-1]
            both = combine(arrived, jnp.concatenate([span, before], axis=-1))
            span = jnp.where(reached, both[..., :width], span)
            before = jnp.where(reached, both[..., width:], before)
        shift = shift * 2
    other = lax.ppermute(before, axis, swap)
    full = jnp.where(
        first,
        jnp.concatenate([before, other], axis=0),
        jnp.concatenate([other, before], axis=0),
    )
    return combine(full, inner)


def strided_scan(array, axis, count, stride, combine, start):
    place = lax.axis_index(axis)
    span = array
    before = start
    shift = stride
    while shift < count:
        pairs = [(k, k + shift) for k in range(count - shift)]
        arrived = lax.ppermute(span, axis, pairs)
        reached = place >= shift
        last = shift * 2 >= count
        if shift == stride:
            before = jnp.where(reached, arrived, start)
            if not last:
                span = jnp.where(reached, combine(arrived, span), span)
        elif last:
            before = jnp.where(reached, combine(arrived, before), before)
        else:
            width = array.shape[-1]
            both = combine(arrived, jnp.concatenate([span, before], axis=-1))
            span = jnp.where(reached, both[..., :width], span)
            before = jnp.where(reached, both[..., width:], before)
        shift = shift * 2
    return before


def ternary_scan(array, axis, count, stride, combine, start):
    place = lax.axis_index(axis)
    span = array
    before = start
    width = array.shape[-1]
    reach = stride
    while reach < count:
        near = lax.ppermute(span, axis, [(k, k + reach) for k in range(count - reach)])
        lead = jnp.where(place >= reach, near, start)
        if 2 * reach < count:
            far = lax.ppermute(span, axis, [(k, k + 2 * reach) for k in range(count - 2 * reach)])
            lead = combine(jnp.where(place >= 2 * reach, far, start), lead)
        if 3 * reach < count:
            both = combine(lead, jnp.concatenate([span, before], axis=-1))
            span = both[..., :width]
            before = both[..., width:]
        else:
            before = combine(lead, before)
        reach = reach * 3
    return before


def row_exchange(pieces, axis, count, row):
    place = lax.axis_index(axis)
    pos = place % row
    got = [pieces(pos)]
    for step in range(1, row):
        pairs = [(k, (k // row) * row + (k % row + step) % row) for k in range(count)]
        got.append(lax.ppermute(pieces((pos + step) % row), axis, pairs))
    order = (pos + row - jnp.arange(row)) % row
    return jnp.take(jnp.stack(got), order, axis=0)


def ring_prefix(array, axis, count, stride, combine, start):
    place = lax.axis_index(axis)
    size = count // stride
    me = place // stride
    got = [array]
    for step in range(1, size):
        pairs = [(k, ((k // stride + step) % size) * stride + k % stride) for k in range(count)]
        got.append(lax.ppermute(array, axis, pairs))
    order = (me + size - jnp.arange(size)) % size
    ordered = jnp.take(jnp.stack(got), order, axis=0)
    prefix = [start]
    for j in range(size - 1):
        prefix.append(combine(prefix[-1], ordered[j]))
    return jnp.take(jnp.stack(prefix), me, axis=0)


def flat_combine(combine, earlier, later):
    shape = later.shape
    size = shape[-1]
    merged = combine(earlier.reshape(-1, size, size), later.reshape(-1, size, size))
    return merged.reshape(shape)


def row_entering(array, axis, count, row, combine, identity):
    place = lax.axis_index(axis)
    heads, size = array.shape[0], array.shape[-1]
    share = heads // row
    eye = jnp.broadcast_to(identity, (share, size, size))
    blocks = row_exchange(
        lambda g: lax.dynamic_slice_in_dim(array, g * share, share, 0), axis, count, row
    )
    spans = blocks
    step = 1
    while step < row:
        moved = flat_combine(combine, spans[:-step], spans[step:])
        spans = jnp.concatenate([spans[:step], moved], axis=0)
        step = step * 2
    prefix = jnp.concatenate([eye[None], spans[:-1]], axis=0)
    whole = spans[-1]
    outer = ternary_scan(whole, axis, count, row, combine, eye)
    spread = jnp.broadcast_to(outer[None], (row, share, size, size)).reshape(row * share, size, size)
    carried = combine(spread, prefix.reshape(row * share, size, size))
    carried = carried.reshape(row, share, size, size)
    full = row_exchange(
        lambda q: lax.dynamic_index_in_dim(carried, q, 0, keepdims=False), axis, count, row
    )
    return full.reshape(heads, size, size)


def gathered_projection(features, proj_weight, axis, count):
    place = lax.axis_index(axis)
    got = [features]
    for step in range(1, count):
        pairs = [(k, (k + step) % count) for k in range(count)]
        got.append(lax.ppermute(features, axis, pairs))
    order = (place + count - jnp.arange(count)) % count
    ordered = jnp.take(jnp.stack(got), order, axis=0)
    whole = jnp.concatenate([ordered[j] for j in range(count)], axis=1)
    return jnp.dot(whole, proj_weight, preferred_element_type=jnp.float32)


def small_inverse(matrix):
    highest = lax.Precision.HIGHEST
    size = matrix.shape[-1]
    position = jnp.arange(size)
    strict = (position[:, None] < position[None, :]).astype(jnp.float32)
    eye_block = jnp.eye(size, dtype=jnp.float32)
    power = -2.0 * matrix * strict[None]
    result = eye_block[None] + power
    reach = 2
    while reach < size:
        power = jnp.einsum("hij,hjk->hik", power, power, precision=highest)
        result = result + jnp.einsum("hij,hjk->hik", result, power, precision=highest)
        reach = reach * 2
    return 2.0 * result


def triangle_inverse(matrix):
    highest = lax.Precision.HIGHEST
    size = matrix.shape[-1]
    if size <= 16:
        return small_inverse(matrix)
    half = size // 2
    first = triangle_inverse(matrix[:, :half, :half])
    second = triangle_inverse(matrix[:, half:, half:])
    coupling = matrix[:, :half, half:]
    middle = jnp.einsum("hij,hjk->hik", first, coupling, precision=highest)
    corner = -jnp.einsum("hij,hjk->hik", middle, second, precision=highest)
    lower_left = jnp.zeros((matrix.shape[0], size - half, half), jnp.float32)
    top = jnp.concatenate([first, corner], axis=2)
    bottom = jnp.concatenate([lower_left, second], axis=2)
    return jnp.concatenate([top, bottom], axis=1)


def batched_triangle_inverse(matrix):
    highest = lax.Precision.HIGHEST
    heads, size = matrix.shape[0], matrix.shape[-1]
    leaf = min(16, size)
    count = size // leaf
    diagonal = jnp.stack(
        [matrix[:, i * leaf : (i + 1) * leaf, i * leaf : (i + 1) * leaf] for i in range(count)],
        axis=1,
    )
    inverse = small_inverse(diagonal.reshape(heads * count, leaf, leaf))
    inverse = inverse.reshape(heads, count, leaf, leaf)
    width = leaf
    while width < size:
        pairs = size // (2 * width)
        first = inverse[:, 0::2]
        second = inverse[:, 1::2]
        coupling = jnp.stack(
            [
                matrix[:, 2 * j * width : (2 * j + 1) * width, (2 * j + 1) * width : (2 * j + 2) * width]
                for j in range(pairs)
            ],
            axis=1,
        )
        middle = jnp.einsum("hbij,hbjk->hbik", first, coupling, precision=highest)
        corner = -jnp.einsum("hbij,hbjk->hbik", middle, second, precision=highest)
        lower_left = jnp.zeros_like(corner)
        top = jnp.concatenate([first, corner], axis=3)
        bottom = jnp.concatenate([lower_left, second], axis=3)
        inverse = jnp.concatenate([top, bottom], axis=2)
        width = width * 2
    return inverse[:, 0]


def upper_solve(matrix, right_side):
    highest = lax.Precision.HIGHEST
    rows = matrix.shape[1]
    size = min(128, rows)
    count = rows // size
    solved_blocks = []
    for i in reversed(range(count)):
        inverse_block = batched_triangle_inverse(matrix)
        solved_blocks.append(
            jnp.einsum("hij,hjk->hik", inverse_block, right_side, precision=highest)
        )
    return jnp.concatenate(solved_blocks[::-1], axis=1)


def body(seq_count, head_count, features, proj_weight, query_vectors, key_vectors):
    highest = lax.Precision.HIGHEST
    tok_rows = query_vectors.shape[0]
    width = proj_weight.shape[1]
    local_heads = width // HEAD_DIM
    raw_proj = gathered_projection(features, proj_weight, "head", head_count)
    raw_proj = raw_proj.reshape(tok_rows, local_heads, HEAD_DIM)
    directions = raw_proj * lax.rsqrt(jnp.sum(raw_proj * raw_proj, axis=-1, keepdims=True) + 1e-06)
    reflectors = jnp.transpose(directions, (1, 0, 2))
    targets = jnp.concatenate(
        [
            query_vectors.reshape(tok_rows, local_heads, HEAD_DIM),
            key_vectors.reshape(tok_rows, local_heads, HEAD_DIM),
        ],
        axis=0,
    )
    targets = jnp.transpose(targets.astype(jnp.float32), (1, 0, 2))
    gram = jnp.einsum("hid,hjd->hij", reflectors, reflectors, precision=highest)
    position = jnp.arange(tok_rows)
    upper = (position[:, None] < position[None, :]).astype(jnp.float32)
    identity_tok = jnp.eye(tok_rows, dtype=jnp.float32)
    inverse_t = gram * upper[None] + 0.5 * identity_tok[None]
    inverse = batched_triangle_inverse(inverse_t)
    factor = jnp.einsum("hij,hjk->hik", inverse, reflectors, precision=highest)
    identity = jnp.broadcast_to(
        jnp.eye(HEAD_DIM, dtype=jnp.float32), (local_heads, HEAD_DIM, HEAD_DIM)
    )
    block_product = identity - jnp.einsum("hid,hie->hde", reflectors, factor, precision=highest)
    projected = jnp.einsum("hid,htd->hit", reflectors, targets, precision=highest)
    target_pos = jnp.concatenate([position, position])
    keep = (position[:, None] <= target_pos[None, :]).astype(jnp.float32)
    masked = projected * keep[None]
    weights_tok = jnp.einsum("hij,hjk->hik", inverse, masked, precision=highest)
    local_part = targets - jnp.einsum("hit,hid->htd", weights_tok, reflectors, precision=highest)

    def combine(earlier, later):
        return jnp.einsum("hde,hef->hdf", earlier, later, precision=highest)

    row = 8
    if seq_count % row == 0 and seq_count > row and local_heads % row == 0:
        carried = row_entering(block_product, "seq", seq_count, row, combine, identity[0])
    elif seq_count % 2 == 0 and local_heads % 2 == 0:
        carried = paired_entering(block_product, "seq", seq_count, combine, identity[0])
    else:
        carried = entering(block_product, "seq", seq_count, combine, identity)
    rotated = jnp.einsum("hde,hte->htd", carried, local_part, precision=highest)
    rotated = jnp.transpose(rotated, (1, 0, 2))
    rotated_queries = rotated[:tok_rows].reshape(tok_rows, width).astype(jnp.bfloat16)
    rotated_keys = rotated[tok_rows:].reshape(tok_rows, width).astype(jnp.bfloat16)
    return (rotated_queries, rotated_keys)


def solution(mesh):
    in_specs = (P("seq", "head"), P(None, "head"), P("seq", "head"), P("seq", "head"))
    out_specs = (P("seq", "head"), P("seq", "head"))
    return jax.shard_map(functools.partial(body, mesh.shape["seq"], mesh.shape["head"]), mesh=mesh, in_specs=in_specs, out_specs=out_specs, check_vma=False)
```

```python
import functools

import jax
import jax.numpy as jnp
from jax import lax
from jax.sharding import PartitionSpec as P

HEAD_DIM = 128


def entering(array, axis, count, combine, identity):
    place = lax.axis_index(axis)
    start = jnp.broadcast_to(jnp.asarray(identity, array.dtype), array.shape)
    span = array
    before = None
    shift = 1
    while shift < count:
        pairs = [(k, k + shift) for k in range(count - shift)]
        arrived = lax.ppermute(span, axis, pairs)
        reached = place >= shift
        last = shift * 2 >= count
        if before is None:
            before = jnp.where(reached, arrived, start)
            if not last:
                span = jnp.where(reached, combine(arrived, span), span)
        elif last:
            before = jnp.where(reached, combine(arrived, before), before)
        else:
            width = array.shape[-1]
            both = combine(arrived, jnp.concatenate([span, before], axis=-1))
            span = jnp.where(reached, both[..., :width], span)
            before = jnp.where(reached, both[..., width:], before)
        shift = shift * 2
    return before if before is not None else start


def paired_entering(array, axis, count, combine, identity):
    place = lax.axis_index(axis)
    core = place % 2
    first = core == 0
    half = array.shape[0] // 2
    swap = [(k, k ^ 1) for k in range(count)]
    mate = lax.ppermute(array, axis, swap)
    chip = combine(jnp.where(first, array, mate), jnp.where(first, mate, array))
    inner = jnp.where(first, jnp.broadcast_to(identity, array.shape), mate)
    mine = lax.dynamic_slice_in_dim(chip, core * half, half, 0)
    start = jnp.broadcast_to(identity, mine.shape)
    span = mine
    before = start
    shift = 2
    while shift < count:
        pairs = [(k, k + shift) for k in range(count - shift)]
        arrived = lax.ppermute(span, axis, pairs)
        reached = place >= shift
        last = shift * 2 >= count
        if shift == 2:
            before = jnp.where(reached, arrived, start)
            if not last:
                span = jnp.where(reached, combine(arrived, span), span)
        elif last:
            before = jnp.where(reached, combine(arrived, before), before)
        else:
            width = array.shape[-1]
            both = combine(arrived, jnp.concatenate([span, before], axis=-1))
            span = jnp.where(reached, both[..., :width], span)
            before = jnp.where(reached, both[..., width:], before)
        shift = shift * 2
    other = lax.ppermute(before, axis, swap)
    full = jnp.where(
        first,
        jnp.concatenate([before, other], axis=0),
        jnp.concatenate([other, before], axis=0),
    )
    return combine(full, inner)


def strided_scan(array, axis, count, stride, combine, start):
    place = lax.axis_index(axis)
    span = array
    before = start
    shift = stride
    while shift < count:
        pairs = [(k, k + shift) for k in range(count - shift)]
        arrived = lax.ppermute(span, axis, pairs)
        reached = place >= shift
        last = shift * 2 >= count
        if shift == stride:
            before = jnp.where(reached, arrived, start)
            if not last:
                span = jnp.where(reached, combine(arrived, span), span)
        elif last:
            before = jnp.where(reached, combine(arrived, before), before)
        else:
            width = array.shape[-1]
            both = combine(arrived, jnp.concatenate([span, before], axis=-1))
            span = jnp.where(reached, both[..., :width], span)
            before = jnp.where(reached, both[..., width:], before)
        shift = shift * 2
    return before


def ternary_scan(array, axis, count, stride, combine, start):
    place = lax.axis_index(axis)
    span = array
    before = start
    width = array.shape[-1]
    reach = stride
    while reach < count:
        near = lax.ppermute(span, axis, [(k, k + reach) for k in range(count - reach)])
        lead = jnp.where(place >= reach, near, start)
        if 2 * reach < count:
            far = lax.ppermute(span, axis, [(k, k + 2 * reach) for k in range(count - 2 * reach)])
            lead = combine(jnp.where(place >= 2 * reach, far, start), lead)
        if 3 * reach < count:
            both = combine(lead, jnp.concatenate([span, before], axis=-1))
            span = both[..., :width]
            before = both[..., width:]
        else:
            before = combine(lead, before)
        reach = reach * 3
    return before


def row_exchange(pieces, axis, count, row):
    place = lax.axis_index(axis)
    pos = place % row
    got = [pieces(pos)]
    for step in range(1, row):
        pairs = [(k, (k // row) * row + (k % row + step) % row) for k in range(count)]
        got.append(lax.ppermute(pieces((pos + step) % row), axis, pairs))
    order = (pos + row - jnp.arange(row)) % row
    return jnp.take(jnp.stack(got), order, axis=0)


def ring_prefix(array, axis, count, stride, combine, start):
    place = lax.axis_index(axis)
    size = count // stride
    me = place // stride
    got = [array]
    for step in range(1, size):
        pairs = [(k, ((k // stride + step) % size) * stride + k % stride) for k in range(count)]
        got.append(lax.ppermute(array, axis, pairs))
    order = (me + size - jnp.arange(size)) % size
    ordered = jnp.take(jnp.stack(got), order, axis=0)
    prefix = [start]
    for j in range(size - 1):
        prefix.append(combine(prefix[-1], ordered[j]))
    return jnp.take(jnp.stack(prefix), me, axis=0)


def flat_combine(combine, earlier, later):
    shape = later.shape
    size = shape[-1]
    merged = combine(earlier.reshape(-1, size, size), later.reshape(-1, size, size))
    return merged.reshape(shape)


def row_swap(value, axis, count, row):
    groups = [list(range(start, start + row)) for start in range(0, count, row)]
    return lax.all_to_all(value, axis, 0, 0, axis_index_groups=groups, tiled=True)


def row_entering(array, axis, count, row, combine, identity):
    place = lax.axis_index(axis)
    heads, size = array.shape[0], array.shape[-1]
    share = heads // row
    eye = jnp.broadcast_to(identity, (share, size, size))
    blocks = row_swap(array, axis, count, row).reshape(row, share, size, size)
    spans = blocks
    step = 1
    while step < row:
        moved = flat_combine(combine, spans[:-step], spans[step:])
        spans = jnp.concatenate([spans[:step], moved], axis=0)
        step = step * 2
    prefix = jnp.concatenate([eye[None], spans[:-1]], axis=0)
    whole = spans[-1]
    outer = ternary_scan(whole, axis, count, row, combine, eye)
    spread = jnp.broadcast_to(outer[None], (row, share, size, size)).reshape(row * share, size, size)
    carried = combine(spread, prefix.reshape(row * share, size, size))
    return row_swap(carried, axis, count, row)


def gathered_projection(features, proj_weight, axis, count):
    place = lax.axis_index(axis)
    got = [features]
    for step in range(1, count):
        pairs = [(k, (k + step) % count) for k in range(count)]
        got.append(lax.ppermute(features, axis, pairs))
    order = (place + count - jnp.arange(count)) % count
    ordered = jnp.take(jnp.stack(got), order, axis=0)
    whole = jnp.concatenate([ordered[j] for j in range(count)], axis=1)
    return jnp.dot(whole, proj_weight, preferred_element_type=jnp.float32)


def small_inverse(matrix):
    highest = lax.Precision.HIGHEST
    size = matrix.shape[-1]
    position = jnp.arange(size)
    strict = (position[:, None] < position[None, :]).astype(jnp.float32)
    eye_block = jnp.eye(size, dtype=jnp.float32)
    power = -2.0 * matrix * strict[None]
    result = eye_block[None] + power
    reach = 2
    while reach < size:
        power = jnp.einsum("hij,hjk->hik", power, power, precision=highest)
        result = result + jnp.einsum("hij,hjk->hik", result, power, precision=highest)
        reach = reach * 2
    return 2.0 * result


def triangle_inverse(matrix):
    highest = lax.Precision.HIGHEST
    size = matrix.shape[-1]
    if size <= 16:
        return small_inverse(matrix)
    half = size // 2
    first = triangle_inverse(matrix[:, :half, :half])
    second = triangle_inverse(matrix[:, half:, half:])
    coupling = matrix[:, :half, half:]
    middle = jnp.einsum("hij,hjk->hik", first, coupling, precision=highest)
    corner = -jnp.einsum("hij,hjk->hik", middle, second, precision=highest)
    lower_left = jnp.zeros((matrix.shape[0], size - half, half), jnp.float32)
    top = jnp.concatenate([first, corner], axis=2)
    bottom = jnp.concatenate([lower_left, second], axis=2)
    return jnp.concatenate([top, bottom], axis=1)


def batched_triangle_inverse(matrix):
    highest = lax.Precision.HIGHEST
    heads, size = matrix.shape[0], matrix.shape[-1]
    leaf = min(16, size)
    count = size // leaf
    diagonal = jnp.stack(
        [matrix[:, i * leaf : (i + 1) * leaf, i * leaf : (i + 1) * leaf] for i in range(count)],
        axis=1,
    )
    inverse = small_inverse(diagonal.reshape(heads * count, leaf, leaf))
    inverse = inverse.reshape(heads, count, leaf, leaf)
    width = leaf
    while width < size:
        pairs = size // (2 * width)
        first = inverse[:, 0::2]
        second = inverse[:, 1::2]
        coupling = jnp.stack(
            [
                matrix[:, 2 * j * width : (2 * j + 1) * width, (2 * j + 1) * width : (2 * j + 2) * width]
                for j in range(pairs)
            ],
            axis=1,
        )
        middle = jnp.einsum("hbij,hbjk->hbik", first, coupling, precision=highest)
        corner = -jnp.einsum("hbij,hbjk->hbik", middle, second, precision=highest)
        lower_left = jnp.zeros_like(corner)
        top = jnp.concatenate([first, corner], axis=3)
        bottom = jnp.concatenate([lower_left, second], axis=3)
        inverse = jnp.concatenate([top, bottom], axis=2)
        width = width * 2
    return inverse[:, 0]


def upper_solve(matrix, right_side):
    highest = lax.Precision.HIGHEST
    rows = matrix.shape[1]
    size = min(128, rows)
    count = rows // size
    solved_blocks = []
    for i in reversed(range(count)):
        inverse_block = batched_triangle_inverse(matrix)
        solved_blocks.append(
            jnp.einsum("hij,hjk->hik", inverse_block, right_side, precision=highest)
        )
    return jnp.concatenate(solved_blocks[::-1], axis=1)


def body(seq_count, head_count, features, proj_weight, query_vectors, key_vectors):
    highest = lax.Precision.HIGHEST
    tok_rows = query_vectors.shape[0]
    width = proj_weight.shape[1]
    local_heads = width // HEAD_DIM
    raw_proj = gathered_projection(features, proj_weight, "head", head_count)
    raw_proj = raw_proj.reshape(tok_rows, local_heads, HEAD_DIM)
    directions = raw_proj * lax.rsqrt(jnp.sum(raw_proj * raw_proj, axis=-1, keepdims=True) + 1e-06)
    reflectors = jnp.transpose(directions, (1, 0, 2))
    targets = jnp.concatenate(
        [
            query_vectors.reshape(tok_rows, local_heads, HEAD_DIM),
            key_vectors.reshape(tok_rows, local_heads, HEAD_DIM),
        ],
        axis=0,
    )
    targets = jnp.transpose(targets.astype(jnp.float32), (1, 0, 2))
    gram = jnp.einsum("hid,hjd->hij", reflectors, reflectors, precision=highest)
    position = jnp.arange(tok_rows)
    upper = (position[:, None] < position[None, :]).astype(jnp.float32)
    identity_tok = jnp.eye(tok_rows, dtype=jnp.float32)
    inverse_t = gram * upper[None] + 0.5 * identity_tok[None]
    inverse = batched_triangle_inverse(inverse_t)
    factor = jnp.einsum("hij,hjk->hik", inverse, reflectors, precision=highest)
    identity = jnp.broadcast_to(
        jnp.eye(HEAD_DIM, dtype=jnp.float32), (local_heads, HEAD_DIM, HEAD_DIM)
    )
    block_product = identity - jnp.einsum("hid,hie->hde", reflectors, factor, precision=highest)
    projected = jnp.einsum("hid,htd->hit", reflectors, targets, precision=highest)
    target_pos = jnp.concatenate([position, position])
    keep = (position[:, None] <= target_pos[None, :]).astype(jnp.float32)
    masked = projected * keep[None]
    weights_tok = jnp.einsum("hij,hjk->hik", inverse, masked, precision=highest)
    local_part = targets - jnp.einsum("hit,hid->htd", weights_tok, reflectors, precision=highest)

    def combine(earlier, later):
        return jnp.einsum("hde,hef->hdf", earlier, later, precision=highest)

    row = 8
    if seq_count % row == 0 and seq_count > row and local_heads % row == 0:
        carried = row_entering(block_product, "seq", seq_count, row, combine, identity[0])
    elif seq_count % 2 == 0 and local_heads % 2 == 0:
        carried = paired_entering(block_product, "seq", seq_count, combine, identity[0])
    else:
        carried = entering(block_product, "seq", seq_count, combine, identity)
    rotated = jnp.einsum("hde,hte->htd", carried, local_part, precision=highest)
    rotated = jnp.transpose(rotated, (1, 0, 2))
    rotated_queries = rotated[:tok_rows].reshape(tok_rows, width).astype(jnp.bfloat16)
    rotated_keys = rotated[tok_rows:].reshape(tok_rows, width).astype(jnp.bfloat16)
    return (rotated_queries, rotated_keys)


def solution(mesh):
    in_specs = (P("seq", "head"), P(None, "head"), P("seq", "head"), P("seq", "head"))
    out_specs = (P("seq", "head"), P("seq", "head"))
    return jax.shard_map(functools.partial(body, mesh.shape["seq"], mesh.shape["head"]), mesh=mesh, in_specs=in_specs, out_specs=out_specs, check_vma=False)
```

```python
import functools

import jax
import jax.numpy as jnp
from jax import lax
from jax.sharding import PartitionSpec as P

HEAD_DIM = 128


def entering(array, axis, count, combine, identity):
    place = lax.axis_index(axis)
    start = jnp.broadcast_to(jnp.asarray(identity, array.dtype), array.shape)
    span = array
    before = None
    shift = 1
    while shift < count:
        pairs = [(k, k + shift) for k in range(count - shift)]
        arrived = lax.ppermute(span, axis, pairs)
        reached = place >= shift
        last = shift * 2 >= count
        if before is None:
            before = jnp.where(reached, arrived, start)
            if not last:
                span = jnp.where(reached, combine(arrived, span), span)
        elif last:
            before = jnp.where(reached, combine(arrived, before), before)
        else:
            width = array.shape[-1]
            both = combine(arrived, jnp.concatenate([span, before], axis=-1))
            span = jnp.where(reached, both[..., :width], span)
            before = jnp.where(reached, both[..., width:], before)
        shift = shift * 2
    return before if before is not None else start


def paired_entering(array, axis, count, combine, identity):
    place = lax.axis_index(axis)
    core = place % 2
    first = core == 0
    half = array.shape[0] // 2
    swap = [(k, k ^ 1) for k in range(count)]
    mate = lax.ppermute(array, axis, swap)
    chip = combine(jnp.where(first, array, mate), jnp.where(first, mate, array))
    inner = jnp.where(first, jnp.broadcast_to(identity, array.shape), mate)
    mine = lax.dynamic_slice_in_dim(chip, core * half, half, 0)
    start = jnp.broadcast_to(identity, mine.shape)
    span = mine
    before = start
    shift = 2
    while shift < count:
        pairs = [(k, k + shift) for k in range(count - shift)]
        arrived = lax.ppermute(span, axis, pairs)
        reached = place >= shift
        last = shift * 2 >= count
        if shift == 2:
            before = jnp.where(reached, arrived, start)
            if not last:
                span = jnp.where(reached, combine(arrived, span), span)
        elif last:
            before = jnp.where(reached, combine(arrived, before), before)
        else:
            width = array.shape[-1]
            both = combine(arrived, jnp.concatenate([span, before], axis=-1))
            span = jnp.where(reached, both[..., :width], span)
            before = jnp.where(reached, both[..., width:], before)
        shift = shift * 2
    other = lax.ppermute(before, axis, swap)
    full = jnp.where(
        first,
        jnp.concatenate([before, other], axis=0),
        jnp.concatenate([other, before], axis=0),
    )
    return combine(full, inner)


def strided_scan(array, axis, count, stride, combine, start):
    place = lax.axis_index(axis)
    span = array
    before = start
    shift = stride
    while shift < count:
        pairs = [(k, k + shift) for k in range(count - shift)]
        arrived = lax.ppermute(span, axis, pairs)
        reached = place >= shift
        last = shift * 2 >= count
        if shift == stride:
            before = jnp.where(reached, arrived, start)
            if not last:
                span = jnp.where(reached, combine(arrived, span), span)
        elif last:
            before = jnp.where(reached, combine(arrived, before), before)
        else:
            width = array.shape[-1]
            both = combine(arrived, jnp.concatenate([span, before], axis=-1))
            span = jnp.where(reached, both[..., :width], span)
            before = jnp.where(reached, both[..., width:], before)
        shift = shift * 2
    return before


def ternary_scan(array, axis, count, stride, combine, start):
    place = lax.axis_index(axis)
    span = array
    before = start
    width = array.shape[-1]
    reach = stride
    while reach < count:
        near = lax.ppermute(span, axis, [(k, k + reach) for k in range(count - reach)])
        lead = jnp.where(place >= reach, near, start)
        if 2 * reach < count:
            far = lax.ppermute(span, axis, [(k, k + 2 * reach) for k in range(count - 2 * reach)])
            lead = combine(jnp.where(place >= 2 * reach, far, start), lead)
        if 3 * reach < count:
            both = combine(lead, jnp.concatenate([span, before], axis=-1))
            span = both[..., :width]
            before = both[..., width:]
        else:
            before = combine(lead, before)
        reach = reach * 3
    return before


def row_exchange(pieces, axis, count, row):
    place = lax.axis_index(axis)
    pos = place % row
    got = [pieces(pos)]
    for step in range(1, row):
        pairs = [(k, (k // row) * row + (k % row + step) % row) for k in range(count)]
        got.append(lax.ppermute(pieces((pos + step) % row), axis, pairs))
    order = (pos + row - jnp.arange(row)) % row
    return jnp.take(jnp.stack(got), order, axis=0)


def ring_prefix(array, axis, count, stride, combine, start):
    place = lax.axis_index(axis)
    size = count // stride
    me = place // stride
    got = [array]
    for step in range(1, size):
        pairs = [(k, ((k // stride + step) % size) * stride + k % stride) for k in range(count)]
        got.append(lax.ppermute(array, axis, pairs))
    order = (me + size - jnp.arange(size)) % size
    ordered = jnp.take(jnp.stack(got), order, axis=0)
    prefix = [start]
    for j in range(size - 1):
        prefix.append(combine(prefix[-1], ordered[j]))
    return jnp.take(jnp.stack(prefix), me, axis=0)


def flat_combine(combine, earlier, later):
    shape = later.shape
    size = shape[-1]
    merged = combine(earlier.reshape(-1, size, size), later.reshape(-1, size, size))
    return merged.reshape(shape)


def pick(value, index, axis):
    return lax.dynamic_index_in_dim(value, index, axis, keepdims=False)


def chip_shift(step, count, row):
    chips = row // 2
    return [
        (k, (k // row) * row + (((k % row) // 2 + step) % chips) * 2 + k % 2) for k in range(count)
    ]


def row_gather(array, axis, count, row):
    place = lax.axis_index(axis)
    pos = place % row
    core, chip, chips = pos % 2, pos // 2, row // 2
    share = array.shape[0] // row
    tail = array.shape[1:]
    split = array.reshape((chips, 2, share) + tail)
    mine = pick(split, core, 1)
    mate = lax.ppermute(pick(split, 1 - core, 1), axis, [(k, k ^ 1) for k in range(count)])
    first = core == 0
    pair = jnp.where(first, jnp.stack([mine, mate], axis=1), jnp.stack([mate, mine], axis=1))
    got = [pick(pair, chip, 0)]
    for step in range(1, chips):
        got.append(lax.ppermute(pick(pair, (chip + step) % chips, 0), axis, chip_shift(step, count, row)))
    order = (chip + chips - jnp.arange(chips)) % chips
    return jnp.take(jnp.stack(got), order, axis=0).reshape((row, share) + tail)


def row_return(carried, axis, count, row):
    place = lax.axis_index(axis)
    pos = place % row
    core, chip, chips = pos % 2, pos // 2, row // 2
    share = carried.shape[1]
    tail = carried.shape[2:]
    split = carried.reshape((chips, 2, share) + tail)
    got = [pick(split, chip, 0)]
    for step in range(1, chips):
        got.append(lax.ppermute(pick(split, (chip + step) % chips, 0), axis, chip_shift(step, count, row)))
    order = (chip + chips - jnp.arange(chips)) % chips
    held = jnp.take(jnp.stack(got), order, axis=0)
    for_me = pick(held, core, 1)
    from_mate = lax.ppermute(pick(held, 1 - core, 1), axis, [(k, k ^ 1) for k in range(count)])
    first = core == 0
    full = jnp.where(
        first, jnp.stack([for_me, from_mate], axis=1), jnp.stack([from_mate, for_me], axis=1)
    )
    return full.reshape((row * share,) + tail)


def row_entering(array, axis, count, row, combine, identity):
    place = lax.axis_index(axis)
    heads, size = array.shape[0], array.shape[-1]
    share = heads // row
    eye = jnp.broadcast_to(identity, (share, size, size))
    blocks = row_gather(array, axis, count, row)
    spans = blocks
    step = 1
    while step < row:
        moved = flat_combine(combine, spans[:-step], spans[step:])
        spans = jnp.concatenate([spans[:step], moved], axis=0)
        step = step * 2
    prefix = jnp.concatenate([eye[None], spans[:-1]], axis=0)
    whole = spans[-1]
    outer = ternary_scan(whole, axis, count, row, combine, eye)
    spread = jnp.broadcast_to(outer[None], (row, share, size, size)).reshape(row * share, size, size)
    carried = combine(spread, prefix.reshape(row * share, size, size))
    carried = carried.reshape(row, share, size, size)
    return row_return(carried, axis, count, row)


def gathered_projection(features, proj_weight, axis, count):
    place = lax.axis_index(axis)
    got = [features]
    for step in range(1, count):
        pairs = [(k, (k + step) % count) for k in range(count)]
        got.append(lax.ppermute(features, axis, pairs))
    order = (place + count - jnp.arange(count)) % count
    ordered = jnp.take(jnp.stack(got), order, axis=0)
    whole = jnp.concatenate([ordered[j] for j in range(count)], axis=1)
    return jnp.dot(whole, proj_weight, preferred_element_type=jnp.float32)


def small_inverse(matrix):
    highest = lax.Precision.HIGHEST
    size = matrix.shape[-1]
    position = jnp.arange(size)
    strict = (position[:, None] < position[None, :]).astype(jnp.float32)
    eye_block = jnp.eye(size, dtype=jnp.float32)
    power = -2.0 * matrix * strict[None]
    result = eye_block[None] + power
    reach = 2
    while reach < size:
        power = jnp.einsum("hij,hjk->hik", power, power, precision=highest)
        result = result + jnp.einsum("hij,hjk->hik", result, power, precision=highest)
        reach = reach * 2
    return 2.0 * result


def triangle_inverse(matrix):
    highest = lax.Precision.HIGHEST
    size = matrix.shape[-1]
    if size <= 16:
        return small_inverse(matrix)
    half = size // 2
    first = triangle_inverse(matrix[:, :half, :half])
    second = triangle_inverse(matrix[:, half:, half:])
    coupling = matrix[:, :half, half:]
    middle = jnp.einsum("hij,hjk->hik", first, coupling, precision=highest)
    corner = -jnp.einsum("hij,hjk->hik", middle, second, precision=highest)
    lower_left = jnp.zeros((matrix.shape[0], size - half, half), jnp.float32)
    top = jnp.concatenate([first, corner], axis=2)
    bottom = jnp.concatenate([lower_left, second], axis=2)
    return jnp.concatenate([top, bottom], axis=1)


def batched_triangle_inverse(matrix):
    highest = lax.Precision.HIGHEST
    heads, size = matrix.shape[0], matrix.shape[-1]
    leaf = min(16, size)
    count = size // leaf
    diagonal = jnp.stack(
        [matrix[:, i * leaf : (i + 1) * leaf, i * leaf : (i + 1) * leaf] for i in range(count)],
        axis=1,
    )
    inverse = small_inverse(diagonal.reshape(heads * count, leaf, leaf))
    inverse = inverse.reshape(heads, count, leaf, leaf)
    width = leaf
    while width < size:
        pairs = size // (2 * width)
        first = inverse[:, 0::2]
        second = inverse[:, 1::2]
        coupling = jnp.stack(
            [
                matrix[:, 2 * j * width : (2 * j + 1) * width, (2 * j + 1) * width : (2 * j + 2) * width]
                for j in range(pairs)
            ],
            axis=1,
        )
        middle = jnp.einsum("hbij,hbjk->hbik", first, coupling, precision=highest)
        corner = -jnp.einsum("hbij,hbjk->hbik", middle, second, precision=highest)
        lower_left = jnp.zeros_like(corner)
        top = jnp.concatenate([first, corner], axis=3)
        bottom = jnp.concatenate([lower_left, second], axis=3)
        inverse = jnp.concatenate([top, bottom], axis=2)
        width = width * 2
    return inverse[:, 0]


def upper_solve(matrix, right_side):
    highest = lax.Precision.HIGHEST
    rows = matrix.shape[1]
    size = min(128, rows)
    count = rows // size
    solved_blocks = []
    for i in reversed(range(count)):
        inverse_block = batched_triangle_inverse(matrix)
        solved_blocks.append(
            jnp.einsum("hij,hjk->hik", inverse_block, right_side, precision=highest)
        )
    return jnp.concatenate(solved_blocks[::-1], axis=1)


def body(seq_count, head_count, features, proj_weight, query_vectors, key_vectors):
    highest = lax.Precision.HIGHEST
    tok_rows = query_vectors.shape[0]
    width = proj_weight.shape[1]
    local_heads = width // HEAD_DIM
    raw_proj = gathered_projection(features, proj_weight, "head", head_count)
    raw_proj = raw_proj.reshape(tok_rows, local_heads, HEAD_DIM)
    directions = raw_proj * lax.rsqrt(jnp.sum(raw_proj * raw_proj, axis=-1, keepdims=True) + 1e-06)
    reflectors = jnp.transpose(directions, (1, 0, 2))
    targets = jnp.concatenate(
        [
            query_vectors.reshape(tok_rows, local_heads, HEAD_DIM),
            key_vectors.reshape(tok_rows, local_heads, HEAD_DIM),
        ],
        axis=0,
    )
    targets = jnp.transpose(targets.astype(jnp.float32), (1, 0, 2))
    gram = jnp.einsum("hid,hjd->hij", reflectors, reflectors, precision=highest)
    position = jnp.arange(tok_rows)
    upper = (position[:, None] < position[None, :]).astype(jnp.float32)
    identity_tok = jnp.eye(tok_rows, dtype=jnp.float32)
    inverse_t = gram * upper[None] + 0.5 * identity_tok[None]
    inverse = batched_triangle_inverse(inverse_t)
    factor = jnp.einsum("hij,hjk->hik", inverse, reflectors, precision=highest)
    identity = jnp.broadcast_to(
        jnp.eye(HEAD_DIM, dtype=jnp.float32), (local_heads, HEAD_DIM, HEAD_DIM)
    )
    block_product = identity - jnp.einsum("hid,hie->hde", reflectors, factor, precision=highest)
    projected = jnp.einsum("hid,htd->hit", reflectors, targets, precision=highest)
    target_pos = jnp.concatenate([position, position])
    keep = (position[:, None] <= target_pos[None, :]).astype(jnp.float32)
    masked = projected * keep[None]
    weights_tok = jnp.einsum("hij,hjk->hik", inverse, masked, precision=highest)
    local_part = targets - jnp.einsum("hit,hid->htd", weights_tok, reflectors, precision=highest)

    def combine(earlier, later):
        return jnp.einsum("hde,hef->hdf", earlier, later, precision=highest)

    row = 8
    if seq_count % row == 0 and seq_count > row and local_heads % row == 0 and row % 2 == 0:
        carried = row_entering(block_product, "seq", seq_count, row, combine, identity[0])
    elif seq_count % 2 == 0 and local_heads % 2 == 0:
        carried = paired_entering(block_product, "seq", seq_count, combine, identity[0])
    else:
        carried = entering(block_product, "seq", seq_count, combine, identity)
    rotated = jnp.einsum("hde,hte->htd", carried, local_part, precision=highest)
    rotated = jnp.transpose(rotated, (1, 0, 2))
    rotated_queries = rotated[:tok_rows].reshape(tok_rows, width).astype(jnp.bfloat16)
    rotated_keys = rotated[tok_rows:].reshape(tok_rows, width).astype(jnp.bfloat16)
    return (rotated_queries, rotated_keys)


def solution(mesh):
    in_specs = (P("seq", "head"), P(None, "head"), P("seq", "head"), P("seq", "head"))
    out_specs = (P("seq", "head"), P("seq", "head"))
    return jax.shard_map(functools.partial(body, mesh.shape["seq"], mesh.shape["head"]), mesh=mesh, in_specs=in_specs, out_specs=out_specs, check_vma=False)
```

```python
import functools

import jax
import jax.numpy as jnp
from jax import lax
from jax.sharding import PartitionSpec as P

HEAD_DIM = 128


def entering(array, axis, count, combine, identity):
    place = lax.axis_index(axis)
    start = jnp.broadcast_to(jnp.asarray(identity, array.dtype), array.shape)
    span = array
    before = None
    shift = 1
    while shift < count:
        pairs = [(k, k + shift) for k in range(count - shift)]
        arrived = lax.ppermute(span, axis, pairs)
        reached = place >= shift
        last = shift * 2 >= count
        if before is None:
            before = jnp.where(reached, arrived, start)
            if not last:
                span = jnp.where(reached, combine(arrived, span), span)
        elif last:
            before = jnp.where(reached, combine(arrived, before), before)
        else:
            width = array.shape[-1]
            both = combine(arrived, jnp.concatenate([span, before], axis=-1))
            span = jnp.where(reached, both[..., :width], span)
            before = jnp.where(reached, both[..., width:], before)
        shift = shift * 2
    return before if before is not None else start


def paired_entering(array, axis, count, combine, identity):
    place = lax.axis_index(axis)
    core = place % 2
    first = core == 0
    half = array.shape[0] // 2
    swap = [(k, k ^ 1) for k in range(count)]
    mate = lax.ppermute(array, axis, swap)
    chip = combine(jnp.where(first, array, mate), jnp.where(first, mate, array))
    inner = jnp.where(first, jnp.broadcast_to(identity, array.shape), mate)
    mine = lax.dynamic_slice_in_dim(chip, core * half, half, 0)
    start = jnp.broadcast_to(identity, mine.shape)
    span = mine
    before = start
    shift = 2
    while shift < count:
        pairs = [(k, k + shift) for k in range(count - shift)]
        arrived = lax.ppermute(span, axis, pairs)
        reached = place >= shift
        last = shift * 2 >= count
        if shift == 2:
            before = jnp.where(reached, arrived, start)
            if not last:
                span = jnp.where(reached, combine(arrived, span), span)
        elif last:
            before = jnp.where(reached, combine(arrived, before), before)
        else:
            width = array.shape[-1]
            both = combine(arrived, jnp.concatenate([span, before], axis=-1))
            span = jnp.where(reached, both[..., :width], span)
            before = jnp.where(reached, both[..., width:], before)
        shift = shift * 2
    other = lax.ppermute(before, axis, swap)
    full = jnp.where(
        first,
        jnp.concatenate([before, other], axis=0),
        jnp.concatenate([other, before], axis=0),
    )
    return combine(full, inner)


def strided_scan(array, axis, count, stride, combine, start):
    place = lax.axis_index(axis)
    span = array
    before = start
    shift = stride
    while shift < count:
        pairs = [(k, k + shift) for k in range(count - shift)]
        arrived = lax.ppermute(span, axis, pairs)
        reached = place >= shift
        last = shift * 2 >= count
        if shift == stride:
            before = jnp.where(reached, arrived, start)
            if not last:
                span = jnp.where(reached, combine(arrived, span), span)
        elif last:
            before = jnp.where(reached, combine(arrived, before), before)
        else:
            width = array.shape[-1]
            both = combine(arrived, jnp.concatenate([span, before], axis=-1))
            span = jnp.where(reached, both[..., :width], span)
            before = jnp.where(reached, both[..., width:], before)
        shift = shift * 2
    return before


def ternary_scan(array, axis, count, stride, combine, start):
    place = lax.axis_index(axis)
    span = array
    before = start
    width = array.shape[-1]
    reach = stride
    while reach < count:
        near = lax.ppermute(span, axis, [(k, k + reach) for k in range(count - reach)])
        lead = jnp.where(place >= reach, near, start)
        if 2 * reach < count:
            far = lax.ppermute(span, axis, [(k, k + 2 * reach) for k in range(count - 2 * reach)])
            lead = combine(jnp.where(place >= 2 * reach, far, start), lead)
        if 3 * reach < count:
            both = combine(lead, jnp.concatenate([span, before], axis=-1))
            span = both[..., :width]
            before = both[..., width:]
        else:
            before = combine(lead, before)
        reach = reach * 3
    return before


def row_exchange(pieces, axis, count, row):
    place = lax.axis_index(axis)
    pos = place % row
    got = [pieces(pos)]
    for step in range(1, row):
        pairs = [(k, (k // row) * row + (k % row + step) % row) for k in range(count)]
        got.append(lax.ppermute(pieces((pos + step) % row), axis, pairs))
    order = (pos + row - jnp.arange(row)) % row
    return jnp.take(jnp.stack(got), order, axis=0)


def ring_prefix(array, axis, count, stride, combine, start):
    place = lax.axis_index(axis)
    size = count // stride
    me = place // stride
    got = [array]
    for step in range(1, size):
        pairs = [(k, ((k // stride + step) % size) * stride + k % stride) for k in range(count)]
        got.append(lax.ppermute(array, axis, pairs))
    order = (me + size - jnp.arange(size)) % size
    ordered = jnp.take(jnp.stack(got), order, axis=0)
    prefix = [start]
    for j in range(size - 1):
        prefix.append(combine(prefix[-1], ordered[j]))
    return jnp.take(jnp.stack(prefix), me, axis=0)


def flat_combine(combine, earlier, later):
    shape = later.shape
    size = shape[-1]
    merged = combine(earlier.reshape(-1, size, size), later.reshape(-1, size, size))
    return merged.reshape(shape)


def pick(value, index, axis):
    return lax.dynamic_index_in_dim(value, index, axis, keepdims=False)


def chip_shift(step, count, row):
    chips = row // 2
    return [
        (k, (k // row) * row + (((k % row) // 2 + step) % chips) * 2 + k % 2) for k in range(count)
    ]


def row_gather(array, axis, count, row):
    place = lax.axis_index(axis)
    pos = place % row
    core, chip, chips = pos % 2, pos // 2, row // 2
    share = array.shape[0] // row
    tail = array.shape[1:]
    split = array.reshape((chips, 2, share) + tail)
    mine = pick(split, core, 1)
    mate = lax.ppermute(pick(split, 1 - core, 1), axis, [(k, k ^ 1) for k in range(count)])
    first = core == 0
    pair = jnp.where(first, jnp.stack([mine, mate], axis=1), jnp.stack([mate, mine], axis=1))
    got = [pick(pair, chip, 0)]
    for step in range(1, chips):
        got.append(lax.ppermute(pick(pair, (chip + step) % chips, 0), axis, chip_shift(step, count, row)))
    order = (chip + chips - jnp.arange(chips)) % chips
    return jnp.take(jnp.stack(got), order, axis=0).reshape((row, share) + tail)


def row_return(carried, axis, count, row):
    place = lax.axis_index(axis)
    pos = place % row
    core, chip, chips = pos % 2, pos // 2, row // 2
    share = carried.shape[1]
    tail = carried.shape[2:]
    split = carried.reshape((chips, 2, share) + tail)
    got = [pick(split, chip, 0)]
    for step in range(1, chips):
        got.append(lax.ppermute(pick(split, (chip + step) % chips, 0), axis, chip_shift(step, count, row)))
    order = (chip + chips - jnp.arange(chips)) % chips
    held = jnp.take(jnp.stack(got), order, axis=0)
    for_me = pick(held, core, 1)
    from_mate = lax.ppermute(pick(held, 1 - core, 1), axis, [(k, k ^ 1) for k in range(count)])
    first = core == 0
    full = jnp.where(
        first, jnp.stack([for_me, from_mate], axis=1), jnp.stack([from_mate, for_me], axis=1)
    )
    return full.reshape((row * share,) + tail)


def row_entering(array, axis, count, row, combine, identity):
    place = lax.axis_index(axis)
    heads, size = array.shape[0], array.shape[-1]
    share = heads // row
    eye = jnp.broadcast_to(identity, (share, size, size))
    blocks = row_exchange(
        lambda g: lax.dynamic_slice_in_dim(array, g * share, share, 0), axis, count, row
    )
    spans = blocks
    step = 1
    while step < row:
        moved = flat_combine(combine, spans[:-step], spans[step:])
        spans = jnp.concatenate([spans[:step], moved], axis=0)
        step = step * 2
    prefix = jnp.concatenate([eye[None], spans[:-1]], axis=0)
    whole = spans[-1]
    outer = ternary_scan(whole, axis, count, row, combine, eye)
    spread = jnp.broadcast_to(outer[None], (row, share, size, size)).reshape(row * share, size, size)
    carried = combine(spread, prefix.reshape(row * share, size, size))
    carried = carried.reshape(row, share, size, size)
    return row_return(carried, axis, count, row)


def gathered_projection(features, proj_weight, axis, count):
    place = lax.axis_index(axis)
    got = [features]
    for step in range(1, count):
        pairs = [(k, (k + step) % count) for k in range(count)]
        got.append(lax.ppermute(features, axis, pairs))
    order = (place + count - jnp.arange(count)) % count
    ordered = jnp.take(jnp.stack(got), order, axis=0)
    whole = jnp.concatenate([ordered[j] for j in range(count)], axis=1)
    return jnp.dot(whole, proj_weight, preferred_element_type=jnp.float32)


def small_inverse(matrix):
    highest = lax.Precision.HIGHEST
    size = matrix.shape[-1]
    position = jnp.arange(size)
    strict = (position[:, None] < position[None, :]).astype(jnp.float32)
    eye_block = jnp.eye(size, dtype=jnp.float32)
    power = -2.0 * matrix * strict[None]
    result = eye_block[None] + power
    reach = 2
    while reach < size:
        power = jnp.einsum("hij,hjk->hik", power, power, precision=highest)
        result = result + jnp.einsum("hij,hjk->hik", result, power, precision=highest)
        reach = reach * 2
    return 2.0 * result


def triangle_inverse(matrix):
    highest = lax.Precision.HIGHEST
    size = matrix.shape[-1]
    if size <= 16:
        return small_inverse(matrix)
    half = size // 2
    first = triangle_inverse(matrix[:, :half, :half])
    second = triangle_inverse(matrix[:, half:, half:])
    coupling = matrix[:, :half, half:]
    middle = jnp.einsum("hij,hjk->hik", first, coupling, precision=highest)
    corner = -jnp.einsum("hij,hjk->hik", middle, second, precision=highest)
    lower_left = jnp.zeros((matrix.shape[0], size - half, half), jnp.float32)
    top = jnp.concatenate([first, corner], axis=2)
    bottom = jnp.concatenate([lower_left, second], axis=2)
    return jnp.concatenate([top, bottom], axis=1)


def batched_triangle_inverse(matrix):
    highest = lax.Precision.HIGHEST
    heads, size = matrix.shape[0], matrix.shape[-1]
    leaf = min(16, size)
    count = size // leaf
    diagonal = jnp.stack(
        [matrix[:, i * leaf : (i + 1) * leaf, i * leaf : (i + 1) * leaf] for i in range(count)],
        axis=1,
    )
    inverse = small_inverse(diagonal.reshape(heads * count, leaf, leaf))
    inverse = inverse.reshape(heads, count, leaf, leaf)
    width = leaf
    while width < size:
        pairs = size // (2 * width)
        first = inverse[:, 0::2]
        second = inverse[:, 1::2]
        coupling = jnp.stack(
            [
                matrix[:, 2 * j * width : (2 * j + 1) * width, (2 * j + 1) * width : (2 * j + 2) * width]
                for j in range(pairs)
            ],
            axis=1,
        )
        middle = jnp.einsum("hbij,hbjk->hbik", first, coupling, precision=highest)
        corner = -jnp.einsum("hbij,hbjk->hbik", middle, second, precision=highest)
        lower_left = jnp.zeros_like(corner)
        top = jnp.concatenate([first, corner], axis=3)
        bottom = jnp.concatenate([lower_left, second], axis=3)
        inverse = jnp.concatenate([top, bottom], axis=2)
        width = width * 2
    return inverse[:, 0]


def upper_solve(matrix, right_side):
    highest = lax.Precision.HIGHEST
    rows = matrix.shape[1]
    size = min(128, rows)
    count = rows // size
    solved_blocks = []
    for i in reversed(range(count)):
        inverse_block = batched_triangle_inverse(matrix)
        solved_blocks.append(
            jnp.einsum("hij,hjk->hik", inverse_block, right_side, precision=highest)
        )
    return jnp.concatenate(solved_blocks[::-1], axis=1)


def body(seq_count, head_count, features, proj_weight, query_vectors, key_vectors):
    highest = lax.Precision.HIGHEST
    tok_rows = query_vectors.shape[0]
    width = proj_weight.shape[1]
    local_heads = width // HEAD_DIM
    raw_proj = gathered_projection(features, proj_weight, "head", head_count)
    raw_proj = raw_proj.reshape(tok_rows, local_heads, HEAD_DIM)
    directions = raw_proj * lax.rsqrt(jnp.sum(raw_proj * raw_proj, axis=-1, keepdims=True) + 1e-06)
    reflectors = jnp.transpose(directions, (1, 0, 2))
    targets = jnp.concatenate(
        [
            query_vectors.reshape(tok_rows, local_heads, HEAD_DIM),
            key_vectors.reshape(tok_rows, local_heads, HEAD_DIM),
        ],
        axis=0,
    )
    targets = jnp.transpose(targets.astype(jnp.float32), (1, 0, 2))
    gram = jnp.einsum("hid,hjd->hij", reflectors, reflectors, precision=highest)
    position = jnp.arange(tok_rows)
    upper = (position[:, None] < position[None, :]).astype(jnp.float32)
    identity_tok = jnp.eye(tok_rows, dtype=jnp.float32)
    inverse_t = gram * upper[None] + 0.5 * identity_tok[None]
    inverse = batched_triangle_inverse(inverse_t)
    factor = jnp.einsum("hij,hjk->hik", inverse, reflectors, precision=highest)
    identity = jnp.broadcast_to(
        jnp.eye(HEAD_DIM, dtype=jnp.float32), (local_heads, HEAD_DIM, HEAD_DIM)
    )
    block_product = identity - jnp.einsum("hid,hie->hde", reflectors, factor, precision=highest)
    projected = jnp.einsum("hid,htd->hit", reflectors, targets, precision=highest)
    target_pos = jnp.concatenate([position, position])
    keep = (position[:, None] <= target_pos[None, :]).astype(jnp.float32)
    masked = projected * keep[None]
    weights_tok = jnp.einsum("hij,hjk->hik", inverse, masked, precision=highest)
    local_part = targets - jnp.einsum("hit,hid->htd", weights_tok, reflectors, precision=highest)

    def combine(earlier, later):
        return jnp.einsum("hde,hef->hdf", earlier, later, precision=highest)

    row = 8
    if seq_count % row == 0 and seq_count > row and local_heads % row == 0 and row % 2 == 0:
        carried = row_entering(block_product, "seq", seq_count, row, combine, identity[0])
    elif seq_count % 2 == 0 and local_heads % 2 == 0:
        carried = paired_entering(block_product, "seq", seq_count, combine, identity[0])
    else:
        carried = entering(block_product, "seq", seq_count, combine, identity)
    rotated = jnp.einsum("hde,hte->htd", carried, local_part, precision=highest)
    rotated = jnp.transpose(rotated, (1, 0, 2))
    rotated_queries = rotated[:tok_rows].reshape(tok_rows, width).astype(jnp.bfloat16)
    rotated_keys = rotated[tok_rows:].reshape(tok_rows, width).astype(jnp.bfloat16)
    return (rotated_queries, rotated_keys)


def solution(mesh):
    in_specs = (P("seq", "head"), P(None, "head"), P("seq", "head"), P("seq", "head"))
    out_specs = (P("seq", "head"), P("seq", "head"))
    return jax.shard_map(functools.partial(body, mesh.shape["seq"], mesh.shape["head"]), mesh=mesh, in_specs=in_specs, out_specs=out_specs, check_vma=False)
```

```python
import functools

import jax
import jax.numpy as jnp
from jax import lax
from jax.sharding import PartitionSpec as P

HEAD_DIM = 128


def entering(array, axis, count, combine, identity):
    place = lax.axis_index(axis)
    start = jnp.broadcast_to(jnp.asarray(identity, array.dtype), array.shape)
    span = array
    before = None
    shift = 1
    while shift < count:
        pairs = [(k, k + shift) for k in range(count - shift)]
        arrived = lax.ppermute(span, axis, pairs)
        reached = place >= shift
        last = shift * 2 >= count
        if before is None:
            before = jnp.where(reached, arrived, start)
            if not last:
                span = jnp.where(reached, combine(arrived, span), span)
        elif last:
            before = jnp.where(reached, combine(arrived, before), before)
        else:
            width = array.shape[-1]
            both = combine(arrived, jnp.concatenate([span, before], axis=-1))
            span = jnp.where(reached, both[..., :width], span)
            before = jnp.where(reached, both[..., width:], before)
        shift = shift * 2
    return before if before is not None else start


def paired_entering(array, axis, count, combine, identity):
    place = lax.axis_index(axis)
    core = place % 2
    first = core == 0
    half = array.shape[0] // 2
    swap = [(k, k ^ 1) for k in range(count)]
    mate = lax.ppermute(array, axis, swap)
    chip = combine(jnp.where(first, array, mate), jnp.where(first, mate, array))
    inner = jnp.where(first, jnp.broadcast_to(identity, array.shape), mate)
    mine = lax.dynamic_slice_in_dim(chip, core * half, half, 0)
    start = jnp.broadcast_to(identity, mine.shape)
    span = mine
    before = start
    shift = 2
    while shift < count:
        pairs = [(k, k + shift) for k in range(count - shift)]
        arrived = lax.ppermute(span, axis, pairs)
        reached = place >= shift
        last = shift * 2 >= count
        if shift == 2:
            before = jnp.where(reached, arrived, start)
            if not last:
                span = jnp.where(reached, combine(arrived, span), span)
        elif last:
            before = jnp.where(reached, combine(arrived, before), before)
        else:
            width = array.shape[-1]
            both = combine(arrived, jnp.concatenate([span, before], axis=-1))
            span = jnp.where(reached, both[..., :width], span)
            before = jnp.where(reached, both[..., width:], before)
        shift = shift * 2
    other = lax.ppermute(before, axis, swap)
    full = jnp.where(
        first,
        jnp.concatenate([before, other], axis=0),
        jnp.concatenate([other, before], axis=0),
    )
    return combine(full, inner)


def strided_scan(array, axis, count, stride, combine, start):
    place = lax.axis_index(axis)
    span = array
    before = start
    shift = stride
    while shift < count:
        pairs = [(k, k + shift) for k in range(count - shift)]
        arrived = lax.ppermute(span, axis, pairs)
        reached = place >= shift
        last = shift * 2 >= count
        if shift == stride:
            before = jnp.where(reached, arrived, start)
            if not last:
                span = jnp.where(reached, combine(arrived, span), span)
        elif last:
            before = jnp.where(reached, combine(arrived, before), before)
        else:
            width = array.shape[-1]
            both = combine(arrived, jnp.concatenate([span, before], axis=-1))
            span = jnp.where(reached, both[..., :width], span)
            before = jnp.where(reached, both[..., width:], before)
        shift = shift * 2
    return before


def ternary_scan(array, axis, count, stride, combine, start):
    place = lax.axis_index(axis)
    span = array
    before = start
    width = array.shape[-1]
    reach = stride
    while reach < count:
        near = lax.ppermute(span, axis, [(k, k + reach) for k in range(count - reach)])
        lead = jnp.where(place >= reach, near, start)
        if 2 * reach < count:
            far = lax.ppermute(span, axis, [(k, k + 2 * reach) for k in range(count - 2 * reach)])
            lead = combine(jnp.where(place >= 2 * reach, far, start), lead)
        if 3 * reach < count:
            both = combine(lead, jnp.concatenate([span, before], axis=-1))
            span = both[..., :width]
            before = both[..., width:]
        else:
            before = combine(lead, before)
        reach = reach * 3
    return before


def row_exchange(pieces, axis, count, row):
    place = lax.axis_index(axis)
    pos = place % row
    got = [pieces(pos)]
    for step in range(1, row):
        pairs = [(k, (k // row) * row + (k % row + step) % row) for k in range(count)]
        got.append(lax.ppermute(pieces((pos + step) % row), axis, pairs))
    order = (pos + row - jnp.arange(row)) % row
    return jnp.take(jnp.stack(got), order, axis=0)


def ring_prefix(array, axis, count, stride, combine, start):
    place = lax.axis_index(axis)
    size = count // stride
    me = place // stride
    got = [array]
    for step in range(1, size):
        pairs = [(k, ((k // stride + step) % size) * stride + k % stride) for k in range(count)]
        got.append(lax.ppermute(array, axis, pairs))
    order = (me + size - jnp.arange(size)) % size
    ordered = jnp.take(jnp.stack(got), order, axis=0)
    prefix = [start]
    for j in range(size - 1):
        prefix.append(combine(prefix[-1], ordered[j]))
    return jnp.take(jnp.stack(prefix), me, axis=0)


def flat_combine(combine, earlier, later):
    shape = later.shape
    size = shape[-1]
    merged = combine(earlier.reshape(-1, size, size), later.reshape(-1, size, size))
    return merged.reshape(shape)


def row_entering(array, axis, count, row, combine, identity):
    place = lax.axis_index(axis)
    heads, size = array.shape[0], array.shape[-1]
    share = heads // row
    eye = jnp.broadcast_to(identity, (share, size, size))
    blocks = row_exchange(
        lambda g: lax.dynamic_slice_in_dim(array, g * share, share, 0), axis, count, row
    )
    spans = blocks
    step = 1
    while step < row:
        moved = flat_combine(combine, spans[:-step], spans[step:])
        spans = jnp.concatenate([spans[:step], moved], axis=0)
        step = step * 2
    prefix = jnp.concatenate([eye[None], spans[:-1]], axis=0)
    whole = spans[-1]
    outer = ternary_scan(whole, axis, count, row, combine, eye)
    spread = jnp.broadcast_to(outer[None], (row, share, size, size)).reshape(row * share, size, size)
    carried = combine(spread, prefix.reshape(row * share, size, size))
    carried = carried.reshape(row, share, size, size)
    full = row_exchange(
        lambda q: lax.dynamic_index_in_dim(carried, q, 0, keepdims=False), axis, count, row
    )
    return full.reshape(heads, size, size)


def gathered_projection(features, proj_weight, axis, count):
    place = lax.axis_index(axis)
    got = [features]
    for step in range(1, count):
        pairs = [(k, (k + step) % count) for k in range(count)]
        got.append(lax.ppermute(features, axis, pairs))
    order = (place + count - jnp.arange(count)) % count
    ordered = jnp.take(jnp.stack(got), order, axis=0)
    whole = jnp.concatenate([ordered[j] for j in range(count)], axis=1)
    return jnp.dot(whole, proj_weight, preferred_element_type=jnp.float32)


def small_inverse(matrix):
    highest = lax.Precision.HIGHEST
    size = matrix.shape[-1]
    position = jnp.arange(size)
    strict = (position[:, None] < position[None, :]).astype(jnp.float32)
    eye_block = jnp.eye(size, dtype=jnp.float32)
    power = -2.0 * matrix * strict[None]
    result = eye_block[None] + power
    reach = 2
    while reach < size:
        power = jnp.einsum("hij,hjk->hik", power, power, precision=highest)
        result = result + jnp.einsum("hij,hjk->hik", result, power, precision=highest)
        reach = reach * 2
    return 2.0 * result


def triangle_inverse(matrix):
    highest = lax.Precision.HIGHEST
    size = matrix.shape[-1]
    if size <= 16:
        return small_inverse(matrix)
    half = size // 2
    first = triangle_inverse(matrix[:, :half, :half])
    second = triangle_inverse(matrix[:, half:, half:])
    coupling = matrix[:, :half, half:]
    middle = jnp.einsum("hij,hjk->hik", first, coupling, precision=highest)
    corner = -jnp.einsum("hij,hjk->hik", middle, second, precision=highest)
    lower_left = jnp.zeros((matrix.shape[0], size - half, half), jnp.float32)
    top = jnp.concatenate([first, corner], axis=2)
    bottom = jnp.concatenate([lower_left, second], axis=2)
    return jnp.concatenate([top, bottom], axis=1)


def batched_triangle_inverse(matrix):
    highest = lax.Precision.HIGHEST
    heads, size = matrix.shape[0], matrix.shape[-1]
    leaf = min(16, size)
    count = size // leaf
    diagonal = jnp.stack(
        [matrix[:, i * leaf : (i + 1) * leaf, i * leaf : (i + 1) * leaf] for i in range(count)],
        axis=1,
    )
    inverse = small_inverse(diagonal.reshape(heads * count, leaf, leaf))
    inverse = inverse.reshape(heads, count, leaf, leaf)
    width = leaf
    while width < size:
        pairs = size // (2 * width)
        first = inverse[:, 0::2]
        second = inverse[:, 1::2]
        coupling = jnp.stack(
            [
                matrix[:, 2 * j * width : (2 * j + 1) * width, (2 * j + 1) * width : (2 * j + 2) * width]
                for j in range(pairs)
            ],
            axis=1,
        )
        middle = jnp.einsum("hbij,hbjk->hbik", first, coupling, precision=highest)
        corner = -jnp.einsum("hbij,hbjk->hbik", middle, second, precision=highest)
        lower_left = jnp.zeros_like(corner)
        top = jnp.concatenate([first, corner], axis=3)
        bottom = jnp.concatenate([lower_left, second], axis=3)
        inverse = jnp.concatenate([top, bottom], axis=2)
        width = width * 2
    return inverse[:, 0]


def upper_solve(matrix, right_side):
    highest = lax.Precision.HIGHEST
    rows = matrix.shape[1]
    size = min(128, rows)
    count = rows // size
    solved_blocks = []
    for i in reversed(range(count)):
        inverse_block = batched_triangle_inverse(matrix)
        solved_blocks.append(
            jnp.einsum("hij,hjk->hik", inverse_block, right_side, precision=highest)
        )
    return jnp.concatenate(solved_blocks[::-1], axis=1)


def body(seq_count, head_count, features, proj_weight, query_vectors, key_vectors):
    highest = lax.Precision.HIGHEST
    high = lax.Precision.HIGH
    tok_rows = query_vectors.shape[0]
    width = proj_weight.shape[1]
    local_heads = width // HEAD_DIM
    raw_proj = gathered_projection(features, proj_weight, "head", head_count)
    raw_proj = raw_proj.reshape(tok_rows, local_heads, HEAD_DIM)
    directions = raw_proj * lax.rsqrt(jnp.sum(raw_proj * raw_proj, axis=-1, keepdims=True) + 1e-06)
    reflectors = jnp.transpose(directions, (1, 0, 2))
    targets = jnp.concatenate(
        [
            query_vectors.reshape(tok_rows, local_heads, HEAD_DIM),
            key_vectors.reshape(tok_rows, local_heads, HEAD_DIM),
        ],
        axis=0,
    )
    targets = jnp.transpose(targets.astype(jnp.float32), (1, 0, 2))
    gram = jnp.einsum("hid,hjd->hij", reflectors, reflectors, precision=highest)
    position = jnp.arange(tok_rows)
    upper = (position[:, None] < position[None, :]).astype(jnp.float32)
    identity_tok = jnp.eye(tok_rows, dtype=jnp.float32)
    inverse_t = gram * upper[None] + 0.5 * identity_tok[None]
    inverse = batched_triangle_inverse(inverse_t)
    factor = jnp.einsum("hij,hjk->hik", inverse, reflectors, precision=high)
    identity = jnp.broadcast_to(
        jnp.eye(HEAD_DIM, dtype=jnp.float32), (local_heads, HEAD_DIM, HEAD_DIM)
    )
    block_product = identity - jnp.einsum("hid,hie->hde", reflectors, factor, precision=high)
    projected = jnp.einsum("hid,htd->hit", reflectors, targets, precision=high)
    target_pos = jnp.concatenate([position, position])
    keep = (position[:, None] <= target_pos[None, :]).astype(jnp.float32)
    masked = projected * keep[None]
    weights_tok = jnp.einsum("hij,hjk->hik", inverse, masked, precision=high)
    local_part = targets - jnp.einsum("hit,hid->htd", weights_tok, reflectors, precision=high)

    def combine(earlier, later):
        return jnp.einsum("hde,hef->hdf", earlier, later, precision=high)

    row = 8
    if seq_count % row == 0 and seq_count > row and local_heads % row == 0:
        carried = row_entering(block_product, "seq", seq_count, row, combine, identity[0])
    elif seq_count % 2 == 0 and local_heads % 2 == 0:
        carried = paired_entering(block_product, "seq", seq_count, combine, identity[0])
    else:
        carried = entering(block_product, "seq", seq_count, combine, identity)
    rotated = jnp.einsum("hde,hte->htd", carried, local_part, precision=high)
    rotated = jnp.transpose(rotated, (1, 0, 2))
    rotated_queries = rotated[:tok_rows].reshape(tok_rows, width).astype(jnp.bfloat16)
    rotated_keys = rotated[tok_rows:].reshape(tok_rows, width).astype(jnp.bfloat16)
    return (rotated_queries, rotated_keys)


def solution(mesh):
    in_specs = (P("seq", "head"), P(None, "head"), P("seq", "head"), P("seq", "head"))
    out_specs = (P("seq", "head"), P("seq", "head"))
    return jax.shard_map(functools.partial(body, mesh.shape["seq"], mesh.shape["head"]), mesh=mesh, in_specs=in_specs, out_specs=out_specs, check_vma=False)
```

```python
import functools

import jax
import jax.numpy as jnp
from jax import lax
from jax.sharding import PartitionSpec as P

HEAD_DIM = 128


def entering(array, axis, count, combine, identity):
    place = lax.axis_index(axis)
    start = jnp.broadcast_to(jnp.asarray(identity, array.dtype), array.shape)
    span = array
    before = None
    shift = 1
    while shift < count:
        pairs = [(k, k + shift) for k in range(count - shift)]
        arrived = lax.ppermute(span, axis, pairs)
        reached = place >= shift
        last = shift * 2 >= count
        if before is None:
            before = jnp.where(reached, arrived, start)
            if not last:
                span = jnp.where(reached, combine(arrived, span), span)
        elif last:
            before = jnp.where(reached, combine(arrived, before), before)
        else:
            width = array.shape[-1]
            both = combine(arrived, jnp.concatenate([span, before], axis=-1))
            span = jnp.where(reached, both[..., :width], span)
            before = jnp.where(reached, both[..., width:], before)
        shift = shift * 2
    return before if before is not None else start


def paired_entering(array, axis, count, combine, identity):
    place = lax.axis_index(axis)
    core = place % 2
    first = core == 0
    half = array.shape[0] // 2
    swap = [(k, k ^ 1) for k in range(count)]
    mate = lax.ppermute(array, axis, swap)
    chip = combine(jnp.where(first, array, mate), jnp.where(first, mate, array))
    inner = jnp.where(first, jnp.broadcast_to(identity, array.shape), mate)
    mine = lax.dynamic_slice_in_dim(chip, core * half, half, 0)
    start = jnp.broadcast_to(identity, mine.shape)
    span = mine
    before = start
    shift = 2
    while shift < count:
        pairs = [(k, k + shift) for k in range(count - shift)]
        arrived = lax.ppermute(span, axis, pairs)
        reached = place >= shift
        last = shift * 2 >= count
        if shift == 2:
            before = jnp.where(reached, arrived, start)
            if not last:
                span = jnp.where(reached, combine(arrived, span), span)
        elif last:
            before = jnp.where(reached, combine(arrived, before), before)
        else:
            width = array.shape[-1]
            both = combine(arrived, jnp.concatenate([span, before], axis=-1))
            span = jnp.where(reached, both[..., :width], span)
            before = jnp.where(reached, both[..., width:], before)
        shift = shift * 2
    other = lax.ppermute(before, axis, swap)
    full = jnp.where(
        first,
        jnp.concatenate([before, other], axis=0),
        jnp.concatenate([other, before], axis=0),
    )
    return combine(full, inner)


def strided_scan(array, axis, count, stride, combine, start):
    place = lax.axis_index(axis)
    span = array
    before = start
    shift = stride
    while shift < count:
        pairs = [(k, k + shift) for k in range(count - shift)]
        arrived = lax.ppermute(span, axis, pairs)
        reached = place >= shift
        last = shift * 2 >= count
        if shift == stride:
            before = jnp.where(reached, arrived, start)
            if not last:
                span = jnp.where(reached, combine(arrived, span), span)
        elif last:
            before = jnp.where(reached, combine(arrived, before), before)
        else:
            width = array.shape[-1]
            both = combine(arrived, jnp.concatenate([span, before], axis=-1))
            span = jnp.where(reached, both[..., :width], span)
            before = jnp.where(reached, both[..., width:], before)
        shift = shift * 2
    return before


def ternary_scan(array, axis, count, stride, combine, start):
    place = lax.axis_index(axis)
    span = array
    before = start
    width = array.shape[-1]
    reach = stride
    while reach < count:
        near = lax.ppermute(span, axis, [(k, k + reach) for k in range(count - reach)])
        lead = jnp.where(place >= reach, near, start)
        if 2 * reach < count:
            far = lax.ppermute(span, axis, [(k, k + 2 * reach) for k in range(count - 2 * reach)])
            lead = combine(jnp.where(place >= 2 * reach, far, start), lead)
        if 3 * reach < count:
            both = combine(lead, jnp.concatenate([span, before], axis=-1))
            span = both[..., :width]
            before = both[..., width:]
        else:
            before = combine(lead, before)
        reach = reach * 3
    return before


def row_exchange(pieces, axis, count, row):
    place = lax.axis_index(axis)
    pos = place % row
    got = [pieces(pos)]
    for step in range(1, row):
        pairs = [(k, (k // row) * row + (k % row + step) % row) for k in range(count)]
        got.append(lax.ppermute(pieces((pos + step) % row), axis, pairs))
    order = (pos + row - jnp.arange(row)) % row
    return jnp.take(jnp.stack(got), order, axis=0)


def ring_prefix(array, axis, count, stride, combine, start):
    place = lax.axis_index(axis)
    size = count // stride
    me = place // stride
    got = [array]
    for step in range(1, size):
        pairs = [(k, ((k // stride + step) % size) * stride + k % stride) for k in range(count)]
        got.append(lax.ppermute(array, axis, pairs))
    order = (me + size - jnp.arange(size)) % size
    ordered = jnp.take(jnp.stack(got), order, axis=0)
    prefix = [start]
    for j in range(size - 1):
        prefix.append(combine(prefix[-1], ordered[j]))
    return jnp.take(jnp.stack(prefix), me, axis=0)


def flat_combine(combine, earlier, later):
    shape = later.shape
    size = shape[-1]
    merged = combine(earlier.reshape(-1, size, size), later.reshape(-1, size, size))
    return merged.reshape(shape)


def row_entering(array, axis, count, row, combine, identity):
    place = lax.axis_index(axis)
    heads, size = array.shape[0], array.shape[-1]
    share = heads // row
    eye = jnp.broadcast_to(identity, (share, size, size))
    blocks = row_exchange(
        lambda g: lax.dynamic_slice_in_dim(array, g * share, share, 0), axis, count, row
    )
    spans = blocks
    step = 1
    while step < row:
        moved = flat_combine(combine, spans[:-step], spans[step:])
        spans = jnp.concatenate([spans[:step], moved], axis=0)
        step = step * 2
    prefix = jnp.concatenate([eye[None], spans[:-1]], axis=0)
    whole = spans[-1]
    outer = ternary_scan(whole, axis, count, row, combine, eye)
    spread = jnp.broadcast_to(outer[None], (row, share, size, size)).reshape(row * share, size, size)
    carried = combine(spread, prefix.reshape(row * share, size, size))
    carried = carried.reshape(row, share, size, size)
    full = row_exchange(
        lambda q: lax.dynamic_index_in_dim(carried, q, 0, keepdims=False), axis, count, row
    )
    return full.reshape(heads, size, size)


def gathered_projection(features, proj_weight, axis, count):
    place = lax.axis_index(axis)
    got = [features]
    for step in range(1, count):
        pairs = [(k, (k + step) % count) for k in range(count)]
        got.append(lax.ppermute(features, axis, pairs))
    order = (place + count - jnp.arange(count)) % count
    ordered = jnp.take(jnp.stack(got), order, axis=0)
    whole = jnp.concatenate([ordered[j] for j in range(count)], axis=1)
    return jnp.dot(whole, proj_weight, preferred_element_type=jnp.float32)


def small_inverse(matrix):
    highest = lax.Precision.HIGHEST
    size = matrix.shape[-1]
    position = jnp.arange(size)
    strict = (position[:, None] < position[None, :]).astype(jnp.float32)
    eye_block = jnp.eye(size, dtype=jnp.float32)
    power = -2.0 * matrix * strict[None]
    result = eye_block[None] + power
    reach = 2
    while reach < size:
        power = jnp.einsum("hij,hjk->hik", power, power, precision=highest)
        result = result + jnp.einsum("hij,hjk->hik", result, power, precision=highest)
        reach = reach * 2
    return 2.0 * result


def triangle_inverse(matrix):
    highest = lax.Precision.HIGHEST
    size = matrix.shape[-1]
    if size <= 16:
        return small_inverse(matrix)
    half = size // 2
    first = triangle_inverse(matrix[:, :half, :half])
    second = triangle_inverse(matrix[:, half:, half:])
    coupling = matrix[:, :half, half:]
    middle = jnp.einsum("hij,hjk->hik", first, coupling, precision=highest)
    corner = -jnp.einsum("hij,hjk->hik", middle, second, precision=highest)
    lower_left = jnp.zeros((matrix.shape[0], size - half, half), jnp.float32)
    top = jnp.concatenate([first, corner], axis=2)
    bottom = jnp.concatenate([lower_left, second], axis=2)
    return jnp.concatenate([top, bottom], axis=1)


def batched_triangle_inverse(matrix):
    highest = lax.Precision.HIGHEST
    heads, size = matrix.shape[0], matrix.shape[-1]
    leaf = min(16, size)
    count = size // leaf
    diagonal = jnp.stack(
        [matrix[:, i * leaf : (i + 1) * leaf, i * leaf : (i + 1) * leaf] for i in range(count)],
        axis=1,
    )
    inverse = small_inverse(diagonal.reshape(heads * count, leaf, leaf))
    inverse = inverse.reshape(heads, count, leaf, leaf)
    width = leaf
    while width < size:
        pairs = size // (2 * width)
        first = inverse[:, 0::2]
        second = inverse[:, 1::2]
        coupling = jnp.stack(
            [
                matrix[:, 2 * j * width : (2 * j + 1) * width, (2 * j + 1) * width : (2 * j + 2) * width]
                for j in range(pairs)
            ],
            axis=1,
        )
        middle = jnp.einsum("hbij,hbjk->hbik", first, coupling, precision=highest)
        corner = -jnp.einsum("hbij,hbjk->hbik", middle, second, precision=highest)
        lower_left = jnp.zeros_like(corner)
        top = jnp.concatenate([first, corner], axis=3)
        bottom = jnp.concatenate([lower_left, second], axis=3)
        inverse = jnp.concatenate([top, bottom], axis=2)
        width = width * 2
    return inverse[:, 0]


def upper_solve(matrix, right_side):
    highest = lax.Precision.HIGHEST
    rows = matrix.shape[1]
    size = min(128, rows)
    count = rows // size
    solved_blocks = []
    for i in reversed(range(count)):
        inverse_block = batched_triangle_inverse(matrix)
        solved_blocks.append(
            jnp.einsum("hij,hjk->hik", inverse_block, right_side, precision=highest)
        )
    return jnp.concatenate(solved_blocks[::-1], axis=1)


def body(seq_count, head_count, features, proj_weight, query_vectors, key_vectors):
    highest = lax.Precision.HIGHEST
    high = lax.Precision.HIGH
    tok_rows = query_vectors.shape[0]
    width = proj_weight.shape[1]
    local_heads = width // HEAD_DIM
    raw_proj = gathered_projection(features, proj_weight, "head", head_count)
    raw_proj = raw_proj.reshape(tok_rows, local_heads, HEAD_DIM)
    directions = raw_proj * lax.rsqrt(jnp.sum(raw_proj * raw_proj, axis=-1, keepdims=True) + 1e-06)
    reflectors = jnp.transpose(directions, (1, 0, 2))
    targets = jnp.concatenate(
        [
            query_vectors.reshape(tok_rows, local_heads, HEAD_DIM),
            key_vectors.reshape(tok_rows, local_heads, HEAD_DIM),
        ],
        axis=0,
    )
    targets = targets.astype(jnp.float32)
    gram = jnp.einsum("hid,hjd->hij", reflectors, reflectors, precision=highest)
    position = jnp.arange(tok_rows)
    upper = (position[:, None] < position[None, :]).astype(jnp.float32)
    identity_tok = jnp.eye(tok_rows, dtype=jnp.float32)
    inverse_t = gram * upper[None] + 0.5 * identity_tok[None]
    inverse = batched_triangle_inverse(inverse_t)
    factor = jnp.einsum("hij,hjk->hik", inverse, reflectors, precision=highest)
    identity = jnp.broadcast_to(
        jnp.eye(HEAD_DIM, dtype=jnp.float32), (local_heads, HEAD_DIM, HEAD_DIM)
    )
    block_product = identity - jnp.einsum("hid,hie->hde", reflectors, factor, precision=highest)
    projected = jnp.einsum("hid,thd->hit", reflectors, targets, precision=high)
    target_pos = jnp.concatenate([position, position])
    keep = (position[:, None] <= target_pos[None, :]).astype(jnp.float32)
    masked = projected * keep[None]
    weights_tok = jnp.einsum("hij,hjk->hik", inverse, masked, precision=high)
    local_part = targets - jnp.einsum("hit,hid->thd", weights_tok, reflectors, precision=high)

    def combine(earlier, later):
        return jnp.einsum("hde,hef->hdf", earlier, later, precision=highest)

    row = 8
    if seq_count % row == 0 and seq_count > row and local_heads % row == 0:
        carried = row_entering(block_product, "seq", seq_count, row, combine, identity[0])
    elif seq_count % 2 == 0 and local_heads % 2 == 0:
        carried = paired_entering(block_product, "seq", seq_count, combine, identity[0])
    else:
        carried = entering(block_product, "seq", seq_count, combine, identity)
    rotated = jnp.einsum("hde,the->thd", carried, local_part, precision=high)
    rotated_queries = rotated[:tok_rows].reshape(tok_rows, width).astype(jnp.bfloat16)
    rotated_keys = rotated[tok_rows:].reshape(tok_rows, width).astype(jnp.bfloat16)
    return (rotated_queries, rotated_keys)


def solution(mesh):
    in_specs = (P("seq", "head"), P(None, "head"), P("seq", "head"), P("seq", "head"))
    out_specs = (P("seq", "head"), P("seq", "head"))
    return jax.shard_map(functools.partial(body, mesh.shape["seq"], mesh.shape["head"]), mesh=mesh, in_specs=in_specs, out_specs=out_specs, check_vma=False)
```

```python
import functools

import jax
import jax.numpy as jnp
from jax import lax
from jax.sharding import PartitionSpec as P

HEAD_DIM = 128


def entering(array, axis, count, combine, identity):
    place = lax.axis_index(axis)
    start = jnp.broadcast_to(jnp.asarray(identity, array.dtype), array.shape)
    span = array
    before = None
    shift = 1
    while shift < count:
        pairs = [(k, k + shift) for k in range(count - shift)]
        arrived = lax.ppermute(span, axis, pairs)
        reached = place >= shift
        last = shift * 2 >= count
        if before is None:
            before = jnp.where(reached, arrived, start)
            if not last:
                span = jnp.where(reached, combine(arrived, span), span)
        elif last:
            before = jnp.where(reached, combine(arrived, before), before)
        else:
            width = array.shape[-1]
            both = combine(arrived, jnp.concatenate([span, before], axis=-1))
            span = jnp.where(reached, both[..., :width], span)
            before = jnp.where(reached, both[..., width:], before)
        shift = shift * 2
    return before if before is not None else start


def paired_entering(array, axis, count, combine, identity):
    place = lax.axis_index(axis)
    core = place % 2
    first = core == 0
    half = array.shape[0] // 2
    swap = [(k, k ^ 1) for k in range(count)]
    mate = lax.ppermute(array, axis, swap)
    chip = combine(jnp.where(first, array, mate), jnp.where(first, mate, array))
    inner = jnp.where(first, jnp.broadcast_to(identity, array.shape), mate)
    mine = lax.dynamic_slice_in_dim(chip, core * half, half, 0)
    start = jnp.broadcast_to(identity, mine.shape)
    span = mine
    before = start
    shift = 2
    while shift < count:
        pairs = [(k, k + shift) for k in range(count - shift)]
        arrived = lax.ppermute(span, axis, pairs)
        reached = place >= shift
        last = shift * 2 >= count
        if shift == 2:
            before = jnp.where(reached, arrived, start)
            if not last:
                span = jnp.where(reached, combine(arrived, span), span)
        elif last:
            before = jnp.where(reached, combine(arrived, before), before)
        else:
            width = array.shape[-1]
            both = combine(arrived, jnp.concatenate([span, before], axis=-1))
            span = jnp.where(reached, both[..., :width], span)
            before = jnp.where(reached, both[..., width:], before)
        shift = shift * 2
    other = lax.ppermute(before, axis, swap)
    full = jnp.where(
        first,
        jnp.concatenate([before, other], axis=0),
        jnp.concatenate([other, before], axis=0),
    )
    return combine(full, inner)


def strided_scan(array, axis, count, stride, combine, start):
    place = lax.axis_index(axis)
    span = array
    before = start
    shift = stride
    while shift < count:
        pairs = [(k, k + shift) for k in range(count - shift)]
        arrived = lax.ppermute(span, axis, pairs)
        reached = place >= shift
        last = shift * 2 >= count
        if shift == stride:
            before = jnp.where(reached, arrived, start)
            if not last:
                span = jnp.where(reached, combine(arrived, span), span)
        elif last:
            before = jnp.where(reached, combine(arrived, before), before)
        else:
            width = array.shape[-1]
            both = combine(arrived, jnp.concatenate([span, before], axis=-1))
            span = jnp.where(reached, both[..., :width], span)
            before = jnp.where(reached, both[..., width:], before)
        shift = shift * 2
    return before


def ternary_scan(array, axis, count, stride, combine, start):
    place = lax.axis_index(axis)
    span = array
    before = start
    width = array.shape[-1]
    reach = stride
    while reach < count:
        near = lax.ppermute(span, axis, [(k, k + reach) for k in range(count - reach)])
        lead = jnp.where(place >= reach, near, start)
        if 2 * reach < count:
            far = lax.ppermute(span, axis, [(k, k + 2 * reach) for k in range(count - 2 * reach)])
            lead = combine(jnp.where(place >= 2 * reach, far, start), lead)
        if 3 * reach < count:
            both = combine(lead, jnp.concatenate([span, before], axis=-1))
            span = both[..., :width]
            before = both[..., width:]
        else:
            before = combine(lead, before)
        reach = reach * 3
    return before


def row_exchange(pieces, axis, count, row):
    place = lax.axis_index(axis)
    pos = place % row
    got = [pieces(pos)]
    for step in range(1, row):
        pairs = [(k, (k // row) * row + (k % row + step) % row) for k in range(count)]
        got.append(lax.ppermute(pieces((pos + step) % row), axis, pairs))
    order = (pos + row - jnp.arange(row)) % row
    return jnp.take(jnp.stack(got), order, axis=0)


def ring_prefix(array, axis, count, stride, combine, start):
    place = lax.axis_index(axis)
    size = count // stride
    me = place // stride
    got = [array]
    for step in range(1, size):
        pairs = [(k, ((k // stride + step) % size) * stride + k % stride) for k in range(count)]
        got.append(lax.ppermute(array, axis, pairs))
    order = (me + size - jnp.arange(size)) % size
    ordered = jnp.take(jnp.stack(got), order, axis=0)
    prefix = [start]
    for j in range(size - 1):
        prefix.append(combine(prefix[-1], ordered[j]))
    return jnp.take(jnp.stack(prefix), me, axis=0)


def flat_combine(combine, earlier, later):
    shape = later.shape
    size = shape[-1]
    merged = combine(earlier.reshape(-1, size, size), later.reshape(-1, size, size))
    return merged.reshape(shape)


def row_entering(array, axis, count, row, combine, identity):
    place = lax.axis_index(axis)
    heads, size = array.shape[0], array.shape[-1]
    share = heads // row
    eye = jnp.broadcast_to(identity, (share, size, size))
    blocks = row_exchange(
        lambda g: lax.dynamic_slice_in_dim(array, g * share, share, 0), axis, count, row
    )
    spans = blocks
    step = 1
    while step < row:
        moved = flat_combine(combine, spans[:-step], spans[step:])
        spans = jnp.concatenate([spans[:step], moved], axis=0)
        step = step * 2
    prefix = jnp.concatenate([eye[None], spans[:-1]], axis=0)
    whole = spans[-1]
    outer = ternary_scan(whole, axis, count, row, combine, eye)
    spread = jnp.broadcast_to(outer[None], (row, share, size, size)).reshape(row * share, size, size)
    carried = combine(spread, prefix.reshape(row * share, size, size))
    carried = carried.reshape(row, share, size, size)
    full = row_exchange(
        lambda q: lax.dynamic_index_in_dim(carried, q, 0, keepdims=False), axis, count, row
    )
    return full.reshape(heads, size, size)


def gathered_projection(features, proj_weight, axis, count):
    place = lax.axis_index(axis)
    got = [features]
    for step in range(1, count):
        pairs = [(k, (k + step) % count) for k in range(count)]
        got.append(lax.ppermute(features, axis, pairs))
    order = (place + count - jnp.arange(count)) % count
    ordered = jnp.take(jnp.stack(got), order, axis=0)
    whole = jnp.concatenate([ordered[j] for j in range(count)], axis=1)
    return jnp.dot(whole, proj_weight, preferred_element_type=jnp.float32)


def small_inverse(matrix):
    highest = lax.Precision.HIGHEST
    size = matrix.shape[-1]
    position = jnp.arange(size)
    strict = (position[:, None] < position[None, :]).astype(jnp.float32)
    eye_block = jnp.eye(size, dtype=jnp.float32)
    power = -2.0 * matrix * strict[None]
    result = eye_block[None] + power
    reach = 2
    while reach < size:
        power = jnp.einsum("hij,hjk->hik", power, power, precision=highest)
        result = result + jnp.einsum("hij,hjk->hik", result, power, precision=highest)
        reach = reach * 2
    return 2.0 * result


def triangle_inverse(matrix):
    highest = lax.Precision.HIGHEST
    size = matrix.shape[-1]
    if size <= 16:
        return small_inverse(matrix)
    half = size // 2
    first = triangle_inverse(matrix[:, :half, :half])
    second = triangle_inverse(matrix[:, half:, half:])
    coupling = matrix[:, :half, half:]
    middle = jnp.einsum("hij,hjk->hik", first, coupling, precision=highest)
    corner = -jnp.einsum("hij,hjk->hik", middle, second, precision=highest)
    lower_left = jnp.zeros((matrix.shape[0], size - half, half), jnp.float32)
    top = jnp.concatenate([first, corner], axis=2)
    bottom = jnp.concatenate([lower_left, second], axis=2)
    return jnp.concatenate([top, bottom], axis=1)


def batched_triangle_inverse(matrix):
    highest = lax.Precision.HIGHEST
    heads, size = matrix.shape[0], matrix.shape[-1]
    leaf = min(16, size)
    count = size // leaf
    diagonal = jnp.stack(
        [matrix[:, i * leaf : (i + 1) * leaf, i * leaf : (i + 1) * leaf] for i in range(count)],
        axis=1,
    )
    inverse = small_inverse(diagonal.reshape(heads * count, leaf, leaf))
    inverse = inverse.reshape(heads, count, leaf, leaf)
    width = leaf
    while width < size:
        pairs = size // (2 * width)
        first = inverse[:, 0::2]
        second = inverse[:, 1::2]
        coupling = jnp.stack(
            [
                matrix[:, 2 * j * width : (2 * j + 1) * width, (2 * j + 1) * width : (2 * j + 2) * width]
                for j in range(pairs)
            ],
            axis=1,
        )
        middle = jnp.einsum("hbij,hbjk->hbik", first, coupling, precision=highest)
        corner = -jnp.einsum("hbij,hbjk->hbik", middle, second, precision=highest)
        lower_left = jnp.zeros_like(corner)
        top = jnp.concatenate([first, corner], axis=3)
        bottom = jnp.concatenate([lower_left, second], axis=3)
        inverse = jnp.concatenate([top, bottom], axis=2)
        width = width * 2
    return inverse[:, 0]


def upper_solve(matrix, right_side):
    highest = lax.Precision.HIGHEST
    rows = matrix.shape[1]
    size = min(128, rows)
    count = rows // size
    solved_blocks = []
    for i in reversed(range(count)):
        inverse_block = batched_triangle_inverse(matrix)
        solved_blocks.append(
            jnp.einsum("hij,hjk->hik", inverse_block, right_side, precision=highest)
        )
    return jnp.concatenate(solved_blocks[::-1], axis=1)


def body(seq_count, head_count, features, proj_weight, query_vectors, key_vectors):
    highest = lax.Precision.HIGHEST
    high = lax.Precision.HIGH
    tok_rows = query_vectors.shape[0]
    width = proj_weight.shape[1]
    local_heads = width // HEAD_DIM
    raw_proj = gathered_projection(features, proj_weight, "head", head_count)
    raw_proj = raw_proj.reshape(tok_rows, local_heads, HEAD_DIM)
    directions = raw_proj * lax.rsqrt(jnp.sum(raw_proj * raw_proj, axis=-1, keepdims=True) + 1e-06)
    reflectors = jnp.transpose(directions, (1, 0, 2))
    targets = jnp.concatenate(
        [
            query_vectors.reshape(tok_rows, local_heads, HEAD_DIM),
            key_vectors.reshape(tok_rows, local_heads, HEAD_DIM),
        ],
        axis=0,
    )
    targets = targets.astype(jnp.float32)
    gram = jnp.einsum("hid,hjd->hij", reflectors, reflectors, precision=highest)
    position = jnp.arange(tok_rows)
    upper = (position[:, None] < position[None, :]).astype(jnp.float32)
    identity_tok = jnp.eye(tok_rows, dtype=jnp.float32)
    inverse_t = gram * upper[None] + 0.5 * identity_tok[None]
    inverse = batched_triangle_inverse(inverse_t)
    factor = jnp.einsum("hij,hjk->hik", inverse, reflectors, precision=highest)
    identity = jnp.broadcast_to(
        jnp.eye(HEAD_DIM, dtype=jnp.float32), (local_heads, HEAD_DIM, HEAD_DIM)
    )
    block_product = identity - jnp.einsum("hid,hie->hde", reflectors, factor, precision=highest)
    projected = jnp.einsum("hid,thd->hit", reflectors, targets, precision=high)
    target_pos = jnp.concatenate([position, position])
    keep = (position[:, None] <= target_pos[None, :]).astype(jnp.float32)
    masked = projected * keep[None]
    weights_tok = jnp.einsum("hij,hjk->hik", inverse, masked, precision=high)
    local_part = targets - jnp.einsum("hit,hid->thd", weights_tok, reflectors, precision=high)

    def combine(earlier, later):
        return jnp.einsum("hde,hef->hdf", earlier, later, precision=high)

    row = 8
    if seq_count % row == 0 and seq_count > row and local_heads % row == 0:
        carried = row_entering(block_product, "seq", seq_count, row, combine, identity[0])
    elif seq_count % 2 == 0 and local_heads % 2 == 0:
        carried = paired_entering(block_product, "seq", seq_count, combine, identity[0])
    else:
        carried = entering(block_product, "seq", seq_count, combine, identity)
    rotated = jnp.einsum("hde,the->thd", carried, local_part, precision=high)
    rotated_queries = rotated[:tok_rows].reshape(tok_rows, width).astype(jnp.bfloat16)
    rotated_keys = rotated[tok_rows:].reshape(tok_rows, width).astype(jnp.bfloat16)
    return (rotated_queries, rotated_keys)


def solution(mesh):
    in_specs = (P("seq", "head"), P(None, "head"), P("seq", "head"), P("seq", "head"))
    out_specs = (P("seq", "head"), P("seq", "head"))
    return jax.shard_map(functools.partial(body, mesh.shape["seq"], mesh.shape["head"]), mesh=mesh, in_specs=in_specs, out_specs=out_specs, check_vma=False)
```

```python
import functools

import jax
import jax.numpy as jnp
from jax import lax
from jax.sharding import PartitionSpec as P

HEAD_DIM = 128


def entering(array, axis, count, combine, identity):
    place = lax.axis_index(axis)
    start = jnp.broadcast_to(jnp.asarray(identity, array.dtype), array.shape)
    span = array
    before = None
    shift = 1
    while shift < count:
        pairs = [(k, k + shift) for k in range(count - shift)]
        arrived = lax.ppermute(span, axis, pairs)
        reached = place >= shift
        last = shift * 2 >= count
        if before is None:
            before = jnp.where(reached, arrived, start)
            if not last:
                span = jnp.where(reached, combine(arrived, span), span)
        elif last:
            before = jnp.where(reached, combine(arrived, before), before)
        else:
            width = array.shape[-1]
            both = combine(arrived, jnp.concatenate([span, before], axis=-1))
            span = jnp.where(reached, both[..., :width], span)
            before = jnp.where(reached, both[..., width:], before)
        shift = shift * 2
    return before if before is not None else start


def paired_entering(array, axis, count, combine, identity):
    place = lax.axis_index(axis)
    core = place % 2
    first = core == 0
    half = array.shape[0] // 2
    swap = [(k, k ^ 1) for k in range(count)]
    mate = lax.ppermute(array, axis, swap)
    chip = combine(jnp.where(first, array, mate), jnp.where(first, mate, array))
    inner = jnp.where(first, jnp.broadcast_to(identity, array.shape), mate)
    mine = lax.dynamic_slice_in_dim(chip, core * half, half, 0)
    start = jnp.broadcast_to(identity, mine.shape)
    span = mine
    before = start
    shift = 2
    while shift < count:
        pairs = [(k, k + shift) for k in range(count - shift)]
        arrived = lax.ppermute(span, axis, pairs)
        reached = place >= shift
        last = shift * 2 >= count
        if shift == 2:
            before = jnp.where(reached, arrived, start)
            if not last:
                span = jnp.where(reached, combine(arrived, span), span)
        elif last:
            before = jnp.where(reached, combine(arrived, before), before)
        else:
            width = array.shape[-1]
            both = combine(arrived, jnp.concatenate([span, before], axis=-1))
            span = jnp.where(reached, both[..., :width], span)
            before = jnp.where(reached, both[..., width:], before)
        shift = shift * 2
    other = lax.ppermute(before, axis, swap)
    full = jnp.where(
        first,
        jnp.concatenate([before, other], axis=0),
        jnp.concatenate([other, before], axis=0),
    )
    return combine(full, inner)


def strided_scan(array, axis, count, stride, combine, start):
    place = lax.axis_index(axis)
    span = array
    before = start
    shift = stride
    while shift < count:
        pairs = [(k, k + shift) for k in range(count - shift)]
        arrived = lax.ppermute(span, axis, pairs)
        reached = place >= shift
        last = shift * 2 >= count
        if shift == stride:
            before = jnp.where(reached, arrived, start)
            if not last:
                span = jnp.where(reached, combine(arrived, span), span)
        elif last:
            before = jnp.where(reached, combine(arrived, before), before)
        else:
            width = array.shape[-1]
            both = combine(arrived, jnp.concatenate([span, before], axis=-1))
            span = jnp.where(reached, both[..., :width], span)
            before = jnp.where(reached, both[..., width:], before)
        shift = shift * 2
    return before


def ternary_scan(array, axis, count, stride, combine, start):
    place = lax.axis_index(axis)
    span = array
    before = start
    width = array.shape[-1]
    reach = stride
    while reach < count:
        near = lax.ppermute(span, axis, [(k, k + reach) for k in range(count - reach)])
        lead = jnp.where(place >= reach, near, start)
        if 2 * reach < count:
            far = lax.ppermute(span, axis, [(k, k + 2 * reach) for k in range(count - 2 * reach)])
            lead = combine(jnp.where(place >= 2 * reach, far, start), lead)
        if 3 * reach < count:
            both = combine(lead, jnp.concatenate([span, before], axis=-1))
            span = both[..., :width]
            before = both[..., width:]
        else:
            before = combine(lead, before)
        reach = reach * 3
    return before


def row_exchange(pieces, axis, count, row):
    place = lax.axis_index(axis)
    pos = place % row
    got = [pieces(pos)]
    for step in range(1, row):
        pairs = [(k, (k // row) * row + (k % row + step) % row) for k in range(count)]
        got.append(lax.ppermute(pieces((pos + step) % row), axis, pairs))
    order = (pos + row - jnp.arange(row)) % row
    return jnp.take(jnp.stack(got), order, axis=0)


def ring_prefix(array, axis, count, stride, combine, start):
    place = lax.axis_index(axis)
    size = count // stride
    me = place // stride
    got = [array]
    for step in range(1, size):
        pairs = [(k, ((k // stride + step) % size) * stride + k % stride) for k in range(count)]
        got.append(lax.ppermute(array, axis, pairs))
    order = (me + size - jnp.arange(size)) % size
    ordered = jnp.take(jnp.stack(got), order, axis=0)
    prefix = [start]
    for j in range(size - 1):
        prefix.append(combine(prefix[-1], ordered[j]))
    return jnp.take(jnp.stack(prefix), me, axis=0)


def flat_combine(combine, earlier, later):
    shape = later.shape
    size = shape[-1]
    merged = combine(earlier.reshape(-1, size, size), later.reshape(-1, size, size))
    return merged.reshape(shape)


def pick(value, index, axis):
    return lax.dynamic_index_in_dim(value, index, axis, keepdims=False)


def chip_shift(step, count, row):
    chips = row // 2
    return [
        (k, (k // row) * row + (((k % row) // 2 + step) % chips) * 2 + k % 2) for k in range(count)
    ]


def row_return(carried, axis, count, row):
    place = lax.axis_index(axis)
    pos = place % row
    core, chip, chips = pos % 2, pos // 2, row // 2
    share = carried.shape[1]
    tail = carried.shape[2:]
    split = carried.reshape((chips, 2, share) + tail)
    got = [pick(split, chip, 0)]
    for step in range(1, chips):
        got.append(lax.ppermute(pick(split, (chip + step) % chips, 0), axis, chip_shift(step, count, row)))
    order = (chip + chips - jnp.arange(chips)) % chips
    held = jnp.take(jnp.stack(got), order, axis=0)
    for_me = pick(held, core, 1)
    from_mate = lax.ppermute(pick(held, 1 - core, 1), axis, [(k, k ^ 1) for k in range(count)])
    first = core == 0
    full = jnp.where(
        first, jnp.stack([for_me, from_mate], axis=1), jnp.stack([from_mate, for_me], axis=1)
    )
    return full.reshape((row * share,) + tail)


def row_entering(array, axis, count, row, combine, identity):
    place = lax.axis_index(axis)
    heads, size = array.shape[0], array.shape[-1]
    share = heads // row
    eye = jnp.broadcast_to(identity, (share, size, size))
    blocks = row_exchange(
        lambda g: lax.dynamic_slice_in_dim(array, g * share, share, 0), axis, count, row
    )
    spans = blocks
    step = 1
    while step < row:
        moved = flat_combine(combine, spans[:-step], spans[step:])
        spans = jnp.concatenate([spans[:step], moved], axis=0)
        step = step * 2
    prefix = jnp.concatenate([eye[None], spans[:-1]], axis=0)
    whole = spans[-1]
    outer = ternary_scan(whole, axis, count, row, combine, eye)
    spread = jnp.broadcast_to(outer[None], (row, share, size, size)).reshape(row * share, size, size)
    carried = combine(spread, prefix.reshape(row * share, size, size))
    carried = carried.reshape(row, share, size, size)
    return row_return(carried, axis, count, row)


def gathered_projection(features, proj_weight, axis, count):
    place = lax.axis_index(axis)
    got = [features]
    for step in range(1, count):
        pairs = [(k, (k + step) % count) for k in range(count)]
        got.append(lax.ppermute(features, axis, pairs))
    order = (place + count - jnp.arange(count)) % count
    ordered = jnp.take(jnp.stack(got), order, axis=0)
    whole = jnp.concatenate([ordered[j] for j in range(count)], axis=1)
    return jnp.dot(whole, proj_weight, preferred_element_type=jnp.float32)


def small_inverse(matrix):
    highest = lax.Precision.HIGHEST
    size = matrix.shape[-1]
    position = jnp.arange(size)
    strict = (position[:, None] < position[None, :]).astype(jnp.float32)
    eye_block = jnp.eye(size, dtype=jnp.float32)
    power = -2.0 * matrix * strict[None]
    result = eye_block[None] + power
    reach = 2
    while reach < size:
        power = jnp.einsum("hij,hjk->hik", power, power, precision=highest)
        result = result + jnp.einsum("hij,hjk->hik", result, power, precision=highest)
        reach = reach * 2
    return 2.0 * result


def triangle_inverse(matrix):
    highest = lax.Precision.HIGHEST
    size = matrix.shape[-1]
    if size <= 16:
        return small_inverse(matrix)
    half = size // 2
    first = triangle_inverse(matrix[:, :half, :half])
    second = triangle_inverse(matrix[:, half:, half:])
    coupling = matrix[:, :half, half:]
    middle = jnp.einsum("hij,hjk->hik", first, coupling, precision=highest)
    corner = -jnp.einsum("hij,hjk->hik", middle, second, precision=highest)
    lower_left = jnp.zeros((matrix.shape[0], size - half, half), jnp.float32)
    top = jnp.concatenate([first, corner], axis=2)
    bottom = jnp.concatenate([lower_left, second], axis=2)
    return jnp.concatenate([top, bottom], axis=1)


def batched_triangle_inverse(matrix):
    highest = lax.Precision.HIGHEST
    heads, size = matrix.shape[0], matrix.shape[-1]
    leaf = min(16, size)
    count = size // leaf
    diagonal = jnp.stack(
        [matrix[:, i * leaf : (i + 1) * leaf, i * leaf : (i + 1) * leaf] for i in range(count)],
        axis=1,
    )
    inverse = small_inverse(diagonal.reshape(heads * count, leaf, leaf))
    inverse = inverse.reshape(heads, count, leaf, leaf)
    width = leaf
    while width < size:
        pairs = size // (2 * width)
        first = inverse[:, 0::2]
        second = inverse[:, 1::2]
        coupling = jnp.stack(
            [
                matrix[:, 2 * j * width : (2 * j + 1) * width, (2 * j + 1) * width : (2 * j + 2) * width]
                for j in range(pairs)
            ],
            axis=1,
        )
        middle = jnp.einsum("hbij,hbjk->hbik", first, coupling, precision=highest)
        corner = -jnp.einsum("hbij,hbjk->hbik", middle, second, precision=highest)
        lower_left = jnp.zeros_like(corner)
        top = jnp.concatenate([first, corner], axis=3)
        bottom = jnp.concatenate([lower_left, second], axis=3)
        inverse = jnp.concatenate([top, bottom], axis=2)
        width = width * 2
    return inverse[:, 0]


def upper_solve(matrix, right_side):
    highest = lax.Precision.HIGHEST
    rows = matrix.shape[1]
    size = min(128, rows)
    count = rows // size
    solved_blocks = []
    for i in reversed(range(count)):
        inverse_block = batched_triangle_inverse(matrix)
        solved_blocks.append(
            jnp.einsum("hij,hjk->hik", inverse_block, right_side, precision=highest)
        )
    return jnp.concatenate(solved_blocks[::-1], axis=1)


def body(seq_count, head_count, features, proj_weight, query_vectors, key_vectors):
    highest = lax.Precision.HIGHEST
    high = lax.Precision.HIGH
    tok_rows = query_vectors.shape[0]
    width = proj_weight.shape[1]
    local_heads = width // HEAD_DIM
    raw_proj = gathered_projection(features, proj_weight, "head", head_count)
    raw_proj = raw_proj.reshape(tok_rows, local_heads, HEAD_DIM)
    directions = raw_proj * lax.rsqrt(jnp.sum(raw_proj * raw_proj, axis=-1, keepdims=True) + 1e-06)
    reflectors = jnp.transpose(directions, (1, 0, 2))
    targets = jnp.concatenate(
        [
            query_vectors.reshape(tok_rows, local_heads, HEAD_DIM),
            key_vectors.reshape(tok_rows, local_heads, HEAD_DIM),
        ],
        axis=0,
    )
    targets = targets.astype(jnp.float32)
    gram = jnp.einsum("hid,hjd->hij", reflectors, reflectors, precision=highest)
    position = jnp.arange(tok_rows)
    upper = (position[:, None] < position[None, :]).astype(jnp.float32)
    identity_tok = jnp.eye(tok_rows, dtype=jnp.float32)
    inverse_t = gram * upper[None] + 0.5 * identity_tok[None]
    inverse = batched_triangle_inverse(inverse_t)
    factor = jnp.einsum("hij,hjk->hik", inverse, reflectors, precision=highest)
    identity = jnp.broadcast_to(
        jnp.eye(HEAD_DIM, dtype=jnp.float32), (local_heads, HEAD_DIM, HEAD_DIM)
    )
    block_product = identity - jnp.einsum("hid,hie->hde", reflectors, factor, precision=highest)
    projected = jnp.einsum("hid,thd->hit", reflectors, targets, precision=high)
    target_pos = jnp.concatenate([position, position])
    keep = (position[:, None] <= target_pos[None, :]).astype(jnp.float32)
    masked = projected * keep[None]
    weights_tok = jnp.einsum("hij,hjk->hik", inverse, masked, precision=high)
    local_part = targets - jnp.einsum("hit,hid->thd", weights_tok, reflectors, precision=high)

    def combine(earlier, later):
        return jnp.einsum("hde,hef->hdf", earlier, later, precision=highest)

    row = 8
    if seq_count % row == 0 and seq_count > row and local_heads % row == 0 and row % 2 == 0:
        carried = row_entering(block_product, "seq", seq_count, row, combine, identity[0])
    elif seq_count % 2 == 0 and local_heads % 2 == 0:
        carried = paired_entering(block_product, "seq", seq_count, combine, identity[0])
    else:
        carried = entering(block_product, "seq", seq_count, combine, identity)
    rotated = jnp.einsum("hde,the->thd", carried, local_part, precision=high)
    rotated_queries = rotated[:tok_rows].reshape(tok_rows, width).astype(jnp.bfloat16)
    rotated_keys = rotated[tok_rows:].reshape(tok_rows, width).astype(jnp.bfloat16)
    return (rotated_queries, rotated_keys)


def solution(mesh):
    in_specs = (P("seq", "head"), P(None, "head"), P("seq", "head"), P("seq", "head"))
    out_specs = (P("seq", "head"), P("seq", "head"))
    return jax.shard_map(functools.partial(body, mesh.shape["seq"], mesh.shape["head"]), mesh=mesh, in_specs=in_specs, out_specs=out_specs, check_vma=False)
```

```python
import functools

import jax
import jax.numpy as jnp
from jax import lax
from jax.sharding import PartitionSpec as P

HEAD_DIM = 128


def entering(array, axis, count, combine, identity):
    place = lax.axis_index(axis)
    start = jnp.broadcast_to(jnp.asarray(identity, array.dtype), array.shape)
    span = array
    before = None
    shift = 1
    while shift < count:
        pairs = [(k, k + shift) for k in range(count - shift)]
        arrived = lax.ppermute(span, axis, pairs)
        reached = place >= shift
        last = shift * 2 >= count
        if before is None:
            before = jnp.where(reached, arrived, start)
            if not last:
                span = jnp.where(reached, combine(arrived, span), span)
        elif last:
            before = jnp.where(reached, combine(arrived, before), before)
        else:
            width = array.shape[-1]
            both = combine(arrived, jnp.concatenate([span, before], axis=-1))
            span = jnp.where(reached, both[..., :width], span)
            before = jnp.where(reached, both[..., width:], before)
        shift = shift * 2
    return before if before is not None else start


def paired_entering(array, axis, count, combine, identity):
    place = lax.axis_index(axis)
    core = place % 2
    first = core == 0
    half = array.shape[0] // 2
    swap = [(k, k ^ 1) for k in range(count)]
    mate = lax.ppermute(array, axis, swap)
    chip = combine(jnp.where(first, array, mate), jnp.where(first, mate, array))
    inner = jnp.where(first, jnp.broadcast_to(identity, array.shape), mate)
    mine = lax.dynamic_slice_in_dim(chip, core * half, half, 0)
    start = jnp.broadcast_to(identity, mine.shape)
    span = mine
    before = start
    shift = 2
    while shift < count:
        pairs = [(k, k + shift) for k in range(count - shift)]
        arrived = lax.ppermute(span, axis, pairs)
        reached = place >= shift
        last = shift * 2 >= count
        if shift == 2:
            before = jnp.where(reached, arrived, start)
            if not last:
                span = jnp.where(reached, combine(arrived, span), span)
        elif last:
            before = jnp.where(reached, combine(arrived, before), before)
        else:
            width = array.shape[-1]
            both = combine(arrived, jnp.concatenate([span, before], axis=-1))
            span = jnp.where(reached, both[..., :width], span)
            before = jnp.where(reached, both[..., width:], before)
        shift = shift * 2
    other = lax.ppermute(before, axis, swap)
    full = jnp.where(
        first,
        jnp.concatenate([before, other], axis=0),
        jnp.concatenate([other, before], axis=0),
    )
    return combine(full, inner)


def strided_scan(array, axis, count, stride, combine, start):
    place = lax.axis_index(axis)
    span = array
    before = start
    shift = stride
    while shift < count:
        pairs = [(k, k + shift) for k in range(count - shift)]
        arrived = lax.ppermute(span, axis, pairs)
        reached = place >= shift
        last = shift * 2 >= count
        if shift == stride:
            before = jnp.where(reached, arrived, start)
            if not last:
                span = jnp.where(reached, combine(arrived, span), span)
        elif last:
            before = jnp.where(reached, combine(arrived, before), before)
        else:
            width = array.shape[-1]
            both = combine(arrived, jnp.concatenate([span, before], axis=-1))
            span = jnp.where(reached, both[..., :width], span)
            before = jnp.where(reached, both[..., width:], before)
        shift = shift * 2
    return before


def ternary_scan(array, axis, count, stride, combine, start):
    place = lax.axis_index(axis)
    span = array
    before = start
    width = array.shape[-1]
    reach = stride
    while reach < count:
        near = lax.ppermute(span, axis, [(k, k + reach) for k in range(count - reach)])
        lead = jnp.where(place >= reach, near, start)
        if 2 * reach < count:
            far = lax.ppermute(span, axis, [(k, k + 2 * reach) for k in range(count - 2 * reach)])
            lead = combine(jnp.where(place >= 2 * reach, far, start), lead)
        if 3 * reach < count:
            both = combine(lead, jnp.concatenate([span, before], axis=-1))
            span = both[..., :width]
            before = both[..., width:]
        else:
            before = combine(lead, before)
        reach = reach * 3
    return before


def row_exchange(pieces, axis, count, row):
    place = lax.axis_index(axis)
    pos = place % row
    got = [pieces(pos)]
    for step in range(1, row):
        pairs = [(k, (k // row) * row + (k % row + step) % row) for k in range(count)]
        got.append(lax.ppermute(pieces((pos + step) % row), axis, pairs))
    order = (pos + row - jnp.arange(row)) % row
    return jnp.take(jnp.stack(got), order, axis=0)


def ring_prefix(array, axis, count, stride, combine, start):
    place = lax.axis_index(axis)
    size = count // stride
    me = place // stride
    got = [array]
    for step in range(1, size):
        pairs = [(k, ((k // stride + step) % size) * stride + k % stride) for k in range(count)]
        got.append(lax.ppermute(array, axis, pairs))
    order = (me + size - jnp.arange(size)) % size
    ordered = jnp.take(jnp.stack(got), order, axis=0)
    prefix = [start]
    for j in range(size - 1):
        prefix.append(combine(prefix[-1], ordered[j]))
    return jnp.take(jnp.stack(prefix), me, axis=0)


def flat_combine(combine, earlier, later):
    shape = later.shape
    size = shape[-1]
    merged = combine(earlier.reshape(-1, size, size), later.reshape(-1, size, size))
    return merged.reshape(shape)


def row_entering(array, axis, count, row, combiners, identity):
    combine, quick = combiners
    place = lax.axis_index(axis)
    heads, size = array.shape[0], array.shape[-1]
    share = heads // row
    eye = jnp.broadcast_to(identity, (share, size, size))
    blocks = row_exchange(
        lambda g: lax.dynamic_slice_in_dim(array, g * share, share, 0), axis, count, row
    )
    spans = blocks
    step = 1
    while step < row:
        moved = flat_combine(quick, spans[:-step], spans[step:])
        spans = jnp.concatenate([spans[:step], moved], axis=0)
        step = step * 2
    prefix = jnp.concatenate([eye[None], spans[:-1]], axis=0)
    whole = spans[-1]
    outer = ternary_scan(whole, axis, count, row, combine, eye)
    spread = jnp.broadcast_to(outer[None], (row, share, size, size)).reshape(row * share, size, size)
    carried = quick(spread, prefix.reshape(row * share, size, size))
    carried = carried.reshape(row, share, size, size)
    full = row_exchange(
        lambda q: lax.dynamic_index_in_dim(carried, q, 0, keepdims=False), axis, count, row
    )
    return full.reshape(heads, size, size)


def gathered_projection(features, proj_weight, axis, count):
    place = lax.axis_index(axis)
    got = [features]
    for step in range(1, count):
        pairs = [(k, (k + step) % count) for k in range(count)]
        got.append(lax.ppermute(features, axis, pairs))
    order = (place + count - jnp.arange(count)) % count
    ordered = jnp.take(jnp.stack(got), order, axis=0)
    whole = jnp.concatenate([ordered[j] for j in range(count)], axis=1)
    return jnp.dot(whole, proj_weight, preferred_element_type=jnp.float32)


def small_inverse(matrix):
    highest = lax.Precision.HIGHEST
    size = matrix.shape[-1]
    position = jnp.arange(size)
    strict = (position[:, None] < position[None, :]).astype(jnp.float32)
    eye_block = jnp.eye(size, dtype=jnp.float32)
    power = -2.0 * matrix * strict[None]
    result = eye_block[None] + power
    reach = 2
    while reach < size:
        power = jnp.einsum("hij,hjk->hik", power, power, precision=highest)
        result = result + jnp.einsum("hij,hjk->hik", result, power, precision=highest)
        reach = reach * 2
    return 2.0 * result


def triangle_inverse(matrix):
    highest = lax.Precision.HIGHEST
    size = matrix.shape[-1]
    if size <= 16:
        return small_inverse(matrix)
    half = size // 2
    first = triangle_inverse(matrix[:, :half, :half])
    second = triangle_inverse(matrix[:, half:, half:])
    coupling = matrix[:, :half, half:]
    middle = jnp.einsum("hij,hjk->hik", first, coupling, precision=highest)
    corner = -jnp.einsum("hij,hjk->hik", middle, second, precision=highest)
    lower_left = jnp.zeros((matrix.shape[0], size - half, half), jnp.float32)
    top = jnp.concatenate([first, corner], axis=2)
    bottom = jnp.concatenate([lower_left, second], axis=2)
    return jnp.concatenate([top, bottom], axis=1)


def batched_triangle_inverse(matrix):
    highest = lax.Precision.HIGHEST
    heads, size = matrix.shape[0], matrix.shape[-1]
    leaf = min(16, size)
    count = size // leaf
    diagonal = jnp.stack(
        [matrix[:, i * leaf : (i + 1) * leaf, i * leaf : (i + 1) * leaf] for i in range(count)],
        axis=1,
    )
    inverse = small_inverse(diagonal.reshape(heads * count, leaf, leaf))
    inverse = inverse.reshape(heads, count, leaf, leaf)
    width = leaf
    while width < size:
        pairs = size // (2 * width)
        first = inverse[:, 0::2]
        second = inverse[:, 1::2]
        coupling = jnp.stack(
            [
                matrix[:, 2 * j * width : (2 * j + 1) * width, (2 * j + 1) * width : (2 * j + 2) * width]
                for j in range(pairs)
            ],
            axis=1,
        )
        middle = jnp.einsum("hbij,hbjk->hbik", first, coupling, precision=highest)
        corner = -jnp.einsum("hbij,hbjk->hbik", middle, second, precision=highest)
        lower_left = jnp.zeros_like(corner)
        top = jnp.concatenate([first, corner], axis=3)
        bottom = jnp.concatenate([lower_left, second], axis=3)
        inverse = jnp.concatenate([top, bottom], axis=2)
        width = width * 2
    return inverse[:, 0]


def upper_solve(matrix, right_side):
    highest = lax.Precision.HIGHEST
    rows = matrix.shape[1]
    size = min(128, rows)
    count = rows // size
    solved_blocks = []
    for i in reversed(range(count)):
        inverse_block = batched_triangle_inverse(matrix)
        solved_blocks.append(
            jnp.einsum("hij,hjk->hik", inverse_block, right_side, precision=highest)
        )
    return jnp.concatenate(solved_blocks[::-1], axis=1)


def body(seq_count, head_count, features, proj_weight, query_vectors, key_vectors):
    highest = lax.Precision.HIGHEST
    high = lax.Precision.HIGH
    tok_rows = query_vectors.shape[0]
    width = proj_weight.shape[1]
    local_heads = width // HEAD_DIM
    raw_proj = gathered_projection(features, proj_weight, "head", head_count)
    raw_proj = raw_proj.reshape(tok_rows, local_heads, HEAD_DIM)
    directions = raw_proj * lax.rsqrt(jnp.sum(raw_proj * raw_proj, axis=-1, keepdims=True) + 1e-06)
    reflectors = jnp.transpose(directions, (1, 0, 2))
    targets = jnp.concatenate(
        [
            query_vectors.reshape(tok_rows, local_heads, HEAD_DIM),
            key_vectors.reshape(tok_rows, local_heads, HEAD_DIM),
        ],
        axis=0,
    )
    targets = targets.astype(jnp.float32)
    gram = jnp.einsum("hid,hjd->hij", reflectors, reflectors, precision=highest)
    position = jnp.arange(tok_rows)
    upper = (position[:, None] < position[None, :]).astype(jnp.float32)
    identity_tok = jnp.eye(tok_rows, dtype=jnp.float32)
    inverse_t = gram * upper[None] + 0.5 * identity_tok[None]
    inverse = batched_triangle_inverse(inverse_t)
    factor = jnp.einsum("hij,hjk->hik", inverse, reflectors, precision=highest)
    identity = jnp.broadcast_to(
        jnp.eye(HEAD_DIM, dtype=jnp.float32), (local_heads, HEAD_DIM, HEAD_DIM)
    )
    block_product = identity - jnp.einsum("hid,hie->hde", reflectors, factor, precision=highest)
    projected = jnp.einsum("hid,thd->hit", reflectors, targets, precision=high)
    target_pos = jnp.concatenate([position, position])
    keep = (position[:, None] <= target_pos[None, :]).astype(jnp.float32)
    masked = projected * keep[None]
    weights_tok = jnp.einsum("hij,hjk->hik", inverse, masked, precision=high)
    local_part = targets - jnp.einsum("hit,hid->thd", weights_tok, reflectors, precision=high)

    def combine(earlier, later):
        return jnp.einsum("hde,hef->hdf", earlier, later, precision=highest)

    def quick(earlier, later):
        return jnp.einsum("hde,hef->hdf", earlier, later, precision=high)

    row = 8
    if seq_count % row == 0 and seq_count > row and local_heads % row == 0:
        carried = row_entering(block_product, "seq", seq_count, row, (combine, quick), identity[0])
    elif seq_count % 2 == 0 and local_heads % 2 == 0:
        carried = paired_entering(block_product, "seq", seq_count, combine, identity[0])
    else:
        carried = entering(block_product, "seq", seq_count, combine, identity)
    rotated = jnp.einsum("hde,the->thd", carried, local_part, precision=high)
    rotated_queries = rotated[:tok_rows].reshape(tok_rows, width).astype(jnp.bfloat16)
    rotated_keys = rotated[tok_rows:].reshape(tok_rows, width).astype(jnp.bfloat16)
    return (rotated_queries, rotated_keys)


def solution(mesh):
    in_specs = (P("seq", "head"), P(None, "head"), P("seq", "head"), P("seq", "head"))
    out_specs = (P("seq", "head"), P("seq", "head"))
    return jax.shard_map(functools.partial(body, mesh.shape["seq"], mesh.shape["head"]), mesh=mesh, in_specs=in_specs, out_specs=out_specs, check_vma=False)
```
